32 devices in a mesh: seq: 8 (over z, x), exp: 4 (over y, core).
Axes of the slice: x: 2, y: 2, z: 4, core: 2. Of those that a mesh axis runs over, the one named last changes fastest.
Arguments:
- hidden_in: bfloat16 [2048, 1536], P('seq'), may hold values from -6 to 6
- attn_gain: float32 [1536], replicated, may hold values from 0.1 to 1.9
- q_weight: bfloat16 [1536, 1536], P(None, 'exp'), may hold values from -1.25 to 1.25
- k_weight: bfloat16 [1536, 512], P(None, 'exp'), may hold values from -0.625 to 0.625
- v_weight: bfloat16 [1536, 512], P(None, 'exp'), may hold values from -0.15625 to 0.15625
- o_weight: bfloat16 [1536, 1536], P('exp'), may hold values from -0.15625 to 0.15625
- cache_kv: bfloat16 [4096, 1024], P('seq', 'exp'), may hold values from -216 to 216
- moe_gain: float32 [1536], replicated, may hold values from 0.1 to 1.9
- expert_in: bfloat16 [32, 1536, 1024], P('seq'), may hold values from -0.15625 to 0.15625
- expert_out: bfloat16 [32, 512, 1536], P('seq'), may hold values from -0.25 to 0.25
- routes: int32 [2048, 8], P(('seq', 'exp')), may hold values from 0 to 31, all different within a row; in each aligned block of 64 rows (0 to 63, 64 to 127, ...) at most 32 rows name the same one
- route_prob: float32 [2048, 8], P(('seq', 'exp')), may hold values from 0.05 to 1
- page_slot: int32 [256], replicated, may hold values from 0 to 31, as said below
Outputs:
- hidden_out: bfloat16 [2048, 1536], P(('seq', 'exp'))
- decode_pages: bfloat16 [256, 8, 2, 512], P('seq', 'exp')
The draws below stay inside these ranges and needn't reach their ends.
Inputs may be any that keep to these rules, and one draw needn't show every extreme that they name: `routes`: in each aligned block of 64 rows (the rows of one device) no expert is named by more than 32 rows; a row names 8 different experts. `page_slot`: for each r, the 32 blocks b with b mod (8) == r have different slots.
All inputs are finite; a program needn't handle non-finite values.
Results may differ from the reference program's by a relative error of at most 0.0074.
Values may be sent and summed in bfloat16 or wider, within the bound.
No kernel may reach another device: no remote copies, remote signals or barrier semaphores. Data moves between devices by JAX's collectives and lax.ppermute only.
A program may use at most 128 MiB of HBM per device.

```python
import math
import jax
import jax.numpy as jnp
import numpy as np
from jax import lax

D = 1536
HEADS = 24
KV_HEADS = 8
HEAD_DIM = 64
FF = 512
EXPERTS = 32
TOPK = 8
PAGE = 8
NEW = 2048
PROMPT = 1024
CACHE = 4096
ROWS_DEV = 64
CAP = 32
PAGES_SEQ = 32
NPAGES = 256
N_SEQ = 8


def draw_cache_kv(key, part):
    shape = (CACHE, KV_HEADS, 2, HEAD_DIM)
    kind_scale = jnp.array([4.0, 1.0], jnp.float32)[None, None, :, None]
    base = jnp.clip(jax.random.normal(key, shape, jnp.float32), -6.0, 6.0)
    return (base * kind_scale).reshape(CACHE, KV_HEADS * 2 * HEAD_DIM).astype(jnp.bfloat16)


def draw_page_slot(key, part):
    groups = NPAGES // PAGES_SEQ
    group_keys = jax.random.split(key, groups)
    orders = jax.vmap(lambda group_key: jax.random.permutation(group_key, PAGES_SEQ))(group_keys)
    return orders.T.reshape(NPAGES).astype(jnp.int32)


def shard_levels(rng, extent, cuts, smallest, high):
    level, own = 1.0, jax.random.fold_in(rng, 6)
    for position, shards_of in cuts:
        draws = jnp.exp(jax.random.uniform(jax.random.fold_in(own, position), (shards_of,), jnp.float32, smallest / len(cuts), high / len(cuts)))
        level = level * jnp.repeat(draws, extent[position] // shards_of).reshape([-1 if axis == position else 1 for axis in range(len(extent))])
    return level


def assign_block(stream_key, own, number, rows, count, top, most, lean):
    ranking = jax.random.permutation(stream_key, count)
    packed, usual = portions_of(count, rows * top, most, lean, True), portions_of(count, rows * top, most, lean, False)
    places = jnp.arange(count)

    def named(lengths, turn):
        used = int((lengths > 0).sum())
        fixed = max(1, used // 4)
        shifted = fixed + (places - fixed + turn * (used - fixed)) % max(1, count - fixed)
        return jnp.zeros((count,), jnp.int32).at[ranking[jnp.where(places < fixed, places, shifted)]].set(jnp.asarray(lengths, jnp.int32))

    lengths = jnp.where(number % 4 == 0, named(packed, number // 4), named(usual, number - number // 4 - 1))
    mixed = jax.random.permutation(jax.random.fold_in(own, 3), count)
    source_of, receiver = mixed[0:count // 2 * 2:2], mixed[1:count // 2 * 2:2]
    margin = jnp.minimum(lengths[source_of] - 1, most - lengths[receiver]) // 2
    margin = jnp.where((source_of == ranking[0]) | (receiver == ranking[0]) | (lengths[receiver] == 0), 0, jnp.maximum(margin, 0))
    shifted = jax.random.randint(jax.random.fold_in(own, 4), (count // 2,), 0, 1 << 20) % (margin + 1)
    lengths = lengths.at[source_of].add(-shifted).at[receiver].add(shifted)
    members = jnp.searchsorted(jnp.cumsum(lengths), jnp.arange(rows * top), side="right").astype(jnp.int32)
    listing = members.reshape(top, rows).T
    listing = listing[jax.random.permutation(jax.random.fold_in(own, 1), rows)]
    turn = jax.random.randint(jax.random.fold_in(own, 2), (rows, 1), 0, top)
    return jnp.take_along_axis(listing, (jnp.arange(top)[None, :] + turn) % top, axis=1)


def portions_of(count, total, most, slope, full):
    weights = [(1 << 20) // math.isqrt(grade ** slope) + 1 for grade in range(1, count + 1)]
    largest = most if full else min(most, max(-(-total // count), total * weights[0] // sum(weights)))
    least = 1 if total - largest >= count - 1 else 0
    given, surplus = [largest] + [least] * (count - 1), total - largest - least * (count - 1)
    while surplus > 0:
        candidates = [i for i in range(1, count) if given[i] < largest] or [i for i in range(1, count) if given[i] < most]
        whole, left = sum([weights[i] for i in candidates]), surplus
        for i in candidates:
            more = min(most - given[i], max(1, left * weights[i] // whole), surplus)
            given[i] = given[i] + more
            surplus = surplus - more
    return np.array(given)


def noise(stream_key, extent, width, bound, pieces=(), kind=jnp.bfloat16):
    entries = width * jax.random.normal(stream_key, extent, jnp.float32)
    if pieces:
        entries = entries * shard_levels(stream_key, extent, pieces, -0.22, 0.18)
    return jnp.clip(entries, -bound, bound).astype(kind)


def setup_inputs(seed: int = 0) -> dict:
    streams_of = jax.random.split(jax.random.key(seed), 14)
    hidden_in = noise(streams_of[0], (NEW, D), 1.0, 6.0, ((0, 8),))
    attn_gain = jnp.clip(1.0 + 0.18 * jax.random.normal(streams_of[1], (D,), jnp.float32), 0.1, 1.9)
    q_weight = noise(streams_of[2], (D, HEADS * HEAD_DIM), (D // 64) ** -0.5, 1.25, ((1, 4),))
    k_weight = noise(streams_of[3], (D, KV_HEADS * HEAD_DIM), (D // 16) ** -0.5, 0.625, ((1, 4),))
    v_weight = noise(streams_of[4], (D, KV_HEADS * HEAD_DIM), D ** -0.5, 0.15625, ((1, 4),))
    o_weight = noise(streams_of[5], (HEADS * HEAD_DIM, D), (HEADS * HEAD_DIM) ** -0.5, 0.15625, ((0, 4),))
    cache_kv = draw_cache_kv(jax.random.fold_in(streams_of[13], 71), 0)
    moe_gain = jnp.clip(1.0 + 0.18 * jax.random.normal(streams_of[7], (D,), jnp.float32), 0.1, 1.9)
    expert_in = noise(streams_of[8], (EXPERTS, D, 2 * FF), D ** -0.5, 0.15625, ((0, 8),))
    expert_out = noise(streams_of[9], (EXPERTS, FF, D), FF ** -0.5, 0.25, ((0, 8),))
    routes_keys = jax.random.split(jax.random.fold_in(streams_of[10], 1), NEW // ROWS_DEV)
    routes_turns = jax.random.permutation(jax.random.fold_in(streams_of[10], 3), NEW // ROWS_DEV)
    routes = jax.vmap(lambda own, number: assign_block(jax.random.fold_in(streams_of[10], 2), own, number, ROWS_DEV, EXPERTS, TOPK, CAP, 2))(routes_keys, routes_turns).reshape((NEW, TOPK))
    route_prob = jnp.clip(0.05 + 0.95 * jax.random.uniform(streams_of[11], (NEW, TOPK), jnp.float32) ** shard_levels(streams_of[11], (NEW, TOPK), ((0, 32),), -0.2, 0.2), 0.05, 1.0)
    page_slot = draw_page_slot(jax.random.fold_in(streams_of[13], 71), 0)
    return {"hidden_in": hidden_in, "attn_gain": attn_gain, "q_weight": q_weight, "k_weight": k_weight, "v_weight": v_weight, "o_weight": o_weight, "cache_kv": cache_kv, "moe_gain": moe_gain, "expert_in": expert_in, "expert_out": expert_out, "routes": routes, "route_prob": route_prob, "page_slot": page_slot}


norm_epsilon = 1e-06
attention_scale = 0.015625
residual_scale = 0.22
masked_score = -1e+30

def rms_norm(values, gain_row):
    widened = values.astype(jnp.float32)
    spread = lax.rsqrt(lax.optimization_barrier(jnp.mean(widened * widened, axis=-1, keepdims=True)) + norm_epsilon)
    return (widened * spread * gain_row).astype(jnp.bfloat16)

def attend_all(queries, keys, values):
    block_rows = math.gcd(NEW, 512)
    key_count = CACHE + NEW
    key_index = jnp.arange(key_count, dtype=jnp.int32)
    key_new = key_index - CACHE
    key_cache = key_index < CACHE
    key_second = key_new >= PROMPT
    query_blocks = queries.reshape(NEW // block_rows, block_rows, KV_HEADS, HEADS // KV_HEADS, HEAD_DIM)
    block_starts = block_rows * jnp.arange(NEW // block_rows, dtype=jnp.int32)

    def one_block(pair_in):
        query_block, block_start = pair_in
        query_index = block_start + jnp.arange(block_rows, dtype=jnp.int32)
        query_second = query_index >= PROMPT
        visible = jnp.where(key_cache[None, :], jnp.logical_not(query_second)[:, None], (key_second[None, :] == query_second[:, None]) & (key_new[None, :] <= query_index[:, None]))

        def one_head(head_id):
            query_head = query_block[:, head_id].astype(jnp.float32)
            key_head = keys[:, head_id].astype(jnp.float32)
            value_head = values[:, head_id].astype(jnp.float32)
            scores = jnp.einsum('tgd,nd->gtn', query_head, key_head) * attention_scale
            scores = jnp.where(visible[None], scores, masked_score)
            row_best = lax.optimization_barrier(jnp.max(scores, axis=-1, keepdims=True))
            weights = jnp.where(visible[None], jnp.exp(scores - row_best), 0.0)
            total_sum = lax.optimization_barrier(jnp.sum(weights, axis=-1, keepdims=True))
            rounded = lax.optimization_barrier(weights.astype(jnp.bfloat16))
            summed = jnp.einsum('gtn,nd->gtd', rounded.astype(jnp.float32), value_head)
            return summed / total_sum
        head_outs = lax.map(one_head, jnp.arange(KV_HEADS, dtype=jnp.int32))
        return head_outs.transpose(2, 0, 1, 3).reshape(block_rows, HEADS * HEAD_DIM).astype(jnp.bfloat16)
    block_outs = lax.map(one_block, (query_blocks, block_starts))
    return block_outs.reshape(NEW, HEADS * HEAD_DIM)

def reference(hidden_in, attn_gain, q_weight, k_weight, v_weight, o_weight, cache_kv, moe_gain, expert_in, expert_out, routes, route_prob, page_slot):
    normed = rms_norm(hidden_in, attn_gain)
    queries = jnp.dot(normed, q_weight, preferred_element_type=jnp.float32).astype(jnp.bfloat16)
    queries = queries.reshape(NEW, KV_HEADS, HEADS // KV_HEADS, HEAD_DIM)
    keys_new = jnp.dot(normed, k_weight, preferred_element_type=jnp.float32).astype(jnp.bfloat16).reshape(NEW, KV_HEADS, HEAD_DIM)
    values_new = jnp.dot(normed, v_weight, preferred_element_type=jnp.float32).astype(jnp.bfloat16).reshape(NEW, KV_HEADS, HEAD_DIM)
    cache_rows = cache_kv.reshape(CACHE, KV_HEADS, 2, HEAD_DIM)
    keys = jnp.concatenate([cache_rows[:, :, 0], keys_new], axis=0)
    values = jnp.concatenate([cache_rows[:, :, 1], values_new], axis=0)
    attended = attend_all(queries, keys, values)
    mixed_rows = jnp.dot(attended, o_weight, preferred_element_type=jnp.float32)
    residual = hidden_in.astype(jnp.float32) + residual_scale * mixed_rows
    moe_in = rms_norm(residual, moe_gain)
    flat_ids = routes.reshape(-1).astype(jnp.int32)
    flat_weights = (route_prob / lax.optimization_barrier(jnp.sum(route_prob, axis=-1, keepdims=True))).reshape(-1)
    assign_count = NEW * TOPK
    load_bound = NEW // ROWS_DEV * CAP

    def one_expert(total_moe, expert):
        picked_ids = jnp.nonzero(flat_ids == expert, size=load_bound, fill_value=assign_count)[0].astype(jnp.int32)
        is_valid = picked_ids < assign_count
        clipped = jnp.minimum(picked_ids, assign_count - 1)
        token_ids = clipped // TOPK
        rows_in = moe_in[token_ids]
        hidden = jnp.dot(rows_in, expert_in[expert], preferred_element_type=jnp.float32)
        active = (jax.nn.silu(hidden[:, :FF]) * hidden[:, FF:]).astype(jnp.bfloat16)
        produced = jnp.dot(active, expert_out[expert], preferred_element_type=jnp.float32).astype(jnp.bfloat16)
        share = jnp.where(is_valid, flat_weights[clipped], 0.0)
        total_moe = total_moe.at[token_ids].add(share[:, None] * produced.astype(jnp.float32))
        return (total_moe, None)
    moe, _ = lax.scan(one_expert, jnp.zeros((NEW, D), jnp.float32), jnp.arange(EXPERTS, dtype=jnp.int32))
    hidden_out = (residual + residual_scale * moe).astype(jnp.bfloat16)
    pair_rows = jnp.stack([keys_new, values_new], axis=2).reshape(NPAGES, PAGE, KV_HEADS, 2, HEAD_DIM)
    block_ids = jnp.arange(NPAGES, dtype=jnp.int32)
    target = block_ids % N_SEQ * PAGES_SEQ + page_slot.astype(jnp.int32)
    placed = jnp.zeros_like(pair_rows).at[target].set(pair_rows)
    decode_pages = placed.transpose(0, 2, 3, 1, 4).reshape(NPAGES, KV_HEADS, 2, PAGE * HEAD_DIM)
    return (hidden_out, decode_pages)
```

```python
import math

import jax
import jax.numpy as jnp
from jax import lax
from jax.sharding import PartitionSpec as P

HEADS = 24
KV_HEADS = 8
HEAD_DIM = 64
EXPERTS = 32
PAGE = 8


norm_epsilon = 1e-06
attention_scale = 0.015625
residual_scale = 0.22
masked_score = -1e30


def rms_norm(values, gain_row):
    widened = values.astype(jnp.float32)
    spread = lax.rsqrt(jnp.mean(widened * widened, axis=-1, keepdims=True) + norm_epsilon)
    return (widened * spread * gain_row).astype(jnp.bfloat16)


def attend_block(carried, query_heads, visible, key_rows, value_rows):
    best_old, total_old, summed_old = carried
    scores = (
        jnp.einsum("tkgd,nkd->kgtn", query_heads, key_rows, preferred_element_type=jnp.float32)
        * attention_scale
    )
    scores = jnp.where(visible, scores, masked_score)
    best_new = jnp.maximum(best_old, jnp.max(scores, axis=-1))
    weights = jnp.where(visible, jnp.exp(scores - best_new[..., None]), 0.0)
    factor = jnp.exp(best_old - best_new)
    total_new = total_old * factor + jnp.sum(weights, axis=-1)
    summed_new = summed_old * factor[..., None] + jnp.einsum(
        "kgtn,nkd->kgtd",
        weights.astype(jnp.bfloat16),
        value_rows,
        preferred_element_type=jnp.float32,
    )
    return (best_new, total_new, summed_new)


def block_size(piece_rows):
    return math.gcd(piece_rows, 512)


def body(
    hidden_in,
    attn_gain,
    q_weight,
    k_weight,
    v_weight,
    o_weight,
    cache_kv,
    moe_gain,
    expert_in,
    expert_out,
    routes,
    route_prob,
    page_slot,
):
    seq_count = lax.axis_size("seq")
    seq_index = lax.axis_index("seq")
    exp_index = lax.axis_index("exp")
    tokens_here = hidden_in.shape[0]
    head_dim = HEAD_DIM
    kv_local = k_weight.shape[1] // head_dim
    group_size = HEADS // KV_HEADS
    prompt_len = tokens_here * seq_count // 2
    first_row = seq_index * tokens_here
    query_rows = first_row + jnp.arange(tokens_here, dtype=jnp.int32)
    query_second = query_rows >= prompt_len
    holds_first = first_row < prompt_len
    normed = rms_norm(hidden_in, attn_gain)
    queries = jnp.dot(normed, q_weight, preferred_element_type=jnp.float32).astype(jnp.bfloat16)
    keys_new = jnp.dot(normed, k_weight, preferred_element_type=jnp.float32).astype(jnp.bfloat16)
    values_new = jnp.dot(normed, v_weight, preferred_element_type=jnp.float32).astype(jnp.bfloat16)
    pair_width = 2 * kv_local * head_dim
    pairs_new = jnp.stack(
        [
            keys_new.reshape(tokens_here, kv_local, head_dim),
            values_new.reshape(tokens_here, kv_local, head_dim),
        ],
        axis=2,
    ).reshape(tokens_here, pair_width)
    query_heads = queries.reshape(tokens_here, kv_local, group_size, head_dim)
    cache_lines = cache_kv.reshape(tokens_here, -1)
    blocks_here = tokens_here // PAGE
    rounds = blocks_here // seq_count
    outgoing = pairs_new.reshape(rounds, seq_count, PAGE * pair_width)
    received = lax.all_to_all(outgoing, "seq", split_axis=1, concat_axis=1, tiled=True)
    block_ids = (
        jnp.arange(seq_count, dtype=jnp.int32)[None, :] * blocks_here
        + jnp.arange(rounds, dtype=jnp.int32)[:, None] * seq_count
        + seq_index
    ).reshape(-1)
    table_ids = jnp.arange(page_slot.shape[0], dtype=jnp.int32)
    page_slots = jnp.sum(
        jnp.where(block_ids[:, None] == table_ids[None, :], page_slot[None, :], 0), axis=1
    )
    local_pages = (
        jnp.zeros((blocks_here, PAGE * pair_width), jnp.bfloat16)
        .at[page_slots]
        .set(received.reshape(blocks_here, -1))
    )
    page_rows = local_pages.reshape(blocks_here, PAGE, kv_local, 2, head_dim).transpose(
        0, 2, 3, 1, 4
    )
    page_rows = page_rows.reshape(blocks_here, kv_local, 2, PAGE * head_dim)
    start_state = (
        jnp.full((kv_local, group_size, tokens_here), masked_score, jnp.float32),
        jnp.zeros((kv_local, group_size, tokens_here), jnp.float32),
        jnp.zeros((kv_local, group_size, tokens_here, head_dim), jnp.float32),
    )

    def new_keys_part(carried, new_block, key_first):
        width_rows = new_block.shape[0]
        key_rows = key_first + jnp.arange(width_rows, dtype=jnp.int32)
        visible = ((key_rows >= prompt_len)[None, :] == query_second[:, None]) & (
            key_rows[None, :] <= query_rows[:, None]
        )
        split_pairs = new_block.reshape(width_rows, kv_local, 2, head_dim)
        return lax.cond(
            jnp.any(visible),
            lambda carried_in: attend_block(
                carried_in, query_heads, visible, split_pairs[:, :, 0], split_pairs[:, :, 1]
            ),
            lambda carried_in: carried_in,
            carried,
        )

    carried = start_state
    new_piece = lax.all_gather(pairs_new, "seq", axis=0, tiled=True)
    cache_piece = lax.all_gather(cache_lines, "seq", axis=0, tiled=True)
    piece_rows = new_piece.shape[0]
    stride = block_size(piece_rows)
    new_blocks = new_piece.reshape(piece_rows // stride, stride, -1)
    cache_blocks = cache_piece.reshape(piece_rows // stride, 2 * stride, kv_local, 2, head_dim)
    offsets = stride * jnp.arange(piece_rows // stride, dtype=jnp.int32)
    everything = jnp.ones((tokens_here, 2 * stride), bool)

    def visit(carried_in, block_part):
        new_block, cache_block, key_first = block_part
        carried_in = new_keys_part(carried_in, new_block, key_first)
        carried_in = lax.cond(
            holds_first,
            lambda inner: attend_block(
                inner, query_heads, everything, cache_block[:, :, 0], cache_block[:, :, 1]
            ),
            lambda inner: inner,
            carried_in,
        )
        return (carried_in, None)

    carried, _ = lax.scan(visit, carried, (new_blocks, cache_blocks, offsets))
    best_final, total_final, summed_final = carried
    attended = (
        (summed_final / total_final[..., None])
        .transpose(2, 0, 1, 3)
        .reshape(tokens_here, -1)
        .astype(jnp.bfloat16)
    )
    mixed_rows = lax.psum_scatter(
        jnp.dot(attended, o_weight, preferred_element_type=jnp.float32).astype(jnp.bfloat16),
        "exp",
        scatter_dimension=0,
        tiled=True,
    ).astype(jnp.float32)
    moe_rows = mixed_rows.shape[0]
    residual = (
        lax.dynamic_slice_in_dim(hidden_in, exp_index * moe_rows, moe_rows, 0).astype(jnp.float32)
        + residual_scale * mixed_rows
    )
    moe_in = rms_norm(residual, moe_gain)
    top_count = routes.shape[1]
    experts_here = expert_in.shape[0]
    capacity = 2 * moe_rows * top_count // EXPERTS
    share = route_prob / jnp.sum(route_prob, axis=-1, keepdims=True)
    rows_all = lax.all_gather(moe_in, "seq", axis=0, tiled=True)
    routes_all = lax.all_gather(routes, "seq", axis=0, tiled=True)
    share_all = lax.all_gather(share, "seq", axis=0, tiled=True)
    total_rows = rows_all.shape[0]
    local_ids = seq_index * experts_here + jnp.arange(experts_here, dtype=jnp.int32)
    hits = routes_all[:, :, None] == local_ids[None, None, :]
    named = jnp.any(hits, axis=1)
    weight = jnp.sum(jnp.where(hits, share_all[:, :, None], 0.0), axis=1)
    named_blocks = named.reshape(seq_count, moe_rows, experts_here).astype(jnp.int32)
    rank = jnp.cumsum(named_blocks, axis=1) - named_blocks
    slot = (jnp.arange(seq_count, dtype=jnp.int32)[:, None, None] * capacity + rank).reshape(
        total_rows, experts_here
    )
    slots_total = seq_count * capacity
    picks = named[:, :, None] & (
        slot[:, :, None] == jnp.arange(slots_total, dtype=jnp.int32)[None, None, :]
    )
    onehot = picks.astype(jnp.bfloat16)
    rows_in = jnp.einsum(
        "nec,nd->ecd", onehot, rows_all, preferred_element_type=jnp.float32
    ).astype(jnp.bfloat16)
    hidden = jnp.einsum("ecd,edf->ecf", rows_in, expert_in, preferred_element_type=jnp.float32)
    half_width = hidden.shape[-1] // 2
    active = (jax.nn.silu(hidden[..., :half_width]) * hidden[..., half_width:]).astype(jnp.bfloat16)
    produced = jnp.einsum(
        "ecf,efd->ecd", active, expert_out, preferred_element_type=jnp.float32
    ).astype(jnp.bfloat16)
    weight_hi = weight.astype(jnp.bfloat16)
    weight_lo = (weight - weight_hi.astype(jnp.float32)).astype(jnp.bfloat16)
    scaled_hi = jnp.where(picks, weight_hi[:, :, None], jnp.zeros_like(onehot))
    scaled_lo = jnp.where(picks, weight_lo[:, :, None], jnp.zeros_like(onehot))
    partial = jnp.einsum(
        "nec,ecd->nd", scaled_hi, produced, preferred_element_type=jnp.float32
    ) + jnp.einsum("nec,ecd->nd", scaled_lo, produced, preferred_element_type=jnp.float32)
    returned = lax.all_to_all(
        partial.astype(jnp.bfloat16).reshape(seq_count, moe_rows, -1),
        "seq",
        split_axis=0,
        concat_axis=0,
        tiled=True,
    )
    moe = jnp.sum(returned.astype(jnp.float32), axis=0)
    hidden_out = (residual + residual_scale * moe).astype(jnp.bfloat16)
    return (hidden_out, page_rows)


def solution(mesh):
    return jax.shard_map(
        body,
        mesh=mesh,
        in_specs=(
            P("seq", None),
            P(),
            P(None, "exp"),
            P(None, "exp"),
            P(None, "exp"),
            P("exp", None),
            P("seq", "exp"),
            P(),
            P("seq", None, None),
            P("seq", None, None),
            P(("seq", "exp"), None),
            P(("seq", "exp"), None),
            P(),
        ),
        out_specs=(P(("seq", "exp"), None), P("seq", "exp", None, None)),
        check_vma=False,
    )
```

```python
import math

import jax
import jax.numpy as jnp
from jax import lax
from jax.sharding import PartitionSpec as P

HEADS = 24
KV_HEADS = 8
HEAD_DIM = 64
EXPERTS = 32
PAGE = 8


norm_epsilon = 1e-06
attention_scale = 0.015625
residual_scale = 0.22
masked_score = -1e30


def rms_norm(values, gain_row):
    widened = values.astype(jnp.float32)
    spread = lax.rsqrt(jnp.mean(widened * widened, axis=-1, keepdims=True) + norm_epsilon)
    return (widened * spread * gain_row).astype(jnp.bfloat16)


def attend_block(carried, query_heads, visible, key_rows, value_rows):
    best_old, total_old, summed_old = carried
    scores = (
        jnp.einsum("tkgd,nkd->kgtn", query_heads, key_rows, preferred_element_type=jnp.float32)
        * attention_scale
    )
    scores = jnp.where(visible, scores, masked_score)
    best_new = jnp.maximum(best_old, jnp.max(scores, axis=-1))
    weights = jnp.where(visible, jnp.exp(scores - best_new[..., None]), 0.0)
    factor = jnp.exp(best_old - best_new)
    total_new = total_old * factor + jnp.sum(weights, axis=-1)
    summed_new = summed_old * factor[..., None] + jnp.einsum(
        "kgtn,nkd->kgtd",
        weights.astype(jnp.bfloat16),
        value_rows,
        preferred_element_type=jnp.float32,
    )
    return (best_new, total_new, summed_new)


def pl_cdiv(a, b):
    return -(-a // b)


def block_size(piece_rows):
    return math.gcd(piece_rows, 512)


def body(
    hidden_in,
    attn_gain,
    q_weight,
    k_weight,
    v_weight,
    o_weight,
    cache_kv,
    moe_gain,
    expert_in,
    expert_out,
    routes,
    route_prob,
    page_slot,
):
    seq_count = lax.axis_size("seq")
    seq_index = lax.axis_index("seq")
    exp_index = lax.axis_index("exp")
    tokens_here = hidden_in.shape[0]
    head_dim = HEAD_DIM
    kv_local = k_weight.shape[1] // head_dim
    group_size = HEADS // KV_HEADS
    prompt_len = tokens_here * seq_count // 2
    first_row = seq_index * tokens_here
    query_rows = first_row + jnp.arange(tokens_here, dtype=jnp.int32)
    query_second = query_rows >= prompt_len
    holds_first = first_row < prompt_len
    normed = rms_norm(hidden_in, attn_gain)
    queries = jnp.dot(normed, q_weight, preferred_element_type=jnp.float32).astype(jnp.bfloat16)
    keys_new = jnp.dot(normed, k_weight, preferred_element_type=jnp.float32).astype(jnp.bfloat16)
    values_new = jnp.dot(normed, v_weight, preferred_element_type=jnp.float32).astype(jnp.bfloat16)
    pair_width = 2 * kv_local * head_dim
    pairs_new = jnp.stack(
        [
            keys_new.reshape(tokens_here, kv_local, head_dim),
            values_new.reshape(tokens_here, kv_local, head_dim),
        ],
        axis=2,
    ).reshape(tokens_here, pair_width)
    query_heads = queries.reshape(tokens_here, kv_local, group_size, head_dim)
    cache_lines = cache_kv.reshape(tokens_here, -1)
    blocks_here = tokens_here // PAGE
    rounds = blocks_here // seq_count
    outgoing = pairs_new.reshape(rounds, seq_count, PAGE * pair_width)
    received = lax.all_to_all(outgoing, "seq", split_axis=1, concat_axis=1, tiled=True)
    block_ids = (
        jnp.arange(seq_count, dtype=jnp.int32)[None, :] * blocks_here
        + jnp.arange(rounds, dtype=jnp.int32)[:, None] * seq_count
        + seq_index
    ).reshape(-1)
    table_ids = jnp.arange(page_slot.shape[0], dtype=jnp.int32)
    page_slots = jnp.sum(
        jnp.where(block_ids[:, None] == table_ids[None, :], page_slot[None, :], 0), axis=1
    )
    local_pages = (
        jnp.zeros((blocks_here, PAGE * pair_width), jnp.bfloat16)
        .at[page_slots]
        .set(received.reshape(blocks_here, -1))
    )
    page_rows = local_pages.reshape(blocks_here, PAGE, kv_local, 2, head_dim).transpose(
        0, 2, 3, 1, 4
    )
    page_rows = page_rows.reshape(blocks_here, kv_local, 2, PAGE * head_dim)
    start_state = (
        jnp.full((kv_local, group_size, tokens_here), masked_score, jnp.float32),
        jnp.zeros((kv_local, group_size, tokens_here), jnp.float32),
        jnp.zeros((kv_local, group_size, tokens_here, head_dim), jnp.float32),
    )

    def new_keys_part(carried, new_block, key_first):
        width_rows = new_block.shape[0]
        key_rows = key_first + jnp.arange(width_rows, dtype=jnp.int32)
        visible = ((key_rows >= prompt_len)[None, :] == query_second[:, None]) & (
            key_rows[None, :] <= query_rows[:, None]
        )
        split_pairs = new_block.reshape(width_rows, kv_local, 2, head_dim)
        return lax.cond(
            jnp.any(visible),
            lambda carried_in: attend_block(
                carried_in, query_heads, visible, split_pairs[:, :, 0], split_pairs[:, :, 1]
            ),
            lambda carried_in: carried_in,
            carried,
        )

    carried = start_state
    new_piece = lax.all_gather(pairs_new, "seq", axis=0, tiled=True)
    cache_piece = lax.all_gather(cache_lines, "seq", axis=0, tiled=True)
    piece_rows = new_piece.shape[0]
    stride = block_size(piece_rows)
    new_blocks = new_piece.reshape(piece_rows // stride, stride, -1)
    cache_blocks = cache_piece.reshape(piece_rows // stride, 2 * stride, kv_local, 2, head_dim)
    offsets = stride * jnp.arange(piece_rows // stride, dtype=jnp.int32)
    everything = jnp.ones((tokens_here, 2 * stride), bool)

    def visit(carried_in, block_part):
        new_block, cache_block, key_first = block_part
        carried_in = new_keys_part(carried_in, new_block, key_first)
        carried_in = lax.cond(
            holds_first,
            lambda inner: attend_block(
                inner, query_heads, everything, cache_block[:, :, 0], cache_block[:, :, 1]
            ),
            lambda inner: inner,
            carried_in,
        )
        return (carried_in, None)

    carried, _ = lax.scan(visit, carried, (new_blocks, cache_blocks, offsets))
    best_final, total_final, summed_final = carried
    attended = (
        (summed_final / total_final[..., None])
        .transpose(2, 0, 1, 3)
        .reshape(tokens_here, -1)
        .astype(jnp.bfloat16)
    )
    mixed_rows = lax.psum_scatter(
        jnp.dot(attended, o_weight, preferred_element_type=jnp.float32).astype(jnp.bfloat16),
        "exp",
        scatter_dimension=0,
        tiled=True,
    ).astype(jnp.float32)
    moe_rows = mixed_rows.shape[0]
    residual = (
        lax.dynamic_slice_in_dim(hidden_in, exp_index * moe_rows, moe_rows, 0).astype(jnp.float32)
        + residual_scale * mixed_rows
    )
    moe_in = rms_norm(residual, moe_gain)
    top_count = routes.shape[1]
    experts_here = expert_in.shape[0]
    capacity = 2 * moe_rows * top_count // EXPERTS
    share = route_prob / jnp.sum(route_prob, axis=-1, keepdims=True)
    expert_ids = jnp.arange(EXPERTS, dtype=jnp.int32)
    route_hits = routes[:, :, None] == expert_ids[None, None, :]
    full_weight = jnp.sum(jnp.where(route_hits, share[:, :, None], 0.0), axis=1)
    full_hi = full_weight.astype(jnp.bfloat16)
    full_lo = (full_weight - full_hi.astype(jnp.float32)).astype(jnp.bfloat16)
    full_named = jnp.any(route_hits, axis=1).astype(jnp.bfloat16)
    model_width = moe_in.shape[1]
    side_width = 128 * pl_cdiv(3 * EXPERTS, 128)
    side = jnp.concatenate(
        [
            full_named,
            full_hi,
            full_lo,
            jnp.zeros((moe_rows, side_width - 3 * EXPERTS), jnp.bfloat16),
        ],
        axis=1,
    )
    packed_all = lax.all_gather(
        jnp.concatenate([moe_in, side], axis=1), "seq", axis=0, tiled=True
    )
    rows_all = packed_all[:, :model_width]
    total_rows = rows_all.shape[0]
    local_first = seq_index * experts_here
    side_all = packed_all[:, model_width:]
    named = (
        lax.dynamic_slice_in_dim(side_all, local_first, experts_here, 1) > 0
    )
    weight_hi = lax.dynamic_slice_in_dim(side_all, EXPERTS + local_first, experts_here, 1)
    weight_lo = lax.dynamic_slice_in_dim(side_all, 2 * EXPERTS + local_first, experts_here, 1)
    named_blocks = named.reshape(seq_count, moe_rows, experts_here).astype(jnp.int32)
    rank = jnp.cumsum(named_blocks, axis=1) - named_blocks
    slot = (jnp.arange(seq_count, dtype=jnp.int32)[:, None, None] * capacity + rank).reshape(
        total_rows, experts_here
    )
    slots_total = seq_count * capacity
    picks = named[:, :, None] & (
        slot[:, :, None] == jnp.arange(slots_total, dtype=jnp.int32)[None, None, :]
    )
    onehot = picks.astype(jnp.bfloat16)
    rows_in = jnp.einsum(
        "nec,nd->ecd", onehot, rows_all, preferred_element_type=jnp.float32
    ).astype(jnp.bfloat16)
    hidden = jnp.einsum("ecd,edf->ecf", rows_in, expert_in, preferred_element_type=jnp.float32)
    half_width = hidden.shape[-1] // 2
    active = (jax.nn.silu(hidden[..., :half_width]) * hidden[..., half_width:]).astype(jnp.bfloat16)
    produced = jnp.einsum(
        "ecf,efd->ecd", active, expert_out, preferred_element_type=jnp.float32
    ).astype(jnp.bfloat16)
    scaled_hi = jnp.where(picks, weight_hi[:, :, None], jnp.zeros_like(onehot))
    scaled_lo = jnp.where(picks, weight_lo[:, :, None], jnp.zeros_like(onehot))
    partial = jnp.einsum(
        "nec,ecd->nd", scaled_hi, produced, preferred_element_type=jnp.float32
    ) + jnp.einsum("nec,ecd->nd", scaled_lo, produced, preferred_element_type=jnp.float32)
    returned = lax.all_to_all(
        partial.astype(jnp.bfloat16).reshape(seq_count, moe_rows, -1),
        "seq",
        split_axis=0,
        concat_axis=0,
        tiled=True,
    )
    moe = jnp.sum(returned.astype(jnp.float32), axis=0)
    hidden_out = (residual + residual_scale * moe).astype(jnp.bfloat16)
    return (hidden_out, page_rows)


def solution(mesh):
    return jax.shard_map(
        body,
        mesh=mesh,
        in_specs=(
            P("seq", None),
            P(),
            P(None, "exp"),
            P(None, "exp"),
            P(None, "exp"),
            P("exp", None),
            P("seq", "exp"),
            P(),
            P("seq", None, None),
            P("seq", None, None),
            P(("seq", "exp"), None),
            P(("seq", "exp"), None),
            P(),
        ),
        out_specs=(P(("seq", "exp"), None), P("seq", "exp", None, None)),
        check_vma=False,
    )
```

```python
import math

import jax
import jax.numpy as jnp
from jax import lax
from jax.sharding import Mesh, PartitionSpec as P

HEADS = 24
KV_HEADS = 8
HEAD_DIM = 64
EXPERTS = 32
PAGE = 8
SEQ_AXES = ("half", "hseq")


norm_epsilon = 1e-06
attention_scale = 0.015625
residual_scale = 0.22
masked_score = -1e30


def rms_norm(values, gain_row):
    widened = values.astype(jnp.float32)
    spread = lax.rsqrt(jnp.mean(widened * widened, axis=-1, keepdims=True) + norm_epsilon)
    return (widened * spread * gain_row).astype(jnp.bfloat16)


def attend_block(carried, query_heads, visible, key_rows, value_rows):
    best_old, total_old, summed_old = carried
    scores = (
        jnp.einsum("tkgd,knd->kgtn", query_heads, key_rows, preferred_element_type=jnp.float32)
        * attention_scale
    )
    scores = jnp.where(visible, scores, masked_score)
    best_new = jnp.maximum(best_old, jnp.max(scores, axis=-1))
    weights = jnp.where(visible, jnp.exp(scores - best_new[..., None]), 0.0)
    factor = jnp.exp(best_old - best_new)
    total_new = total_old * factor + jnp.sum(weights, axis=-1)
    summed_new = summed_old * factor[..., None] + jnp.einsum(
        "kgtn,knd->kgtd",
        weights.astype(jnp.bfloat16),
        value_rows,
        preferred_element_type=jnp.float32,
    )
    return (best_new, total_new, summed_new)


def pl_cdiv(a, b):
    return -(-a // b)


def block_size(piece_rows):
    return math.gcd(piece_rows, 512)


def body(
    hidden_in,
    attn_gain,
    q_weight,
    k_weight,
    v_weight,
    o_weight,
    cache_kv,
    moe_gain,
    expert_in,
    expert_out,
    routes,
    route_prob,
    page_slot,
):
    halves = lax.axis_size("half")
    half_size = lax.axis_size("hseq")
    seq_count = halves * half_size
    half_index = lax.axis_index("half")
    half_pos = lax.axis_index("hseq")
    seq_index = half_index * half_size + half_pos
    exp_index = lax.axis_index("exp")
    tokens_here = hidden_in.shape[0]
    head_dim = HEAD_DIM
    kv_local = k_weight.shape[1] // head_dim
    group_size = HEADS // KV_HEADS
    holds_first = half_index == 0
    normed = rms_norm(hidden_in, attn_gain)
    queries = jnp.dot(normed, q_weight, preferred_element_type=jnp.float32).astype(jnp.bfloat16)
    keys_new = jnp.dot(normed, k_weight, preferred_element_type=jnp.float32).astype(jnp.bfloat16)
    values_new = jnp.dot(normed, v_weight, preferred_element_type=jnp.float32).astype(jnp.bfloat16)
    pair_width = 2 * kv_local * head_dim
    split_new = jnp.stack(
        [
            keys_new.reshape(tokens_here, kv_local, head_dim),
            values_new.reshape(tokens_here, kv_local, head_dim),
        ],
        axis=2,
    )
    pairs_new = split_new.reshape(tokens_here, pair_width)
    query_heads = queries.reshape(tokens_here, kv_local, group_size, head_dim)
    blocks_here = tokens_here // PAGE
    rounds = blocks_here // seq_count
    outgoing = pairs_new.reshape(rounds, seq_count, PAGE * pair_width)
    received = lax.all_to_all(outgoing, SEQ_AXES, split_axis=1, concat_axis=1, tiled=True)
    block_ids = (
        jnp.arange(seq_count, dtype=jnp.int32)[None, :] * blocks_here
        + jnp.arange(rounds, dtype=jnp.int32)[:, None] * seq_count
        + seq_index
    ).reshape(-1)
    table_ids = jnp.arange(page_slot.shape[0], dtype=jnp.int32)
    page_slots = jnp.sum(
        jnp.where(block_ids[:, None] == table_ids[None, :], page_slot[None, :], 0), axis=1
    )
    local_pages = (
        jnp.zeros((blocks_here, PAGE * pair_width), jnp.bfloat16)
        .at[page_slots]
        .set(received.reshape(blocks_here, -1))
    )
    page_rows = local_pages.reshape(blocks_here, PAGE, kv_local, 2, head_dim).transpose(
        0, 2, 3, 1, 4
    )
    page_rows = page_rows.reshape(blocks_here, kv_local, 2, PAGE * head_dim)
    start_state = (
        jnp.full((kv_local, group_size, tokens_here), masked_score, jnp.float32),
        jnp.zeros((kv_local, group_size, tokens_here), jnp.float32),
        jnp.zeros((kv_local, group_size, tokens_here, head_dim), jnp.float32),
    )
    kv_own = split_new.transpose(2, 1, 0, 3)
    kv_half = lax.all_gather(kv_own, "hseq", axis=2, tiled=True)
    cache_rows = cache_kv.shape[0]
    cache_own = cache_kv.reshape(cache_rows, kv_local, 2, head_dim).transpose(2, 1, 0, 3)
    cache_far = lax.ppermute(cache_own, "half", perm=[(1, 0)])
    cache_piece = jnp.concatenate([cache_own, cache_far], axis=2)
    cache_all = lax.all_gather(cache_piece, "hseq", axis=2, tiled=True)
    query_pos = half_pos * tokens_here + jnp.arange(tokens_here, dtype=jnp.int32)
    key_pos = jnp.arange(kv_half.shape[2], dtype=jnp.int32)
    visible_new = key_pos[None, :] <= query_pos[:, None]
    carried = attend_block(start_state, query_heads, visible_new, kv_half[0], kv_half[1])
    stride = block_size(cache_all.shape[2])
    cache_blocks = cache_all.reshape(2, kv_local, cache_all.shape[2] // stride, stride, head_dim)
    cache_blocks = cache_blocks.transpose(2, 0, 1, 3, 4)
    everything = jnp.ones((tokens_here, stride), bool)

    def visit(carried_in, cache_block):
        carried_in = lax.cond(
            holds_first,
            lambda inner: attend_block(
                inner, query_heads, everything, cache_block[0], cache_block[1]
            ),
            lambda inner: inner,
            carried_in,
        )
        return (carried_in, None)

    carried, _ = lax.scan(visit, carried, cache_blocks)
    best_final, total_final, summed_final = carried
    attended = (
        (summed_final / total_final[..., None])
        .transpose(2, 0, 1, 3)
        .reshape(tokens_here, -1)
        .astype(jnp.bfloat16)
    )
    mixed_rows = lax.psum_scatter(
        jnp.dot(attended, o_weight, preferred_element_type=jnp.float32).astype(jnp.bfloat16),
        "exp",
        scatter_dimension=0,
        tiled=True,
    ).astype(jnp.float32)
    moe_rows = mixed_rows.shape[0]
    residual = (
        lax.dynamic_slice_in_dim(hidden_in, exp_index * moe_rows, moe_rows, 0).astype(jnp.float32)
        + residual_scale * mixed_rows
    )
    moe_in = rms_norm(residual, moe_gain)
    top_count = routes.shape[1]
    experts_here = expert_in.shape[0]
    capacity = 2 * moe_rows * top_count // EXPERTS
    share = route_prob / jnp.sum(route_prob, axis=-1, keepdims=True)
    expert_ids = jnp.arange(EXPERTS, dtype=jnp.int32)
    route_hits = routes[:, :, None] == expert_ids[None, None, :]
    full_weight = jnp.sum(jnp.where(route_hits, share[:, :, None], 0.0), axis=1)
    full_hi = full_weight.astype(jnp.bfloat16)
    full_lo = (full_weight - full_hi.astype(jnp.float32)).astype(jnp.bfloat16)
    full_named = jnp.any(route_hits, axis=1).astype(jnp.bfloat16)
    model_width = moe_in.shape[1]
    side_width = 128 * pl_cdiv(3 * EXPERTS, 128)
    side = jnp.concatenate(
        [
            full_named,
            full_hi,
            full_lo,
            jnp.zeros((moe_rows, side_width - 3 * EXPERTS), jnp.bfloat16),
        ],
        axis=1,
    )
    packed_all = lax.all_gather(
        jnp.concatenate([moe_in, side], axis=1), SEQ_AXES, axis=0, tiled=True
    )
    rows_all = packed_all[:, :model_width]
    total_rows = rows_all.shape[0]
    local_first = seq_index * experts_here
    side_all = packed_all[:, model_width:]
    named = (
        lax.dynamic_slice_in_dim(side_all, local_first, experts_here, 1) > 0
    )
    weight_hi = lax.dynamic_slice_in_dim(side_all, EXPERTS + local_first, experts_here, 1)
    weight_lo = lax.dynamic_slice_in_dim(side_all, 2 * EXPERTS + local_first, experts_here, 1)
    named_blocks = named.reshape(seq_count, moe_rows, experts_here).astype(jnp.int32)
    rank = jnp.cumsum(named_blocks, axis=1) - named_blocks
    slot = (jnp.arange(seq_count, dtype=jnp.int32)[:, None, None] * capacity + rank).reshape(
        total_rows, experts_here
    )
    slots_total = seq_count * capacity
    picks = named[:, :, None] & (
        slot[:, :, None] == jnp.arange(slots_total, dtype=jnp.int32)[None, None, :]
    )
    onehot = picks.astype(jnp.bfloat16)
    rows_in = jnp.einsum(
        "nec,nd->ecd", onehot, rows_all, preferred_element_type=jnp.float32
    ).astype(jnp.bfloat16)
    hidden = jnp.einsum("ecd,edf->ecf", rows_in, expert_in, preferred_element_type=jnp.float32)
    half_width = hidden.shape[-1] // 2
    active = (jax.nn.silu(hidden[..., :half_width]) * hidden[..., half_width:]).astype(jnp.bfloat16)
    produced = jnp.einsum(
        "ecf,efd->ecd", active, expert_out, preferred_element_type=jnp.float32
    ).astype(jnp.bfloat16)
    scaled_hi = jnp.where(picks, weight_hi[:, :, None], jnp.zeros_like(onehot))
    scaled_lo = jnp.where(picks, weight_lo[:, :, None], jnp.zeros_like(onehot))
    partial = jnp.einsum(
        "nec,ecd->nd", scaled_hi, produced, preferred_element_type=jnp.float32
    ) + jnp.einsum("nec,ecd->nd", scaled_lo, produced, preferred_element_type=jnp.float32)
    returned = lax.all_to_all(
        partial.astype(jnp.bfloat16).reshape(seq_count, moe_rows, -1),
        SEQ_AXES,
        split_axis=0,
        concat_axis=0,
        tiled=True,
    )
    moe = jnp.sum(returned.astype(jnp.float32), axis=0)
    hidden_out = (residual + residual_scale * moe).astype(jnp.bfloat16)
    return (hidden_out, page_rows)


def solution(mesh):
    seq_count, exp_count = mesh.devices.shape
    split_mesh = Mesh(
        mesh.devices.reshape(2, seq_count // 2, exp_count), ("half", "hseq", "exp")
    )
    return jax.shard_map(
        body,
        mesh=split_mesh,
        in_specs=(
            P(SEQ_AXES, None),
            P(),
            P(None, "exp"),
            P(None, "exp"),
            P(None, "exp"),
            P("exp", None),
            P(SEQ_AXES, "exp"),
            P(),
            P(SEQ_AXES, None, None),
            P(SEQ_AXES, None, None),
            P(("half", "hseq", "exp"), None),
            P(("half", "hseq", "exp"), None),
            P(),
        ),
        out_specs=(P(("half", "hseq", "exp"), None), P(SEQ_AXES, "exp", None, None)),
        check_vma=False,
    )
```

```python
import functools
import math

import jax
import jax.numpy as jnp
from jax import lax
from jax.experimental import pallas as pl
from jax.experimental.pallas import tpu as pltpu
from jax.sharding import Mesh, PartitionSpec as P

HEADS = 24
KV_HEADS = 8
HEAD_DIM = 64
EXPERTS = 32
PAGE = 8
SEQ_AXES = ("half", "hseq")


norm_epsilon = 1e-06
attention_scale = 0.015625
residual_scale = 0.22
masked_score = -1e30


def rms_norm(values, gain_row):
    widened = values.astype(jnp.float32)
    spread = lax.rsqrt(jnp.mean(widened * widened, axis=-1, keepdims=True) + norm_epsilon)
    return (widened * spread * gain_row).astype(jnp.bfloat16)


KEY_BLOCK = 512


def flash_kernel(flags_ref, q_ref, ck_ref, cv_ref, nk_ref, nv_ref, o_ref, m_sc, l_sc, acc_sc, *, cache_blocks, group_rows):
    step = pl.program_id(1)
    last = pl.num_programs(1) - 1
    query_first = flags_ref[0]
    use_cache = flags_ref[1]

    @pl.when(step == 0)
    def _():
        m_sc[...] = jnp.full(m_sc.shape, masked_score, jnp.float32)
        l_sc[...] = jnp.zeros(l_sc.shape, jnp.float32)
        acc_sc[...] = jnp.zeros(acc_sc.shape, jnp.float32)

    def update(k_ref, v_ref, visible):
        q = q_ref[0]
        k = k_ref[0, 0]
        v = v_ref[0, 0]
        scores = lax.dot_general(q, k, (((1,), (1,)), ((), ())), preferred_element_type=jnp.float32) * attention_scale
        if visible is not None:
            scores = jnp.where(visible, scores, masked_score)
        m_prev = m_sc[...]
        m_new = jnp.maximum(m_prev, jnp.max(scores, axis=1, keepdims=True))
        weights = jnp.exp(scores - m_new)
        if visible is not None:
            weights = jnp.where(visible, weights, 0.0)
        factor = jnp.exp(m_prev - m_new)
        l_sc[...] = l_sc[...] * factor + jnp.sum(weights, axis=1, keepdims=True)
        acc_sc[...] = acc_sc[...] * factor + jnp.dot(weights.astype(jnp.bfloat16), v, preferred_element_type=jnp.float32)
        m_sc[...] = m_new

    @pl.when((step < cache_blocks) & (use_cache > 0))
    def _():
        update(ck_ref, cv_ref, None)

    new_first = (step - cache_blocks) * KEY_BLOCK

    @pl.when((step >= cache_blocks) & (new_first <= query_first + group_rows - 1))
    def _():
        rows = q_ref.shape[1]
        query_pos = query_first + lax.broadcasted_iota(jnp.int32, (rows, KEY_BLOCK), 0) % group_rows
        key_pos = new_first + lax.broadcasted_iota(jnp.int32, (rows, KEY_BLOCK), 1)
        update(nk_ref, nv_ref, key_pos <= query_pos)

    @pl.when(step == last)
    def _():
        o_ref[0] = (acc_sc[...] / l_sc[...]).astype(o_ref.dtype)


def flash_attend(flags, q, cache_all, kv_half, group_rows):
    heads, rows, dim = q.shape
    cache_blocks = cache_all.shape[2] // KEY_BLOCK
    new_blocks = kv_half.shape[2] // KEY_BLOCK
    kernel = functools.partial(flash_kernel, cache_blocks=cache_blocks, group_rows=group_rows)

    def cache_map(kind):
        return lambda h, s, f: (kind, h, jnp.minimum(s, cache_blocks - 1), 0)

    def new_map(kind):
        return lambda h, s, f: (kind, h, jnp.maximum(s - cache_blocks, 0), 0)

    kv_block = (1, 1, KEY_BLOCK, dim)
    return pl.pallas_call(
        kernel,
        out_shape=jax.ShapeDtypeStruct((heads, rows, dim), jnp.bfloat16),
        grid_spec=pltpu.PrefetchScalarGridSpec(
            num_scalar_prefetch=1,
            grid=(heads, cache_blocks + new_blocks),
            in_specs=[
                pl.BlockSpec((1, rows, dim), lambda h, s, f: (h, 0, 0)),
                pl.BlockSpec(kv_block, cache_map(0)),
                pl.BlockSpec(kv_block, cache_map(1)),
                pl.BlockSpec(kv_block, new_map(0)),
                pl.BlockSpec(kv_block, new_map(1)),
            ],
            out_specs=pl.BlockSpec((1, rows, dim), lambda h, s, f: (h, 0, 0)),
            scratch_shapes=[
                pltpu.VMEM((rows, 1), jnp.float32),
                pltpu.VMEM((rows, 1), jnp.float32),
                pltpu.VMEM((rows, dim), jnp.float32),
            ],
        ),
        compiler_params=pltpu.CompilerParams(dimension_semantics=("arbitrary", "arbitrary")),
    )(flags, q, cache_all, cache_all, kv_half, kv_half)


def pl_cdiv(a, b):
    return -(-a // b)


def block_size(piece_rows):
    return math.gcd(piece_rows, 512)


def body(
    hidden_in,
    attn_gain,
    q_weight,
    k_weight,
    v_weight,
    o_weight,
    cache_kv,
    moe_gain,
    expert_in,
    expert_out,
    routes,
    route_prob,
    page_slot,
):
    halves = lax.axis_size("half")
    half_size = lax.axis_size("hseq")
    seq_count = halves * half_size
    half_index = lax.axis_index("half")
    half_pos = lax.axis_index("hseq")
    seq_index = half_index * half_size + half_pos
    exp_index = lax.axis_index("exp")
    tokens_here = hidden_in.shape[0]
    head_dim = HEAD_DIM
    kv_local = k_weight.shape[1] // head_dim
    group_size = HEADS // KV_HEADS
    holds_first = half_index == 0
    normed = rms_norm(hidden_in, attn_gain)
    queries = jnp.dot(normed, q_weight, preferred_element_type=jnp.float32).astype(jnp.bfloat16)
    keys_new = jnp.dot(normed, k_weight, preferred_element_type=jnp.float32).astype(jnp.bfloat16)
    values_new = jnp.dot(normed, v_weight, preferred_element_type=jnp.float32).astype(jnp.bfloat16)
    pair_width = 2 * kv_local * head_dim
    split_new = jnp.stack(
        [
            keys_new.reshape(tokens_here, kv_local, head_dim),
            values_new.reshape(tokens_here, kv_local, head_dim),
        ],
        axis=2,
    )
    pairs_new = split_new.reshape(tokens_here, pair_width)
    blocks_here = tokens_here // PAGE
    rounds = blocks_here // seq_count
    outgoing = pairs_new.reshape(rounds, seq_count, PAGE * pair_width)
    received = lax.all_to_all(outgoing, SEQ_AXES, split_axis=1, concat_axis=1, tiled=True)
    block_ids = (
        jnp.arange(seq_count, dtype=jnp.int32)[None, :] * blocks_here
        + jnp.arange(rounds, dtype=jnp.int32)[:, None] * seq_count
        + seq_index
    ).reshape(-1)
    table_ids = jnp.arange(page_slot.shape[0], dtype=jnp.int32)
    page_slots = jnp.sum(
        jnp.where(block_ids[:, None] == table_ids[None, :], page_slot[None, :], 0), axis=1
    )
    local_pages = (
        jnp.zeros((blocks_here, PAGE * pair_width), jnp.bfloat16)
        .at[page_slots]
        .set(received.reshape(blocks_here, -1))
    )
    page_rows = local_pages.reshape(blocks_here, PAGE, kv_local, 2, head_dim).transpose(
        0, 2, 3, 1, 4
    )
    page_rows = page_rows.reshape(blocks_here, kv_local, 2, PAGE * head_dim)
    kv_own = split_new.transpose(2, 1, 0, 3)
    kv_half = lax.all_gather(kv_own, "hseq", axis=2, tiled=True)
    cache_rows = cache_kv.shape[0]
    cache_own = cache_kv.reshape(cache_rows, kv_local, 2, head_dim).transpose(2, 1, 0, 3)
    cache_far = lax.ppermute(cache_own, "half", perm=[(1, 0)])
    cache_piece = jnp.concatenate([cache_own, cache_far], axis=2)
    cache_all = lax.all_gather(cache_piece, "hseq", axis=2, tiled=True)
    query_rows = queries.reshape(tokens_here, kv_local, group_size, head_dim)
    query_rows = query_rows.transpose(1, 2, 0, 3).reshape(kv_local, group_size * tokens_here, head_dim)
    flags = jnp.stack([half_pos * tokens_here, holds_first.astype(jnp.int32)]).astype(jnp.int32)
    attended = flash_attend(flags, query_rows, cache_all, kv_half, tokens_here)
    attended = attended.reshape(kv_local, group_size, tokens_here, head_dim).transpose(2, 0, 1, 3)
    attended = attended.reshape(tokens_here, -1)
    mixed_rows = lax.psum_scatter(
        jnp.dot(attended, o_weight, preferred_element_type=jnp.float32).astype(jnp.bfloat16),
        "exp",
        scatter_dimension=0,
        tiled=True,
    ).astype(jnp.float32)
    moe_rows = mixed_rows.shape[0]
    residual = (
        lax.dynamic_slice_in_dim(hidden_in, exp_index * moe_rows, moe_rows, 0).astype(jnp.float32)
        + residual_scale * mixed_rows
    )
    moe_in = rms_norm(residual, moe_gain)
    top_count = routes.shape[1]
    experts_here = expert_in.shape[0]
    capacity = 2 * moe_rows * top_count // EXPERTS
    share = route_prob / jnp.sum(route_prob, axis=-1, keepdims=True)
    expert_ids = jnp.arange(EXPERTS, dtype=jnp.int32)
    route_hits = routes[:, :, None] == expert_ids[None, None, :]
    full_weight = jnp.sum(jnp.where(route_hits, share[:, :, None], 0.0), axis=1)
    full_hi = full_weight.astype(jnp.bfloat16)
    full_lo = (full_weight - full_hi.astype(jnp.float32)).astype(jnp.bfloat16)
    full_named = jnp.any(route_hits, axis=1).astype(jnp.bfloat16)
    model_width = moe_in.shape[1]
    side_width = 128 * pl_cdiv(3 * EXPERTS, 128)
    side = jnp.concatenate(
        [
            full_named,
            full_hi,
            full_lo,
            jnp.zeros((moe_rows, side_width - 3 * EXPERTS), jnp.bfloat16),
        ],
        axis=1,
    )
    packed_all = lax.all_gather(
        jnp.concatenate([moe_in, side], axis=1), SEQ_AXES, axis=0, tiled=True
    )
    rows_all = packed_all[:, :model_width]
    total_rows = rows_all.shape[0]
    local_first = seq_index * experts_here
    side_all = packed_all[:, model_width:]
    named = (
        lax.dynamic_slice_in_dim(side_all, local_first, experts_here, 1) > 0
    )
    weight_hi = lax.dynamic_slice_in_dim(side_all, EXPERTS + local_first, experts_here, 1)
    weight_lo = lax.dynamic_slice_in_dim(side_all, 2 * EXPERTS + local_first, experts_here, 1)
    named_blocks = named.reshape(seq_count, moe_rows, experts_here).astype(jnp.int32)
    rank = jnp.cumsum(named_blocks, axis=1) - named_blocks
    slot = (jnp.arange(seq_count, dtype=jnp.int32)[:, None, None] * capacity + rank).reshape(
        total_rows, experts_here
    )
    slots_total = seq_count * capacity
    picks = named[:, :, None] & (
        slot[:, :, None] == jnp.arange(slots_total, dtype=jnp.int32)[None, None, :]
    )
    onehot = picks.astype(jnp.bfloat16)
    rows_in = jnp.einsum(
        "nec,nd->ecd", onehot, rows_all, preferred_element_type=jnp.float32
    ).astype(jnp.bfloat16)
    hidden = jnp.einsum("ecd,edf->ecf", rows_in, expert_in, preferred_element_type=jnp.float32)
    half_width = hidden.shape[-1] // 2
    active = (jax.nn.silu(hidden[..., :half_width]) * hidden[..., half_width:]).astype(jnp.bfloat16)
    produced = jnp.einsum(
        "ecf,efd->ecd", active, expert_out, preferred_element_type=jnp.float32
    ).astype(jnp.bfloat16)
    scaled_hi = jnp.where(picks, weight_hi[:, :, None], jnp.zeros_like(onehot))
    scaled_lo = jnp.where(picks, weight_lo[:, :, None], jnp.zeros_like(onehot))
    partial = jnp.einsum(
        "nec,ecd->nd", scaled_hi, produced, preferred_element_type=jnp.float32
    ) + jnp.einsum("nec,ecd->nd", scaled_lo, produced, preferred_element_type=jnp.float32)
    returned = lax.all_to_all(
        partial.astype(jnp.bfloat16).reshape(seq_count, moe_rows, -1),
        SEQ_AXES,
        split_axis=0,
        concat_axis=0,
        tiled=True,
    )
    moe = jnp.sum(returned.astype(jnp.float32), axis=0)
    hidden_out = (residual + residual_scale * moe).astype(jnp.bfloat16)
    return (hidden_out, page_rows)


def solution(mesh):
    seq_count, exp_count = mesh.devices.shape
    split_mesh = Mesh(
        mesh.devices.reshape(2, seq_count // 2, exp_count), ("half", "hseq", "exp")
    )
    return jax.shard_map(
        body,
        mesh=split_mesh,
        in_specs=(
            P(SEQ_AXES, None),
            P(),
            P(None, "exp"),
            P(None, "exp"),
            P(None, "exp"),
            P("exp", None),
            P(SEQ_AXES, "exp"),
            P(),
            P(SEQ_AXES, None, None),
            P(SEQ_AXES, None, None),
            P(("half", "hseq", "exp"), None),
            P(("half", "hseq", "exp"), None),
            P(),
        ),
        out_specs=(P(("half", "hseq", "exp"), None), P(SEQ_AXES, "exp", None, None)),
        check_vma=False,
    )
```

```python
import functools
import math

import jax
import jax.numpy as jnp
from jax import lax
from jax.experimental import pallas as pl
from jax.experimental.pallas import tpu as pltpu
from jax.sharding import Mesh, PartitionSpec as P

HEADS = 24
KV_HEADS = 8
HEAD_DIM = 64
EXPERTS = 32
PAGE = 8
SEQ_AXES = ("half", "hseq")


norm_epsilon = 1e-06
attention_scale = 0.015625
residual_scale = 0.22
masked_score = -1e30


def rms_norm(values, gain_row):
    widened = values.astype(jnp.float32)
    spread = lax.rsqrt(jnp.mean(widened * widened, axis=-1, keepdims=True) + norm_epsilon)
    return (widened * spread * gain_row).astype(jnp.bfloat16)


def partial_kernel(
    flags_ref, q_ref, k_ref, v_ref, acc_ref, m_ref, l_ref, m_sc, l_sc, acc_sc, *, mode, cache_per,
    new_per, key_block, group_rows
):
    step = pl.program_id(1)
    last = pl.num_programs(1) - 1
    query_first = flags_ref[0]
    stride = cache_per + new_per
    if mode == "all":
        within = step % stride
        new_index = (step // stride) * new_per + within - cache_per
    elif mode == "new":
        within = cache_per
        new_index = step
    else:
        within = 0
        new_index = 0
    new_first = new_index * key_block

    @pl.when(step == 0)
    def _():
        m_sc[...] = jnp.full(m_sc.shape, masked_score, jnp.float32)
        l_sc[...] = jnp.zeros(l_sc.shape, jnp.float32)
        acc_sc[...] = jnp.zeros(acc_sc.shape, jnp.float32)

    def update(visible):
        q = q_ref[0]
        k = k_ref[0, 0]
        v = v_ref[0, 0]
        scores = lax.dot_general(
            q, k, (((1,), (1,)), ((), ())), preferred_element_type=jnp.float32
        ) * attention_scale
        if visible is not None:
            scores = jnp.where(visible, scores, masked_score)
        m_prev = m_sc[...]
        m_new = jnp.maximum(m_prev, jnp.max(scores, axis=1, keepdims=True))
        weights = jnp.exp(scores - m_new)
        if visible is not None:
            weights = jnp.where(visible, weights, 0.0)
        factor = jnp.exp(m_prev - m_new)
        l_sc[...] = l_sc[...] * factor + jnp.sum(weights, axis=1, keepdims=True)
        acc_sc[...] = acc_sc[...] * factor + jnp.dot(
            weights.astype(jnp.bfloat16), v, preferred_element_type=jnp.float32
        )
        m_sc[...] = m_new

    if mode != "new":

        @pl.when(within < cache_per)
        def _():
            update(None)

    if mode != "cache":

        @pl.when((within >= cache_per) & (new_first <= query_first + group_rows - 1))
        def _():
            rows = q_ref.shape[1]
            query_pos = (
                query_first + lax.broadcasted_iota(jnp.int32, (rows, key_block), 0) % group_rows
            )
            key_pos = new_first + lax.broadcasted_iota(jnp.int32, (rows, key_block), 1)
            update(key_pos <= query_pos)

    @pl.when(step == last)
    def _():
        acc_ref[0] = acc_sc[...]
        m_ref[0] = m_sc[...]
        l_ref[0] = l_sc[...]


def attend_partial(flags, q, kv_all, mode, cache_per, new_per, key_block, group_rows):
    heads, rows, dim = q.shape
    stride = cache_per + new_per
    devices = kv_all.shape[2] // (key_block * stride)
    if mode == "all":
        steps = devices * stride
        block_of = lambda s: s
    elif mode == "new":
        steps = devices * new_per
        block_of = lambda s: (s // new_per) * stride + cache_per + s % new_per
    else:
        steps = devices * cache_per
        block_of = lambda s: (s // cache_per) * stride + s % cache_per
    kernel = functools.partial(
        partial_kernel,
        mode=mode,
        cache_per=cache_per,
        new_per=new_per,
        key_block=key_block,
        group_rows=group_rows,
    )
    kv_block = (1, 1, key_block, dim)
    row_block = pl.BlockSpec((1, rows, 1), lambda h, s, f: (h, 0, 0))
    return pl.pallas_call(
        kernel,
        out_shape=(
            jax.ShapeDtypeStruct((heads, rows, dim), jnp.float32),
            jax.ShapeDtypeStruct((heads, rows, 1), jnp.float32),
            jax.ShapeDtypeStruct((heads, rows, 1), jnp.float32),
        ),
        grid_spec=pltpu.PrefetchScalarGridSpec(
            num_scalar_prefetch=1,
            grid=(heads, steps),
            in_specs=[
                pl.BlockSpec((1, rows, dim), lambda h, s, f: (h, 0, 0)),
                pl.BlockSpec(kv_block, lambda h, s, f: (0, h, block_of(s), 0)),
                pl.BlockSpec(kv_block, lambda h, s, f: (1, h, block_of(s), 0)),
            ],
            out_specs=[pl.BlockSpec((1, rows, dim), lambda h, s, f: (h, 0, 0)), row_block, row_block],
            scratch_shapes=[
                pltpu.VMEM((rows, 1), jnp.float32),
                pltpu.VMEM((rows, 1), jnp.float32),
                pltpu.VMEM((rows, dim), jnp.float32),
            ],
        ),
        compiler_params=pltpu.CompilerParams(dimension_semantics=("arbitrary", "arbitrary")),
    )(flags, q, kv_all, kv_all)


def pl_cdiv(a, b):
    return -(-a // b)


def block_size(piece_rows):
    return math.gcd(piece_rows, 512)


def body(
    hidden_in,
    attn_gain,
    q_weight,
    k_weight,
    v_weight,
    o_weight,
    cache_kv,
    moe_gain,
    expert_in,
    expert_out,
    routes,
    route_prob,
    page_slot,
):
    halves = lax.axis_size("half")
    half_size = lax.axis_size("hseq")
    seq_count = halves * half_size
    half_index = lax.axis_index("half")
    half_pos = lax.axis_index("hseq")
    seq_index = half_index * half_size + half_pos
    exp_index = lax.axis_index("exp")
    tokens_here = hidden_in.shape[0]
    head_dim = HEAD_DIM
    kv_local = k_weight.shape[1] // head_dim
    group_size = HEADS // KV_HEADS
    holds_first = half_index == 0
    normed = rms_norm(hidden_in, attn_gain)
    queries = jnp.dot(normed, q_weight, preferred_element_type=jnp.float32).astype(jnp.bfloat16)
    keys_new = jnp.dot(normed, k_weight, preferred_element_type=jnp.float32).astype(jnp.bfloat16)
    values_new = jnp.dot(normed, v_weight, preferred_element_type=jnp.float32).astype(jnp.bfloat16)
    pair_width = 2 * kv_local * head_dim
    split_new = jnp.stack(
        [
            keys_new.reshape(tokens_here, kv_local, head_dim),
            values_new.reshape(tokens_here, kv_local, head_dim),
        ],
        axis=2,
    )
    pairs_new = split_new.reshape(tokens_here, pair_width)
    blocks_here = tokens_here // PAGE
    rounds = blocks_here // seq_count
    outgoing = pairs_new.reshape(rounds, seq_count, PAGE * pair_width)
    received = lax.all_to_all(outgoing, SEQ_AXES, split_axis=1, concat_axis=1, tiled=True)
    block_ids = (
        jnp.arange(seq_count, dtype=jnp.int32)[None, :] * blocks_here
        + jnp.arange(rounds, dtype=jnp.int32)[:, None] * seq_count
        + seq_index
    ).reshape(-1)
    table_ids = jnp.arange(page_slot.shape[0], dtype=jnp.int32)
    page_slots = jnp.sum(
        jnp.where(block_ids[:, None] == table_ids[None, :], page_slot[None, :], 0), axis=1
    )
    local_pages = (
        jnp.zeros((blocks_here, PAGE * pair_width), jnp.bfloat16)
        .at[page_slots]
        .set(received.reshape(blocks_here, -1))
    )
    page_rows = local_pages.reshape(blocks_here, PAGE, kv_local, 2, head_dim).transpose(
        0, 2, 3, 1, 4
    )
    page_rows = page_rows.reshape(blocks_here, kv_local, 2, PAGE * head_dim)
    kv_own = split_new.transpose(2, 1, 0, 3)
    cache_rows = cache_kv.shape[0]
    cache_own = cache_kv.reshape(cache_rows, kv_local, 2, head_dim).transpose(2, 1, 0, 3)
    kv_all = lax.all_gather(
        jnp.concatenate([cache_own, kv_own], axis=2), "hseq", axis=2, tiled=True
    )
    key_block = math.gcd(math.gcd(cache_rows, tokens_here), 256)
    cache_per = cache_rows // key_block
    new_per = tokens_here // key_block
    query_rows = queries.reshape(tokens_here, kv_local, group_size, head_dim)
    query_rows = query_rows.transpose(1, 2, 0, 3).reshape(kv_local, group_size * tokens_here, head_dim)
    partner_rows = lax.ppermute(query_rows, "half", perm=[(0, 1)])
    flags = jnp.reshape(half_pos * tokens_here, (1,)).astype(jnp.int32)
    shapes = dict(cache_per=cache_per, new_per=new_per, key_block=key_block, group_rows=tokens_here)

    def empty_partial(rows_in):
        heads, rows, _ = rows_in.shape
        return (
            jnp.zeros((heads, rows, head_dim), jnp.float32),
            jnp.full((heads, rows, 1), masked_score, jnp.float32),
            jnp.zeros((heads, rows, 1), jnp.float32),
        )

    far_part = lax.cond(
        holds_first,
        empty_partial,
        lambda rows_in: attend_partial(flags, rows_in, kv_all, "cache", **shapes),
        partner_rows,
    )
    own_part = lax.cond(
        holds_first,
        lambda rows_in: attend_partial(flags, rows_in, kv_all, "all", **shapes),
        lambda rows_in: attend_partial(flags, rows_in, kv_all, "new", **shapes),
        query_rows,
    )
    back_acc, back_best, back_total = lax.ppermute(far_part, "half", perm=[(1, 0)])
    back_best = jnp.where(holds_first, back_best, masked_score)
    back_total = jnp.where(holds_first, back_total, 0.0)
    back_acc = jnp.where(holds_first, back_acc, 0.0)
    own_acc, own_best, own_total = own_part
    best = jnp.maximum(own_best, back_best)
    own_scale = jnp.exp(own_best - best)
    back_scale = jnp.exp(back_best - best)
    attended = (own_acc * own_scale + back_acc * back_scale) / (
        own_total * own_scale + back_total * back_scale
    )
    attended = attended.astype(jnp.bfloat16).reshape(kv_local, group_size, tokens_here, head_dim)
    attended = attended.transpose(2, 0, 1, 3).reshape(tokens_here, -1)
    mixed_rows = lax.psum_scatter(
        jnp.dot(attended, o_weight, preferred_element_type=jnp.float32).astype(jnp.bfloat16),
        "exp",
        scatter_dimension=0,
        tiled=True,
    ).astype(jnp.float32)
    moe_rows = mixed_rows.shape[0]
    residual = (
        lax.dynamic_slice_in_dim(hidden_in, exp_index * moe_rows, moe_rows, 0).astype(jnp.float32)
        + residual_scale * mixed_rows
    )
    moe_in = rms_norm(residual, moe_gain)
    top_count = routes.shape[1]
    experts_here = expert_in.shape[0]
    capacity = 2 * moe_rows * top_count // EXPERTS
    share = route_prob / jnp.sum(route_prob, axis=-1, keepdims=True)
    expert_ids = jnp.arange(EXPERTS, dtype=jnp.int32)
    route_hits = routes[:, :, None] == expert_ids[None, None, :]
    full_weight = jnp.sum(jnp.where(route_hits, share[:, :, None], 0.0), axis=1)
    full_hi = full_weight.astype(jnp.bfloat16)
    full_lo = (full_weight - full_hi.astype(jnp.float32)).astype(jnp.bfloat16)
    full_named = jnp.any(route_hits, axis=1).astype(jnp.bfloat16)
    model_width = moe_in.shape[1]
    side_width = 128 * pl_cdiv(3 * EXPERTS, 128)
    side = jnp.concatenate(
        [
            full_named,
            full_hi,
            full_lo,
            jnp.zeros((moe_rows, side_width - 3 * EXPERTS), jnp.bfloat16),
        ],
        axis=1,
    )
    packed_all = lax.all_gather(
        jnp.concatenate([moe_in, side], axis=1), SEQ_AXES, axis=0, tiled=True
    )
    rows_all = packed_all[:, :model_width]
    total_rows = rows_all.shape[0]
    local_first = seq_index * experts_here
    side_all = packed_all[:, model_width:]
    named = (
        lax.dynamic_slice_in_dim(side_all, local_first, experts_here, 1) > 0
    )
    weight_hi = lax.dynamic_slice_in_dim(side_all, EXPERTS + local_first, experts_here, 1)
    weight_lo = lax.dynamic_slice_in_dim(side_all, 2 * EXPERTS + local_first, experts_here, 1)
    named_blocks = named.reshape(seq_count, moe_rows, experts_here).astype(jnp.int32)
    rank = jnp.cumsum(named_blocks, axis=1) - named_blocks
    slot = (jnp.arange(seq_count, dtype=jnp.int32)[:, None, None] * capacity + rank).reshape(
        total_rows, experts_here
    )
    slots_total = seq_count * capacity
    picks = named[:, :, None] & (
        slot[:, :, None] == jnp.arange(slots_total, dtype=jnp.int32)[None, None, :]
    )
    onehot = picks.astype(jnp.bfloat16)
    rows_in = jnp.einsum(
        "nec,nd->ecd", onehot, rows_all, preferred_element_type=jnp.float32
    ).astype(jnp.bfloat16)
    hidden = jnp.einsum("ecd,edf->ecf", rows_in, expert_in, preferred_element_type=jnp.float32)
    half_width = hidden.shape[-1] // 2
    active = (jax.nn.silu(hidden[..., :half_width]) * hidden[..., half_width:]).astype(jnp.bfloat16)
    produced = jnp.einsum(
        "ecf,efd->ecd", active, expert_out, preferred_element_type=jnp.float32
    ).astype(jnp.bfloat16)
    scaled_hi = jnp.where(picks, weight_hi[:, :, None], jnp.zeros_like(onehot))
    scaled_lo = jnp.where(picks, weight_lo[:, :, None], jnp.zeros_like(onehot))
    partial = jnp.einsum(
        "nec,ecd->nd", scaled_hi, produced, preferred_element_type=jnp.float32
    ) + jnp.einsum("nec,ecd->nd", scaled_lo, produced, preferred_element_type=jnp.float32)
    returned = lax.all_to_all(
        partial.astype(jnp.bfloat16).reshape(seq_count, moe_rows, -1),
        SEQ_AXES,
        split_axis=0,
        concat_axis=0,
        tiled=True,
    )
    moe = jnp.sum(returned.astype(jnp.float32), axis=0)
    hidden_out = (residual + residual_scale * moe).astype(jnp.bfloat16)
    return (hidden_out, page_rows)


def solution(mesh):
    seq_count, exp_count = mesh.devices.shape
    split_mesh = Mesh(
        mesh.devices.reshape(2, seq_count // 2, exp_count), ("half", "hseq", "exp")
    )
    return jax.shard_map(
        body,
        mesh=split_mesh,
        in_specs=(
            P(SEQ_AXES, None),
            P(),
            P(None, "exp"),
            P(None, "exp"),
            P(None, "exp"),
            P("exp", None),
            P(SEQ_AXES, "exp"),
            P(),
            P(SEQ_AXES, None, None),
            P(SEQ_AXES, None, None),
            P(("half", "hseq", "exp"), None),
            P(("half", "hseq", "exp"), None),
            P(),
        ),
        out_specs=(P(("half", "hseq", "exp"), None), P(SEQ_AXES, "exp", None, None)),
        check_vma=False,
    )
```

```python
import functools
import math

import jax
import jax.numpy as jnp
from jax import lax
from jax.experimental import pallas as pl
from jax.experimental.pallas import tpu as pltpu
from jax.sharding import Mesh, PartitionSpec as P

HEADS = 24
KV_HEADS = 8
HEAD_DIM = 64
EXPERTS = 32
PAGE = 8
SEQ_AXES = ("half", "hseq")
EXP_AXES = ("ey", "ec")


norm_epsilon = 1e-06
attention_scale = 0.015625
residual_scale = 0.22
masked_score = -1e30


def rms_norm(values, gain_row):
    widened = values.astype(jnp.float32)
    spread = lax.rsqrt(jnp.mean(widened * widened, axis=-1, keepdims=True) + norm_epsilon)
    return (widened * spread * gain_row).astype(jnp.bfloat16)


def partial_kernel(
    flags_ref, q_ref, k_ref, v_ref, acc_ref, m_ref, l_ref, m_sc, l_sc, acc_sc, *, mode, cache_per,
    new_per, key_block, group_rows
):
    step = pl.program_id(1)
    last = pl.num_programs(1) - 1
    query_first = flags_ref[0]
    stride = cache_per + new_per
    if mode == "all":
        within = step % stride
        new_index = (step // stride) * new_per + within - cache_per
    elif mode == "new":
        within = cache_per
        new_index = step
    else:
        within = 0
        new_index = 0
    new_first = new_index * key_block

    @pl.when(step == 0)
    def _():
        m_sc[...] = jnp.full(m_sc.shape, masked_score, jnp.float32)
        l_sc[...] = jnp.zeros(l_sc.shape, jnp.float32)
        acc_sc[...] = jnp.zeros(acc_sc.shape, jnp.float32)

    def update(visible):
        q = q_ref[0]
        k = k_ref[0, 0]
        v = v_ref[0, 0]
        scores = lax.dot_general(
            q, k, (((1,), (1,)), ((), ())), preferred_element_type=jnp.float32
        ) * attention_scale
        if visible is not None:
            scores = jnp.where(visible, scores, masked_score)
        m_prev = m_sc[...]
        m_new = jnp.maximum(m_prev, jnp.max(scores, axis=1, keepdims=True))
        weights = jnp.exp(scores - m_new)
        if visible is not None:
            weights = jnp.where(visible, weights, 0.0)
        factor = jnp.exp(m_prev - m_new)
        l_sc[...] = l_sc[...] * factor + jnp.sum(weights, axis=1, keepdims=True)
        acc_sc[...] = acc_sc[...] * factor + jnp.dot(
            weights.astype(jnp.bfloat16), v, preferred_element_type=jnp.float32
        )
        m_sc[...] = m_new

    if mode != "new":

        @pl.when(within < cache_per)
        def _():
            update(None)

    if mode != "cache":

        @pl.when((within >= cache_per) & (new_first <= query_first + group_rows - 1))
        def _():
            rows = q_ref.shape[1]
            query_pos = (
                query_first + lax.broadcasted_iota(jnp.int32, (rows, key_block), 0) % group_rows
            )
            key_pos = new_first + lax.broadcasted_iota(jnp.int32, (rows, key_block), 1)
            update(key_pos <= query_pos)

    @pl.when(step == last)
    def _():
        acc_ref[0] = acc_sc[...]
        m_ref[0] = m_sc[...]
        l_ref[0] = l_sc[...]


def attend_partial(flags, q, kv_all, mode, cache_per, new_per, key_block, group_rows):
    heads, rows, dim = q.shape
    stride = cache_per + new_per
    devices = kv_all.shape[2] // (key_block * stride)
    if mode == "all":
        steps = devices * stride
        block_of = lambda s: s
    elif mode == "new":
        steps = devices * new_per
        block_of = lambda s: (s // new_per) * stride + cache_per + s % new_per
    else:
        steps = devices * cache_per
        block_of = lambda s: (s // cache_per) * stride + s % cache_per
    kernel = functools.partial(
        partial_kernel,
        mode=mode,
        cache_per=cache_per,
        new_per=new_per,
        key_block=key_block,
        group_rows=group_rows,
    )
    kv_block = (1, 1, key_block, dim)
    row_block = pl.BlockSpec((1, rows, 1), lambda h, s, f: (h, 0, 0))
    return pl.pallas_call(
        kernel,
        out_shape=(
            jax.ShapeDtypeStruct((heads, rows, dim), jnp.float32),
            jax.ShapeDtypeStruct((heads, rows, 1), jnp.float32),
            jax.ShapeDtypeStruct((heads, rows, 1), jnp.float32),
        ),
        grid_spec=pltpu.PrefetchScalarGridSpec(
            num_scalar_prefetch=1,
            grid=(heads, steps),
            in_specs=[
                pl.BlockSpec((1, rows, dim), lambda h, s, f: (h, 0, 0)),
                pl.BlockSpec(kv_block, lambda h, s, f: (0, h, block_of(s), 0)),
                pl.BlockSpec(kv_block, lambda h, s, f: (1, h, block_of(s), 0)),
            ],
            out_specs=[pl.BlockSpec((1, rows, dim), lambda h, s, f: (h, 0, 0)), row_block, row_block],
            scratch_shapes=[
                pltpu.VMEM((rows, 1), jnp.float32),
                pltpu.VMEM((rows, 1), jnp.float32),
                pltpu.VMEM((rows, dim), jnp.float32),
            ],
        ),
        compiler_params=pltpu.CompilerParams(dimension_semantics=("arbitrary", "arbitrary")),
    )(flags, q, kv_all, kv_all)


def pl_cdiv(a, b):
    return -(-a // b)


def block_size(piece_rows):
    return math.gcd(piece_rows, 512)


def body(
    hidden_in,
    attn_gain,
    q_weight,
    k_weight,
    v_weight,
    o_weight,
    cache_kv,
    moe_gain,
    expert_in,
    expert_out,
    routes,
    route_prob,
    page_slot,
):
    halves = lax.axis_size("half")
    half_size = lax.axis_size("hseq")
    seq_count = halves * half_size
    half_index = lax.axis_index("half")
    half_pos = lax.axis_index("hseq")
    seq_index = half_index * half_size + half_pos
    exp_index = lax.axis_index("ey") * lax.axis_size("ec") + lax.axis_index("ec")
    tokens_here = hidden_in.shape[0]
    head_dim = HEAD_DIM
    kv_local = k_weight.shape[1] // head_dim
    group_size = HEADS // KV_HEADS
    holds_first = half_index == 0
    normed = rms_norm(hidden_in, attn_gain)
    queries = jnp.dot(normed, q_weight, preferred_element_type=jnp.float32).astype(jnp.bfloat16)
    keys_new = jnp.dot(normed, k_weight, preferred_element_type=jnp.float32).astype(jnp.bfloat16)
    values_new = jnp.dot(normed, v_weight, preferred_element_type=jnp.float32).astype(jnp.bfloat16)
    pair_width = 2 * kv_local * head_dim
    split_new = jnp.stack(
        [
            keys_new.reshape(tokens_here, kv_local, head_dim),
            values_new.reshape(tokens_here, kv_local, head_dim),
        ],
        axis=2,
    )
    pairs_new = split_new.reshape(tokens_here, pair_width)
    blocks_here = tokens_here // PAGE
    rounds = blocks_here // seq_count
    outgoing = pairs_new.reshape(rounds, seq_count, PAGE * pair_width)
    received = lax.all_to_all(outgoing, SEQ_AXES, split_axis=1, concat_axis=1, tiled=True)
    block_ids = (
        jnp.arange(seq_count, dtype=jnp.int32)[None, :] * blocks_here
        + jnp.arange(rounds, dtype=jnp.int32)[:, None] * seq_count
        + seq_index
    ).reshape(-1)
    table_ids = jnp.arange(page_slot.shape[0], dtype=jnp.int32)
    page_slots = jnp.sum(
        jnp.where(block_ids[:, None] == table_ids[None, :], page_slot[None, :], 0), axis=1
    )
    local_pages = (
        jnp.zeros((blocks_here, PAGE * pair_width), jnp.bfloat16)
        .at[page_slots]
        .set(received.reshape(blocks_here, -1))
    )
    page_rows = local_pages.reshape(blocks_here, PAGE, kv_local, 2, head_dim).transpose(
        0, 2, 3, 1, 4
    )
    page_rows = page_rows.reshape(blocks_here, kv_local, 2, PAGE * head_dim)
    kv_own = split_new.transpose(2, 1, 0, 3)
    cache_rows = cache_kv.shape[0]
    cache_own = cache_kv.reshape(cache_rows, kv_local, 2, head_dim).transpose(2, 1, 0, 3)
    kv_all = lax.all_gather(
        jnp.concatenate([cache_own, kv_own], axis=2), "hseq", axis=2, tiled=True
    )
    key_block = math.gcd(math.gcd(cache_rows, tokens_here), 256)
    cache_per = cache_rows // key_block
    new_per = tokens_here // key_block
    query_rows = queries.reshape(tokens_here, kv_local, group_size, head_dim)
    query_rows = query_rows.transpose(1, 2, 0, 3).reshape(kv_local, group_size * tokens_here, head_dim)
    partner_rows = lax.ppermute(query_rows, "half", perm=[(0, 1)])
    flags = jnp.reshape(half_pos * tokens_here, (1,)).astype(jnp.int32)
    shapes = dict(cache_per=cache_per, new_per=new_per, key_block=key_block, group_rows=tokens_here)

    def empty_partial(rows_in):
        heads, rows, _ = rows_in.shape
        return (
            jnp.zeros((heads, rows, head_dim), jnp.float32),
            jnp.full((heads, rows, 1), masked_score, jnp.float32),
            jnp.zeros((heads, rows, 1), jnp.float32),
        )

    far_part = lax.cond(
        holds_first,
        empty_partial,
        lambda rows_in: attend_partial(flags, rows_in, kv_all, "cache", **shapes),
        partner_rows,
    )
    own_part = lax.cond(
        holds_first,
        lambda rows_in: attend_partial(flags, rows_in, kv_all, "all", **shapes),
        lambda rows_in: attend_partial(flags, rows_in, kv_all, "new", **shapes),
        query_rows,
    )
    back_acc, back_best, back_total = lax.ppermute(far_part, "half", perm=[(1, 0)])
    back_best = jnp.where(holds_first, back_best, masked_score)
    back_total = jnp.where(holds_first, back_total, 0.0)
    back_acc = jnp.where(holds_first, back_acc, 0.0)
    own_acc, own_best, own_total = own_part
    best = jnp.maximum(own_best, back_best)
    own_scale = jnp.exp(own_best - best)
    back_scale = jnp.exp(back_best - best)
    attended = (own_acc * own_scale + back_acc * back_scale) / (
        own_total * own_scale + back_total * back_scale
    )
    attended = attended.astype(jnp.bfloat16).reshape(kv_local, group_size, tokens_here, head_dim)
    attended = attended.transpose(2, 0, 1, 3).reshape(tokens_here, -1)
    ey_size = lax.axis_size("ey")
    ec_size = lax.axis_size("ec")
    projected = jnp.dot(attended, o_weight, preferred_element_type=jnp.float32).astype(jnp.bfloat16)
    projected = projected.reshape(ey_size, ec_size, -1, projected.shape[1]).transpose(1, 0, 2, 3)
    projected = projected.reshape(tokens_here, -1)
    on_chip = lax.psum_scatter(projected, "ec", scatter_dimension=0, tiled=True)
    mixed_rows = lax.psum_scatter(on_chip, "ey", scatter_dimension=0, tiled=True).astype(jnp.float32)
    moe_rows = mixed_rows.shape[0]
    residual = (
        lax.dynamic_slice_in_dim(hidden_in, exp_index * moe_rows, moe_rows, 0).astype(jnp.float32)
        + residual_scale * mixed_rows
    )
    moe_in = rms_norm(residual, moe_gain)
    top_count = routes.shape[1]
    experts_here = expert_in.shape[0]
    capacity = 2 * moe_rows * top_count // EXPERTS
    share = route_prob / jnp.sum(route_prob, axis=-1, keepdims=True)
    expert_ids = jnp.arange(EXPERTS, dtype=jnp.int32)
    route_hits = routes[:, :, None] == expert_ids[None, None, :]
    full_weight = jnp.sum(jnp.where(route_hits, share[:, :, None], 0.0), axis=1)
    full_hi = full_weight.astype(jnp.bfloat16)
    full_lo = (full_weight - full_hi.astype(jnp.float32)).astype(jnp.bfloat16)
    full_named = jnp.any(route_hits, axis=1).astype(jnp.bfloat16)
    model_width = moe_in.shape[1]
    side_width = 128 * pl_cdiv(3 * EXPERTS, 128)
    side = jnp.concatenate(
        [
            full_named,
            full_hi,
            full_lo,
            jnp.zeros((moe_rows, side_width - 3 * EXPERTS), jnp.bfloat16),
        ],
        axis=1,
    )
    crossed = lax.all_gather(
        jnp.concatenate([moe_in, side], axis=1), "half", axis=0, tiled=True
    )
    packed_all = lax.all_gather(crossed, "hseq", axis=0, tiled=True)
    rows_all = packed_all[:, :model_width]
    total_rows = rows_all.shape[0]
    local_first = seq_index * experts_here
    side_all = packed_all[:, model_width:]
    named = (
        lax.dynamic_slice_in_dim(side_all, local_first, experts_here, 1) > 0
    )
    weight_hi = lax.dynamic_slice_in_dim(side_all, EXPERTS + local_first, experts_here, 1)
    weight_lo = lax.dynamic_slice_in_dim(side_all, 2 * EXPERTS + local_first, experts_here, 1)
    named_blocks = named.reshape(seq_count, moe_rows, experts_here).astype(jnp.int32)
    rank = jnp.cumsum(named_blocks, axis=1) - named_blocks
    slot = (jnp.arange(seq_count, dtype=jnp.int32)[:, None, None] * capacity + rank).reshape(
        total_rows, experts_here
    )
    slots_total = seq_count * capacity
    picks = named[:, :, None] & (
        slot[:, :, None] == jnp.arange(slots_total, dtype=jnp.int32)[None, None, :]
    )
    onehot = picks.astype(jnp.bfloat16)
    rows_in = jnp.einsum(
        "nec,nd->ecd", onehot, rows_all, preferred_element_type=jnp.float32
    ).astype(jnp.bfloat16)
    hidden = jnp.einsum("ecd,edf->ecf", rows_in, expert_in, preferred_element_type=jnp.float32)
    half_width = hidden.shape[-1] // 2
    active = (jax.nn.silu(hidden[..., :half_width]) * hidden[..., half_width:]).astype(jnp.bfloat16)
    produced = jnp.einsum(
        "ecf,efd->ecd", active, expert_out, preferred_element_type=jnp.float32
    ).astype(jnp.bfloat16)
    scaled_hi = jnp.where(picks, weight_hi[:, :, None], jnp.zeros_like(onehot))
    scaled_lo = jnp.where(picks, weight_lo[:, :, None], jnp.zeros_like(onehot))
    partial = jnp.einsum(
        "nec,ecd->nd", scaled_hi, produced, preferred_element_type=jnp.float32
    ) + jnp.einsum("nec,ecd->nd", scaled_lo, produced, preferred_element_type=jnp.float32)
    partial = partial.astype(jnp.bfloat16).reshape(half_size, halves, moe_rows, -1)
    in_half = lax.psum_scatter(partial, "hseq", scatter_dimension=0, tiled=True)
    moe = lax.psum_scatter(
        in_half.reshape(halves, moe_rows, -1), "half", scatter_dimension=0, tiled=True
    )
    moe = moe.reshape(moe_rows, -1).astype(jnp.float32)
    hidden_out = (residual + residual_scale * moe).astype(jnp.bfloat16)
    return (hidden_out, page_rows)


def solution(mesh):
    seq_count, exp_count = mesh.devices.shape
    split_mesh = Mesh(
        mesh.devices.reshape(2, seq_count // 2, 2, exp_count // 2), SEQ_AXES + EXP_AXES
    )
    return jax.shard_map(
        body,
        mesh=split_mesh,
        in_specs=(
            P(SEQ_AXES, None),
            P(),
            P(None, EXP_AXES),
            P(None, EXP_AXES),
            P(None, EXP_AXES),
            P(EXP_AXES, None),
            P(SEQ_AXES, EXP_AXES),
            P(),
            P(SEQ_AXES, None, None),
            P(SEQ_AXES, None, None),
            P(SEQ_AXES + EXP_AXES, None),
            P(SEQ_AXES + EXP_AXES, None),
            P(),
        ),
        out_specs=(P(SEQ_AXES + EXP_AXES, None), P(SEQ_AXES, EXP_AXES, None, None)),
        check_vma=False,
    )
```

```python
import functools
import math

import jax
import jax.numpy as jnp
from jax import lax
from jax.experimental import pallas as pl
from jax.experimental.pallas import tpu as pltpu
from jax.sharding import Mesh, PartitionSpec as P

HEADS = 24
KV_HEADS = 8
HEAD_DIM = 64
EXPERTS = 32
PAGE = 8
SEQ_AXES = ("half", "hseq")


norm_epsilon = 1e-06
attention_scale = 0.015625
residual_scale = 0.22
masked_score = -1e30


def rms_norm(values, gain_row):
    widened = values.astype(jnp.float32)
    spread = lax.rsqrt(jnp.mean(widened * widened, axis=-1, keepdims=True) + norm_epsilon)
    return (widened * spread * gain_row).astype(jnp.bfloat16)


def partial_kernel(
    flags_ref, q_ref, k_ref, v_ref, acc_ref, m_ref, l_ref, m_sc, l_sc, acc_sc, *, mode, cache_per,
    new_per, key_block, group_rows
):
    step = pl.program_id(1)
    last = pl.num_programs(1) - 1
    query_first = flags_ref[0]
    stride = cache_per + new_per
    if mode == "all":
        within = step % stride
        new_index = (step // stride) * new_per + within - cache_per
    elif mode == "new":
        within = cache_per
        new_index = step
    else:
        within = 0
        new_index = 0
    new_first = new_index * key_block

    @pl.when(step == 0)
    def _():
        m_sc[...] = jnp.full(m_sc.shape, masked_score, jnp.float32)
        l_sc[...] = jnp.zeros(l_sc.shape, jnp.float32)
        acc_sc[...] = jnp.zeros(acc_sc.shape, jnp.float32)

    def update(visible):
        q = q_ref[0]
        k = k_ref[0, 0]
        v = v_ref[0, 0]
        scores = lax.dot_general(
            q, k, (((1,), (1,)), ((), ())), preferred_element_type=jnp.float32
        ) * attention_scale
        if visible is not None:
            scores = jnp.where(visible, scores, masked_score)
        m_prev = m_sc[...]
        m_new = jnp.maximum(m_prev, jnp.max(scores, axis=1, keepdims=True))
        weights = jnp.exp(scores - m_new)
        if visible is not None:
            weights = jnp.where(visible, weights, 0.0)
        factor = jnp.exp(m_prev - m_new)
        l_sc[...] = l_sc[...] * factor + jnp.sum(weights, axis=1, keepdims=True)
        acc_sc[...] = acc_sc[...] * factor + jnp.dot(
            weights.astype(jnp.bfloat16), v, preferred_element_type=jnp.float32
        )
        m_sc[...] = m_new

    if mode != "new":

        @pl.when(within < cache_per)
        def _():
            update(None)

    if mode != "cache":

        @pl.when((within >= cache_per) & (new_first <= query_first + group_rows - 1))
        def _():
            rows = q_ref.shape[1]
            query_pos = (
                query_first + lax.broadcasted_iota(jnp.int32, (rows, key_block), 0) % group_rows
            )
            key_pos = new_first + lax.broadcasted_iota(jnp.int32, (rows, key_block), 1)
            update(key_pos <= query_pos)

    @pl.when(step == last)
    def _():
        acc_ref[0] = acc_sc[...]
        m_ref[0] = m_sc[...]
        l_ref[0] = l_sc[...]


def attend_partial(flags, q, kv_all, mode, cache_per, new_per, key_block, group_rows):
    heads, rows, dim = q.shape
    stride = cache_per + new_per
    devices = kv_all.shape[2] // (key_block * stride)
    if mode == "all":
        steps = devices * stride
        block_of = lambda s: s
    elif mode == "new":
        steps = devices * new_per
        block_of = lambda s: (s // new_per) * stride + cache_per + s % new_per
    else:
        steps = devices * cache_per
        block_of = lambda s: (s // cache_per) * stride + s % cache_per
    kernel = functools.partial(
        partial_kernel,
        mode=mode,
        cache_per=cache_per,
        new_per=new_per,
        key_block=key_block,
        group_rows=group_rows,
    )
    kv_block = (1, 1, key_block, dim)
    row_block = pl.BlockSpec((1, rows, 1), lambda h, s, f: (h, 0, 0))
    return pl.pallas_call(
        kernel,
        out_shape=(
            jax.ShapeDtypeStruct((heads, rows, dim), jnp.float32),
            jax.ShapeDtypeStruct((heads, rows, 1), jnp.float32),
            jax.ShapeDtypeStruct((heads, rows, 1), jnp.float32),
        ),
        grid_spec=pltpu.PrefetchScalarGridSpec(
            num_scalar_prefetch=1,
            grid=(heads, steps),
            in_specs=[
                pl.BlockSpec((1, rows, dim), lambda h, s, f: (h, 0, 0)),
                pl.BlockSpec(kv_block, lambda h, s, f: (0, h, block_of(s), 0)),
                pl.BlockSpec(kv_block, lambda h, s, f: (1, h, block_of(s), 0)),
            ],
            out_specs=[pl.BlockSpec((1, rows, dim), lambda h, s, f: (h, 0, 0)), row_block, row_block],
            scratch_shapes=[
                pltpu.VMEM((rows, 1), jnp.float32),
                pltpu.VMEM((rows, 1), jnp.float32),
                pltpu.VMEM((rows, dim), jnp.float32),
            ],
        ),
        compiler_params=pltpu.CompilerParams(dimension_semantics=("arbitrary", "arbitrary")),
    )(flags, q, kv_all, kv_all)


def gather_by_all_to_all(values, axis_name, axis):
    count = lax.axis_size(axis_name)
    spread = jnp.broadcast_to(values[None], (count,) + values.shape)
    moved = lax.all_to_all(spread, axis_name, split_axis=0, concat_axis=0, tiled=True)
    moved = jnp.moveaxis(moved, 0, axis)
    shape = list(values.shape)
    shape[axis] = shape[axis] * count
    return moved.reshape(shape)


def pl_cdiv(a, b):
    return -(-a // b)


def block_size(piece_rows):
    return math.gcd(piece_rows, 512)


def body(
    hidden_in,
    attn_gain,
    q_weight,
    k_weight,
    v_weight,
    o_weight,
    cache_kv,
    moe_gain,
    expert_in,
    expert_out,
    routes,
    route_prob,
    page_slot,
):
    halves = lax.axis_size("half")
    half_size = lax.axis_size("hseq")
    seq_count = halves * half_size
    half_index = lax.axis_index("half")
    half_pos = lax.axis_index("hseq")
    seq_index = half_index * half_size + half_pos
    exp_index = lax.axis_index("exp")
    tokens_here = hidden_in.shape[0]
    head_dim = HEAD_DIM
    kv_local = k_weight.shape[1] // head_dim
    group_size = HEADS // KV_HEADS
    holds_first = half_index == 0
    normed = rms_norm(hidden_in, attn_gain)
    queries = jnp.dot(normed, q_weight, preferred_element_type=jnp.float32).astype(jnp.bfloat16)
    keys_new = jnp.dot(normed, k_weight, preferred_element_type=jnp.float32).astype(jnp.bfloat16)
    values_new = jnp.dot(normed, v_weight, preferred_element_type=jnp.float32).astype(jnp.bfloat16)
    pair_width = 2 * kv_local * head_dim
    split_new = jnp.stack(
        [
            keys_new.reshape(tokens_here, kv_local, head_dim),
            values_new.reshape(tokens_here, kv_local, head_dim),
        ],
        axis=2,
    )
    pairs_new = split_new.reshape(tokens_here, pair_width)
    blocks_here = tokens_here // PAGE
    rounds = blocks_here // seq_count
    outgoing = pairs_new.reshape(rounds, seq_count, PAGE * pair_width)
    received = lax.all_to_all(outgoing, SEQ_AXES, split_axis=1, concat_axis=1, tiled=True)
    block_ids = (
        jnp.arange(seq_count, dtype=jnp.int32)[None, :] * blocks_here
        + jnp.arange(rounds, dtype=jnp.int32)[:, None] * seq_count
        + seq_index
    ).reshape(-1)
    table_ids = jnp.arange(page_slot.shape[0], dtype=jnp.int32)
    page_slots = jnp.sum(
        jnp.where(block_ids[:, None] == table_ids[None, :], page_slot[None, :], 0), axis=1
    )
    local_pages = (
        jnp.zeros((blocks_here, PAGE * pair_width), jnp.bfloat16)
        .at[page_slots]
        .set(received.reshape(blocks_here, -1))
    )
    page_rows = local_pages.reshape(blocks_here, PAGE, kv_local, 2, head_dim).transpose(
        0, 2, 3, 1, 4
    )
    page_rows = page_rows.reshape(blocks_here, kv_local, 2, PAGE * head_dim)
    kv_own = split_new.transpose(2, 1, 0, 3)
    cache_rows = cache_kv.shape[0]
    cache_own = cache_kv.reshape(cache_rows, kv_local, 2, head_dim).transpose(2, 1, 0, 3)
    kv_all = gather_by_all_to_all(jnp.concatenate([cache_own, kv_own], axis=2), "hseq", 2)
    key_block = math.gcd(math.gcd(cache_rows, tokens_here), 256)
    cache_per = cache_rows // key_block
    new_per = tokens_here // key_block
    query_rows = queries.reshape(tokens_here, kv_local, group_size, head_dim)
    query_rows = query_rows.transpose(1, 2, 0, 3).reshape(kv_local, group_size * tokens_here, head_dim)
    partner_rows = lax.ppermute(query_rows, "half", perm=[(0, 1)])
    flags = jnp.reshape(half_pos * tokens_here, (1,)).astype(jnp.int32)
    shapes = dict(cache_per=cache_per, new_per=new_per, key_block=key_block, group_rows=tokens_here)

    def empty_partial(rows_in):
        heads, rows, _ = rows_in.shape
        return (
            jnp.zeros((heads, rows, head_dim), jnp.float32),
            jnp.full((heads, rows, 1), masked_score, jnp.float32),
            jnp.zeros((heads, rows, 1), jnp.float32),
        )

    far_part = lax.cond(
        holds_first,
        empty_partial,
        lambda rows_in: attend_partial(flags, rows_in, kv_all, "cache", **shapes),
        partner_rows,
    )
    own_part = lax.cond(
        holds_first,
        lambda rows_in: attend_partial(flags, rows_in, kv_all, "all", **shapes),
        lambda rows_in: attend_partial(flags, rows_in, kv_all, "new", **shapes),
        query_rows,
    )
    back_acc, back_best, back_total = lax.ppermute(far_part, "half", perm=[(1, 0)])
    back_best = jnp.where(holds_first, back_best, masked_score)
    back_total = jnp.where(holds_first, back_total, 0.0)
    back_acc = jnp.where(holds_first, back_acc, 0.0)
    own_acc, own_best, own_total = own_part
    best = jnp.maximum(own_best, back_best)
    own_scale = jnp.exp(own_best - best)
    back_scale = jnp.exp(back_best - best)
    attended = (own_acc * own_scale + back_acc * back_scale) / (
        own_total * own_scale + back_total * back_scale
    )
    attended = attended.astype(jnp.bfloat16).reshape(kv_local, group_size, tokens_here, head_dim)
    attended = attended.transpose(2, 0, 1, 3).reshape(tokens_here, -1)
    exp_count = lax.axis_size("exp")
    projected = jnp.dot(attended, o_weight, preferred_element_type=jnp.float32).astype(jnp.bfloat16)
    pieces = lax.all_to_all(
        projected.reshape(exp_count, -1, projected.shape[1]), "exp", split_axis=0, concat_axis=0, tiled=True
    )
    mixed_rows = jnp.sum(pieces.astype(jnp.float32), axis=0)
    moe_rows = mixed_rows.shape[0]
    residual = (
        lax.dynamic_slice_in_dim(hidden_in, exp_index * moe_rows, moe_rows, 0).astype(jnp.float32)
        + residual_scale * mixed_rows
    )
    moe_in = rms_norm(residual, moe_gain)
    top_count = routes.shape[1]
    experts_here = expert_in.shape[0]
    capacity = 2 * moe_rows * top_count // EXPERTS
    share = route_prob / jnp.sum(route_prob, axis=-1, keepdims=True)
    expert_ids = jnp.arange(EXPERTS, dtype=jnp.int32)
    route_hits = routes[:, :, None] == expert_ids[None, None, :]
    full_weight = jnp.sum(jnp.where(route_hits, share[:, :, None], 0.0), axis=1)
    full_hi = full_weight.astype(jnp.bfloat16)
    full_lo = (full_weight - full_hi.astype(jnp.float32)).astype(jnp.bfloat16)
    full_named = jnp.any(route_hits, axis=1).astype(jnp.bfloat16)
    model_width = moe_in.shape[1]
    side_width = 128 * pl_cdiv(3 * EXPERTS, 128)
    side = jnp.concatenate(
        [
            full_named,
            full_hi,
            full_lo,
            jnp.zeros((moe_rows, side_width - 3 * EXPERTS), jnp.bfloat16),
        ],
        axis=1,
    )
    packed_all = gather_by_all_to_all(jnp.concatenate([moe_in, side], axis=1), SEQ_AXES, 0)
    rows_all = packed_all[:, :model_width]
    total_rows = rows_all.shape[0]
    local_first = seq_index * experts_here
    side_all = packed_all[:, model_width:]
    named = (
        lax.dynamic_slice_in_dim(side_all, local_first, experts_here, 1) > 0
    )
    weight_hi = lax.dynamic_slice_in_dim(side_all, EXPERTS + local_first, experts_here, 1)
    weight_lo = lax.dynamic_slice_in_dim(side_all, 2 * EXPERTS + local_first, experts_here, 1)
    named_blocks = named.reshape(seq_count, moe_rows, experts_here).astype(jnp.int32)
    rank = jnp.cumsum(named_blocks, axis=1) - named_blocks
    slot = (jnp.arange(seq_count, dtype=jnp.int32)[:, None, None] * capacity + rank).reshape(
        total_rows, experts_here
    )
    slots_total = seq_count * capacity
    picks = named[:, :, None] & (
        slot[:, :, None] == jnp.arange(slots_total, dtype=jnp.int32)[None, None, :]
    )
    onehot = picks.astype(jnp.bfloat16)
    rows_in = jnp.einsum(
        "nec,nd->ecd", onehot, rows_all, preferred_element_type=jnp.float32
    ).astype(jnp.bfloat16)
    hidden = jnp.einsum("ecd,edf->ecf", rows_in, expert_in, preferred_element_type=jnp.float32)
    half_width = hidden.shape[-1] // 2
    active = (jax.nn.silu(hidden[..., :half_width]) * hidden[..., half_width:]).astype(jnp.bfloat16)
    produced = jnp.einsum(
        "ecf,efd->ecd", active, expert_out, preferred_element_type=jnp.float32
    ).astype(jnp.bfloat16)
    scaled_hi = jnp.where(picks, weight_hi[:, :, None], jnp.zeros_like(onehot))
    scaled_lo = jnp.where(picks, weight_lo[:, :, None], jnp.zeros_like(onehot))
    partial = jnp.einsum(
        "nec,ecd->nd", scaled_hi, produced, preferred_element_type=jnp.float32
    ) + jnp.einsum("nec,ecd->nd", scaled_lo, produced, preferred_element_type=jnp.float32)
    returned = lax.all_to_all(
        partial.astype(jnp.bfloat16).reshape(seq_count, moe_rows, -1),
        SEQ_AXES,
        split_axis=0,
        concat_axis=0,
        tiled=True,
    )
    moe = jnp.sum(returned.astype(jnp.float32), axis=0)
    hidden_out = (residual + residual_scale * moe).astype(jnp.bfloat16)
    return (hidden_out, page_rows)


def solution(mesh):
    seq_count, exp_count = mesh.devices.shape
    split_mesh = Mesh(
        mesh.devices.reshape(2, seq_count // 2, exp_count), ("half", "hseq", "exp")
    )
    return jax.shard_map(
        body,
        mesh=split_mesh,
        in_specs=(
            P(SEQ_AXES, None),
            P(),
            P(None, "exp"),
            P(None, "exp"),
            P(None, "exp"),
            P("exp", None),
            P(SEQ_AXES, "exp"),
            P(),
            P(SEQ_AXES, None, None),
            P(SEQ_AXES, None, None),
            P(("half", "hseq", "exp"), None),
            P(("half", "hseq", "exp"), None),
            P(),
        ),
        out_specs=(P(("half", "hseq", "exp"), None), P(SEQ_AXES, "exp", None, None)),
        check_vma=False,
    )
```

```python
import functools
import math

import jax
import jax.numpy as jnp
from jax import lax
from jax.experimental import pallas as pl
from jax.experimental.pallas import tpu as pltpu
from jax.sharding import Mesh, PartitionSpec as P

HEADS = 24
KV_HEADS = 8
HEAD_DIM = 64
EXPERTS = 32
PAGE = 8
SEQ_AXES = ("half", "hseq")


norm_epsilon = 1e-06
attention_scale = 0.015625
residual_scale = 0.22
masked_score = -1e30


def rms_norm(values, gain_row):
    widened = values.astype(jnp.float32)
    spread = lax.rsqrt(jnp.mean(widened * widened, axis=-1, keepdims=True) + norm_epsilon)
    return (widened * spread * gain_row).astype(jnp.bfloat16)


def partial_kernel(
    flags_ref, q_ref, k_ref, v_ref, acc_ref, m_ref, l_ref, m_sc, l_sc, acc_sc, *, mode, cache_rows,
    group_rows
):
    step = pl.program_id(1)
    last = pl.num_programs(1) - 1
    query_first = flags_ref[0]
    chunk = k_ref.shape[1]
    new_rows = chunk - cache_rows
    new_first = step * new_rows

    @pl.when(step == 0)
    def _():
        m_sc[...] = jnp.full(m_sc.shape, masked_score, jnp.float32)
        l_sc[...] = jnp.zeros(l_sc.shape, jnp.float32)
        acc_sc[...] = jnp.zeros(acc_sc.shape, jnp.float32)

    def update(first, count, causal):
        q = q_ref[0]
        k = k_ref[0, pl.ds(first, count), :]
        v = v_ref[0, pl.ds(first, count), :]
        scores = lax.dot_general(
            q, k, (((1,), (1,)), ((), ())), preferred_element_type=jnp.float32
        ) * attention_scale
        if causal:
            rows = q.shape[0]
            query_pos = query_first + lax.broadcasted_iota(jnp.int32, (rows, count), 0) % group_rows
            column = lax.broadcasted_iota(jnp.int32, (rows, count), 1) + first
            visible = (column < cache_rows) | (new_first + column - cache_rows <= query_pos)
            scores = jnp.where(visible, scores, masked_score)
        m_prev = m_sc[...]
        m_new = jnp.maximum(m_prev, jnp.max(scores, axis=1, keepdims=True))
        weights = jnp.exp(scores - m_new)
        if causal:
            weights = jnp.where(visible, weights, 0.0)
        factor = jnp.exp(m_prev - m_new)
        l_sc[...] = l_sc[...] * factor + jnp.sum(weights, axis=1, keepdims=True)
        acc_sc[...] = acc_sc[...] * factor + jnp.dot(
            weights.astype(jnp.bfloat16), v, preferred_element_type=jnp.float32
        )
        m_sc[...] = m_new

    if mode == "all":
        update(0, chunk, True)
    elif mode == "cache":
        update(0, cache_rows, False)
    else:

        @pl.when(new_first <= query_first + group_rows - 1)
        def _():
            update(cache_rows, new_rows, True)

    @pl.when(step == last)
    def _():
        acc_ref[0] = acc_sc[...]
        m_ref[0] = m_sc[...]
        l_ref[0] = l_sc[...]


def attend_partial(flags, q, kv_all, mode, cache_rows, group_rows):
    heads, rows, dim = q.shape
    devices, _, _, chunk, _ = kv_all.shape
    kernel = functools.partial(partial_kernel, mode=mode, cache_rows=cache_rows, group_rows=group_rows)
    kv_block = (None, None, 1, chunk, dim)
    row_block = pl.BlockSpec((1, rows, 1), lambda h, s, f: (h, 0, 0))
    return pl.pallas_call(
        kernel,
        out_shape=(
            jax.ShapeDtypeStruct((heads, rows, dim), jnp.float32),
            jax.ShapeDtypeStruct((heads, rows, 1), jnp.float32),
            jax.ShapeDtypeStruct((heads, rows, 1), jnp.float32),
        ),
        grid_spec=pltpu.PrefetchScalarGridSpec(
            num_scalar_prefetch=1,
            grid=(heads, devices),
            in_specs=[
                pl.BlockSpec((1, rows, dim), lambda h, s, f: (h, 0, 0)),
                pl.BlockSpec(kv_block, lambda h, s, f: (s, 0, h, 0, 0)),
                pl.BlockSpec(kv_block, lambda h, s, f: (s, 1, h, 0, 0)),
            ],
            out_specs=[pl.BlockSpec((1, rows, dim), lambda h, s, f: (h, 0, 0)), row_block, row_block],
            scratch_shapes=[
                pltpu.VMEM((rows, 1), jnp.float32),
                pltpu.VMEM((rows, 1), jnp.float32),
                pltpu.VMEM((rows, dim), jnp.float32),
            ],
        ),
        compiler_params=pltpu.CompilerParams(dimension_semantics=("arbitrary", "arbitrary")),
    )(flags, q, kv_all, kv_all)


def pl_cdiv(a, b):
    return -(-a // b)


def block_size(piece_rows):
    return math.gcd(piece_rows, 512)


def body(
    hidden_in,
    attn_gain,
    q_weight,
    k_weight,
    v_weight,
    o_weight,
    cache_kv,
    moe_gain,
    expert_in,
    expert_out,
    routes,
    route_prob,
    page_slot,
):
    halves = lax.axis_size("half")
    half_size = lax.axis_size("hseq")
    seq_count = halves * half_size
    half_index = lax.axis_index("half")
    half_pos = lax.axis_index("hseq")
    seq_index = half_index * half_size + half_pos
    exp_index = lax.axis_index("exp")
    tokens_here = hidden_in.shape[0]
    head_dim = HEAD_DIM
    kv_local = k_weight.shape[1] // head_dim
    group_size = HEADS // KV_HEADS
    holds_first = half_index == 0
    normed = rms_norm(hidden_in, attn_gain)
    queries = jnp.dot(normed, q_weight, preferred_element_type=jnp.float32).astype(jnp.bfloat16)
    keys_new = jnp.dot(normed, k_weight, preferred_element_type=jnp.float32).astype(jnp.bfloat16)
    values_new = jnp.dot(normed, v_weight, preferred_element_type=jnp.float32).astype(jnp.bfloat16)
    pair_width = 2 * kv_local * head_dim
    split_new = jnp.stack(
        [
            keys_new.reshape(tokens_here, kv_local, head_dim),
            values_new.reshape(tokens_here, kv_local, head_dim),
        ],
        axis=2,
    )
    pairs_new = split_new.reshape(tokens_here, pair_width)
    blocks_here = tokens_here // PAGE
    rounds = blocks_here // seq_count
    outgoing = pairs_new.reshape(rounds, seq_count, PAGE * pair_width)
    received = lax.all_to_all(outgoing, SEQ_AXES, split_axis=1, concat_axis=1, tiled=True)
    block_ids = (
        jnp.arange(seq_count, dtype=jnp.int32)[None, :] * blocks_here
        + jnp.arange(rounds, dtype=jnp.int32)[:, None] * seq_count
        + seq_index
    ).reshape(-1)
    table_ids = jnp.arange(page_slot.shape[0], dtype=jnp.int32)
    page_slots = jnp.sum(
        jnp.where(block_ids[:, None] == table_ids[None, :], page_slot[None, :], 0), axis=1
    )
    local_pages = (
        jnp.zeros((blocks_here, PAGE * pair_width), jnp.bfloat16)
        .at[page_slots]
        .set(received.reshape(blocks_here, -1))
    )
    page_rows = local_pages.reshape(blocks_here, PAGE, kv_local, 2, head_dim).transpose(
        0, 2, 3, 1, 4
    )
    page_rows = page_rows.reshape(blocks_here, kv_local, 2, PAGE * head_dim)
    kv_own = split_new.transpose(2, 1, 0, 3)
    cache_rows = cache_kv.shape[0]
    cache_own = cache_kv.reshape(cache_rows, kv_local, 2, head_dim).transpose(2, 1, 0, 3)
    kv_piece = jnp.concatenate([cache_own, kv_own], axis=2)
    kv_all = lax.all_to_all(
        jnp.broadcast_to(kv_piece[None], (half_size,) + kv_piece.shape),
        "hseq",
        split_axis=0,
        concat_axis=0,
        tiled=True,
    )
    query_rows = queries.reshape(tokens_here, kv_local, group_size, head_dim)
    query_rows = query_rows.transpose(1, 2, 0, 3).reshape(kv_local, group_size * tokens_here, head_dim)
    partner_rows = lax.ppermute(query_rows, "half", perm=[(0, 1)])
    flags = jnp.reshape(half_pos * tokens_here, (1,)).astype(jnp.int32)
    shapes = dict(cache_rows=cache_rows, group_rows=tokens_here)

    def empty_partial(rows_in):
        heads, rows, _ = rows_in.shape
        return (
            jnp.zeros((heads, rows, head_dim), jnp.float32),
            jnp.full((heads, rows, 1), masked_score, jnp.float32),
            jnp.zeros((heads, rows, 1), jnp.float32),
        )

    far_part = lax.cond(
        holds_first,
        empty_partial,
        lambda rows_in: attend_partial(flags, rows_in, kv_all, "cache", **shapes),
        partner_rows,
    )
    own_part = lax.cond(
        holds_first,
        lambda rows_in: attend_partial(flags, rows_in, kv_all, "all", **shapes),
        lambda rows_in: attend_partial(flags, rows_in, kv_all, "new", **shapes),
        query_rows,
    )
    back_acc, back_best, back_total = lax.ppermute(far_part, "half", perm=[(1, 0)])
    back_best = jnp.where(holds_first, back_best, masked_score)
    back_total = jnp.where(holds_first, back_total, 0.0)
    back_acc = jnp.where(holds_first, back_acc, 0.0)
    own_acc, own_best, own_total = own_part
    best = jnp.maximum(own_best, back_best)
    own_scale = jnp.exp(own_best - best)
    back_scale = jnp.exp(back_best - best)
    attended = (own_acc * own_scale + back_acc * back_scale) / (
        own_total * own_scale + back_total * back_scale
    )
    attended = attended.astype(jnp.bfloat16).reshape(kv_local, group_size, tokens_here, head_dim)
    attended = attended.transpose(2, 0, 1, 3).reshape(tokens_here, -1)
    exp_count = lax.axis_size("exp")
    projected = jnp.dot(attended, o_weight, preferred_element_type=jnp.float32).astype(jnp.bfloat16)
    pieces = lax.all_to_all(
        projected.reshape(exp_count, -1, projected.shape[1]), "exp", split_axis=0, concat_axis=0, tiled=True
    )
    mixed_rows = jnp.sum(pieces.astype(jnp.float32), axis=0)
    moe_rows = mixed_rows.shape[0]
    residual = (
        lax.dynamic_slice_in_dim(hidden_in, exp_index * moe_rows, moe_rows, 0).astype(jnp.float32)
        + residual_scale * mixed_rows
    )
    moe_in = rms_norm(residual, moe_gain)
    top_count = routes.shape[1]
    experts_here = expert_in.shape[0]
    capacity = 2 * moe_rows * top_count // EXPERTS
    share = route_prob / jnp.sum(route_prob, axis=-1, keepdims=True)
    expert_ids = jnp.arange(EXPERTS, dtype=jnp.int32)
    route_hits = routes[:, :, None] == expert_ids[None, None, :]
    full_weight = jnp.sum(jnp.where(route_hits, share[:, :, None], 0.0), axis=1)
    full_hi = full_weight.astype(jnp.bfloat16)
    full_lo = (full_weight - full_hi.astype(jnp.float32)).astype(jnp.bfloat16)
    full_named = jnp.any(route_hits, axis=1).astype(jnp.bfloat16)
    model_width = moe_in.shape[1]
    side_width = 128 * pl_cdiv(3 * EXPERTS, 128)
    side = jnp.concatenate(
        [
            full_named,
            full_hi,
            full_lo,
            jnp.zeros((moe_rows, side_width - 3 * EXPERTS), jnp.bfloat16),
        ],
        axis=1,
    )
    packed_all = lax.all_gather(
        jnp.concatenate([moe_in, side], axis=1), SEQ_AXES, axis=0, tiled=True
    )
    rows_all = packed_all[:, :model_width]
    total_rows = rows_all.shape[0]
    local_first = seq_index * experts_here
    side_all = packed_all[:, model_width:]
    named = (
        lax.dynamic_slice_in_dim(side_all, local_first, experts_here, 1) > 0
    )
    weight_hi = lax.dynamic_slice_in_dim(side_all, EXPERTS + local_first, experts_here, 1)
    weight_lo = lax.dynamic_slice_in_dim(side_all, 2 * EXPERTS + local_first, experts_here, 1)
    named_blocks = named.reshape(seq_count, moe_rows, experts_here).astype(jnp.int32)
    rank = jnp.cumsum(named_blocks, axis=1) - named_blocks
    slot = (jnp.arange(seq_count, dtype=jnp.int32)[:, None, None] * capacity + rank).reshape(
        total_rows, experts_here
    )
    slots_total = seq_count * capacity
    picks = named[:, :, None] & (
        slot[:, :, None] == jnp.arange(slots_total, dtype=jnp.int32)[None, None, :]
    )
    onehot = picks.astype(jnp.bfloat16)
    rows_in = jnp.einsum(
        "nec,nd->ecd", onehot, rows_all, preferred_element_type=jnp.float32
    ).astype(jnp.bfloat16)
    hidden = jnp.einsum("ecd,edf->ecf", rows_in, expert_in, preferred_element_type=jnp.float32)
    half_width = hidden.shape[-1] // 2
    active = (jax.nn.silu(hidden[..., :half_width]) * hidden[..., half_width:]).astype(jnp.bfloat16)
    produced = jnp.einsum(
        "ecf,efd->ecd", active, expert_out, preferred_element_type=jnp.float32
    ).astype(jnp.bfloat16)
    scaled_hi = jnp.where(picks, weight_hi[:, :, None], jnp.zeros_like(onehot))
    scaled_lo = jnp.where(picks, weight_lo[:, :, None], jnp.zeros_like(onehot))
    partial = jnp.einsum(
        "nec,ecd->nd", scaled_hi, produced, preferred_element_type=jnp.float32
    ) + jnp.einsum("nec,ecd->nd", scaled_lo, produced, preferred_element_type=jnp.float32)
    returned = lax.all_to_all(
        partial.astype(jnp.bfloat16).reshape(seq_count, moe_rows, -1),
        SEQ_AXES,
        split_axis=0,
        concat_axis=0,
        tiled=True,
    )
    moe = jnp.sum(returned.astype(jnp.float32), axis=0)
    hidden_out = (residual + residual_scale * moe).astype(jnp.bfloat16)
    return (hidden_out, page_rows)


def solution(mesh):
    seq_count, exp_count = mesh.devices.shape
    split_mesh = Mesh(
        mesh.devices.reshape(2, seq_count // 2, exp_count), ("half", "hseq", "exp")
    )
    return jax.shard_map(
        body,
        mesh=split_mesh,
        in_specs=(
            P(SEQ_AXES, None),
            P(),
            P(None, "exp"),
            P(None, "exp"),
            P(None, "exp"),
            P("exp", None),
            P(SEQ_AXES, "exp"),
            P(),
            P(SEQ_AXES, None, None),
            P(SEQ_AXES, None, None),
            P(("half", "hseq", "exp"), None),
            P(("half", "hseq", "exp"), None),
            P(),
        ),
        out_specs=(P(("half", "hseq", "exp"), None), P(SEQ_AXES, "exp", None, None)),
        check_vma=False,
    )
```

```python
import functools
import math

import jax
import jax.numpy as jnp
from jax import lax
from jax.experimental import pallas as pl
from jax.experimental.pallas import tpu as pltpu
from jax.sharding import Mesh, PartitionSpec as P

HEADS = 24
KV_HEADS = 8
HEAD_DIM = 64
EXPERTS = 32
PAGE = 8
SEQ_AXES = ("half", "hseq")


norm_epsilon = 1e-06
attention_scale = 0.015625
residual_scale = 0.22
masked_score = -1e30


def rms_norm(values, gain_row):
    widened = values.astype(jnp.float32)
    spread = lax.rsqrt(jnp.mean(widened * widened, axis=-1, keepdims=True) + norm_epsilon)
    return (widened * spread * gain_row).astype(jnp.bfloat16)


def partial_kernel(
    flags_ref, q_ref, k_ref, v_ref, acc_ref, m_ref, l_ref, m_sc, l_sc, acc_sc, *, mode, cache_rows,
    group_rows
):
    step = pl.program_id(1)
    last = pl.num_programs(1) - 1
    query_first = flags_ref[0]
    chunk = k_ref.shape[1]
    new_rows = chunk - cache_rows
    new_first = step * new_rows

    @pl.when(step == 0)
    def _():
        m_sc[...] = jnp.full(m_sc.shape, masked_score, jnp.float32)
        l_sc[...] = jnp.zeros(l_sc.shape, jnp.float32)
        acc_sc[...] = jnp.zeros(acc_sc.shape, jnp.float32)

    def update(first, count, causal):
        q = q_ref[0]
        k = k_ref[0, pl.ds(first, count), :]
        v = v_ref[0, pl.ds(first, count), :]
        scores = lax.dot_general(
            q, k, (((1,), (1,)), ((), ())), preferred_element_type=jnp.float32
        ) * attention_scale
        if causal:
            rows = q.shape[0]
            query_pos = query_first + lax.broadcasted_iota(jnp.int32, (rows, count), 0) % group_rows
            column = lax.broadcasted_iota(jnp.int32, (rows, count), 1) + first
            visible = (column < cache_rows) | (new_first + column - cache_rows <= query_pos)
            scores = jnp.where(visible, scores, masked_score)
        m_prev = m_sc[...]
        m_new = jnp.maximum(m_prev, jnp.max(scores, axis=1, keepdims=True))
        weights = jnp.exp(scores - m_new)
        if causal:
            weights = jnp.where(visible, weights, 0.0)
        factor = jnp.exp(m_prev - m_new)
        l_sc[...] = l_sc[...] * factor + jnp.sum(weights, axis=1, keepdims=True)
        acc_sc[...] = acc_sc[...] * factor + jnp.dot(
            weights.astype(jnp.bfloat16), v, preferred_element_type=jnp.float32
        )
        m_sc[...] = m_new

    if mode == "all":
        update(0, chunk, True)
    elif mode == "cache":
        update(0, cache_rows, False)
    else:

        @pl.when(new_first <= query_first + group_rows - 1)
        def _():
            update(cache_rows, new_rows, True)

    @pl.when(step == last)
    def _():
        acc_ref[0] = acc_sc[...]
        m_ref[0] = m_sc[...]
        l_ref[0] = l_sc[...]


def attend_partial(flags, q, kv_all, mode, cache_rows, group_rows):
    heads, rows, dim = q.shape
    devices, _, _, chunk, _ = kv_all.shape
    kernel = functools.partial(partial_kernel, mode=mode, cache_rows=cache_rows, group_rows=group_rows)
    kv_block = (None, None, 1, chunk, dim)
    row_block = pl.BlockSpec((1, rows, 1), lambda h, s, f: (h, 0, 0))
    return pl.pallas_call(
        kernel,
        out_shape=(
            jax.ShapeDtypeStruct((heads, rows, dim), jnp.float32),
            jax.ShapeDtypeStruct((heads, rows, 1), jnp.float32),
            jax.ShapeDtypeStruct((heads, rows, 1), jnp.float32),
        ),
        grid_spec=pltpu.PrefetchScalarGridSpec(
            num_scalar_prefetch=1,
            grid=(heads, devices),
            in_specs=[
                pl.BlockSpec((1, rows, dim), lambda h, s, f: (h, 0, 0)),
                pl.BlockSpec(kv_block, lambda h, s, f: (s, 0, h, 0, 0)),
                pl.BlockSpec(kv_block, lambda h, s, f: (s, 1, h, 0, 0)),
            ],
            out_specs=[pl.BlockSpec((1, rows, dim), lambda h, s, f: (h, 0, 0)), row_block, row_block],
            scratch_shapes=[
                pltpu.VMEM((rows, 1), jnp.float32),
                pltpu.VMEM((rows, 1), jnp.float32),
                pltpu.VMEM((rows, dim), jnp.float32),
            ],
        ),
        compiler_params=pltpu.CompilerParams(dimension_semantics=("arbitrary", "arbitrary")),
    )(flags, q, kv_all, kv_all)


def pl_cdiv(a, b):
    return -(-a // b)


def block_size(piece_rows):
    return math.gcd(piece_rows, 512)


def body(
    hidden_in,
    attn_gain,
    q_weight,
    k_weight,
    v_weight,
    o_weight,
    cache_kv,
    moe_gain,
    expert_in,
    expert_out,
    routes,
    route_prob,
    page_slot,
):
    halves = lax.axis_size("half")
    half_size = lax.axis_size("hseq")
    seq_count = halves * half_size
    half_index = lax.axis_index("half")
    half_pos = lax.axis_index("hseq")
    seq_index = half_index * half_size + half_pos
    exp_index = lax.axis_index("exp")
    tokens_here = hidden_in.shape[0]
    head_dim = HEAD_DIM
    kv_local = k_weight.shape[1] // head_dim
    group_size = HEADS // KV_HEADS
    holds_first = half_index == 0
    normed = rms_norm(hidden_in, attn_gain)
    queries = jnp.dot(normed, q_weight, preferred_element_type=jnp.float32).astype(jnp.bfloat16)
    keys_new = jnp.dot(normed, k_weight, preferred_element_type=jnp.float32).astype(jnp.bfloat16)
    values_new = jnp.dot(normed, v_weight, preferred_element_type=jnp.float32).astype(jnp.bfloat16)
    pair_width = 2 * kv_local * head_dim
    split_new = jnp.stack(
        [
            keys_new.reshape(tokens_here, kv_local, head_dim),
            values_new.reshape(tokens_here, kv_local, head_dim),
        ],
        axis=2,
    )
    pairs_new = split_new.reshape(tokens_here, pair_width)
    blocks_here = tokens_here // PAGE
    rounds = blocks_here // seq_count
    outgoing = pairs_new.reshape(rounds, seq_count, PAGE * pair_width).transpose(1, 0, 2)
    outgoing = outgoing.reshape(seq_count, -1)
    kv_own = split_new.transpose(2, 1, 0, 3)
    cache_rows = cache_kv.shape[0]
    cache_own = cache_kv.reshape(cache_rows, kv_local, 2, head_dim).transpose(2, 1, 0, 3)
    kv_piece = jnp.concatenate([cache_own, kv_own], axis=2)
    kv_all = lax.all_to_all(
        jnp.broadcast_to(kv_piece[None], (half_size,) + kv_piece.shape),
        "hseq",
        split_axis=0,
        concat_axis=0,
        tiled=True,
    )
    query_rows = queries.reshape(tokens_here, kv_local, group_size, head_dim)
    query_rows = query_rows.transpose(1, 2, 0, 3).reshape(kv_local, group_size * tokens_here, head_dim)
    partner_rows = lax.ppermute(query_rows, "half", perm=[(0, 1)])
    flags = jnp.reshape(half_pos * tokens_here, (1,)).astype(jnp.int32)
    shapes = dict(cache_rows=cache_rows, group_rows=tokens_here)

    def empty_partial(rows_in):
        heads, rows, _ = rows_in.shape
        return (
            jnp.zeros((heads, rows, head_dim), jnp.float32),
            jnp.full((heads, rows, 1), masked_score, jnp.float32),
            jnp.zeros((heads, rows, 1), jnp.float32),
        )

    own_part = lax.cond(
        holds_first,
        lambda rows_in: attend_partial(flags, rows_in, kv_all, "all", **shapes),
        lambda rows_in: attend_partial(flags, rows_in, kv_all, "new", **shapes),
        query_rows,
    )
    partner_rows, own_part = lax.optimization_barrier((partner_rows, own_part))
    far_part = lax.cond(
        holds_first,
        empty_partial,
        lambda rows_in: attend_partial(flags, rows_in, kv_all, "cache", **shapes),
        partner_rows,
    )
    back_acc, back_best, back_total = lax.ppermute(far_part, "half", perm=[(1, 0)])
    back_best = jnp.where(holds_first, back_best, masked_score)
    back_total = jnp.where(holds_first, back_total, 0.0)
    back_acc = jnp.where(holds_first, back_acc, 0.0)
    own_acc, own_best, own_total = own_part
    best = jnp.maximum(own_best, back_best)
    own_scale = jnp.exp(own_best - best)
    back_scale = jnp.exp(back_best - best)
    attended = (own_acc * own_scale + back_acc * back_scale) / (
        own_total * own_scale + back_total * back_scale
    )
    attended = attended.astype(jnp.bfloat16).reshape(kv_local, group_size, tokens_here, head_dim)
    attended = attended.transpose(2, 0, 1, 3).reshape(tokens_here, -1)
    exp_count = lax.axis_size("exp")
    projected = jnp.dot(attended, o_weight, preferred_element_type=jnp.float32).astype(jnp.bfloat16)
    pieces = lax.all_to_all(
        projected.reshape(exp_count, -1, projected.shape[1]), "exp", split_axis=0, concat_axis=0, tiled=True
    )
    mixed_rows = jnp.sum(pieces.astype(jnp.float32), axis=0)
    moe_rows = mixed_rows.shape[0]
    residual = (
        lax.dynamic_slice_in_dim(hidden_in, exp_index * moe_rows, moe_rows, 0).astype(jnp.float32)
        + residual_scale * mixed_rows
    )
    moe_in = rms_norm(residual, moe_gain)
    top_count = routes.shape[1]
    experts_here = expert_in.shape[0]
    capacity = 2 * moe_rows * top_count // EXPERTS
    share = route_prob / jnp.sum(route_prob, axis=-1, keepdims=True)
    expert_ids = jnp.arange(EXPERTS, dtype=jnp.int32)
    route_hits = routes[:, :, None] == expert_ids[None, None, :]
    full_weight = jnp.sum(jnp.where(route_hits, share[:, :, None], 0.0), axis=1)
    full_hi = full_weight.astype(jnp.bfloat16)
    full_lo = (full_weight - full_hi.astype(jnp.float32)).astype(jnp.bfloat16)
    full_named = jnp.any(route_hits, axis=1).astype(jnp.bfloat16)
    moe_width = moe_in.shape[1]
    side_width = 128 * pl_cdiv(3 * EXPERTS, 128)
    side = jnp.concatenate(
        [
            full_named,
            full_hi,
            full_lo,
            jnp.zeros((moe_rows, side_width - 3 * EXPERTS), jnp.bfloat16),
        ],
        axis=1,
    )
    packed_all = lax.all_gather(
        jnp.concatenate([moe_in, side], axis=1), SEQ_AXES, axis=0, tiled=True
    )
    rows_all = packed_all[:, :moe_width]
    total_rows = rows_all.shape[0]
    local_first = seq_index * experts_here
    side_all = packed_all[:, moe_width:]
    named = (
        lax.dynamic_slice_in_dim(side_all, local_first, experts_here, 1) > 0
    )
    weight_hi = lax.dynamic_slice_in_dim(side_all, EXPERTS + local_first, experts_here, 1)
    weight_lo = lax.dynamic_slice_in_dim(side_all, 2 * EXPERTS + local_first, experts_here, 1)
    named_blocks = named.reshape(seq_count, moe_rows, experts_here).astype(jnp.int32)
    rank = jnp.cumsum(named_blocks, axis=1) - named_blocks
    slot = (jnp.arange(seq_count, dtype=jnp.int32)[:, None, None] * capacity + rank).reshape(
        total_rows, experts_here
    )
    slots_total = seq_count * capacity
    picks = named[:, :, None] & (
        slot[:, :, None] == jnp.arange(slots_total, dtype=jnp.int32)[None, None, :]
    )
    onehot = picks.astype(jnp.bfloat16)
    rows_in = jnp.einsum(
        "nec,nd->ecd", onehot, rows_all, preferred_element_type=jnp.float32
    ).astype(jnp.bfloat16)
    hidden = jnp.einsum("ecd,edf->ecf", rows_in, expert_in, preferred_element_type=jnp.float32)
    half_width = hidden.shape[-1] // 2
    active = (jax.nn.silu(hidden[..., :half_width]) * hidden[..., half_width:]).astype(jnp.bfloat16)
    produced = jnp.einsum(
        "ecf,efd->ecd", active, expert_out, preferred_element_type=jnp.float32
    ).astype(jnp.bfloat16)
    scaled_hi = jnp.where(picks, weight_hi[:, :, None], jnp.zeros_like(onehot))
    scaled_lo = jnp.where(picks, weight_lo[:, :, None], jnp.zeros_like(onehot))
    partial = jnp.einsum(
        "nec,ecd->nd", scaled_hi, produced, preferred_element_type=jnp.float32
    ) + jnp.einsum("nec,ecd->nd", scaled_lo, produced, preferred_element_type=jnp.float32)
    model_width = partial.shape[1]
    page_lines = pl_cdiv(outgoing.shape[1], model_width)
    page_part = jnp.pad(outgoing, ((0, 0), (0, page_lines * model_width - outgoing.shape[1])))
    both = jnp.concatenate(
        [
            partial.astype(jnp.bfloat16).reshape(seq_count, moe_rows, model_width),
            page_part.reshape(seq_count, page_lines, model_width),
        ],
        axis=1,
    )
    returned = lax.all_to_all(both, SEQ_AXES, split_axis=0, concat_axis=0, tiled=True)
    moe = jnp.sum(returned[:, :moe_rows].astype(jnp.float32), axis=0)
    received = returned[:, moe_rows:].reshape(seq_count, -1)[:, : outgoing.shape[1]]
    received = received.reshape(seq_count, rounds, -1).transpose(1, 0, 2)
    block_ids = (
        jnp.arange(seq_count, dtype=jnp.int32)[None, :] * blocks_here
        + jnp.arange(rounds, dtype=jnp.int32)[:, None] * seq_count
        + seq_index
    ).reshape(-1)
    table_ids = jnp.arange(page_slot.shape[0], dtype=jnp.int32)
    page_slots = jnp.sum(
        jnp.where(block_ids[:, None] == table_ids[None, :], page_slot[None, :], 0), axis=1
    )
    local_pages = (
        jnp.zeros((blocks_here, PAGE * pair_width), jnp.bfloat16)
        .at[page_slots]
        .set(received.reshape(blocks_here, -1))
    )
    page_rows = local_pages.reshape(blocks_here, PAGE, kv_local, 2, head_dim).transpose(
        0, 2, 3, 1, 4
    )
    page_rows = page_rows.reshape(blocks_here, kv_local, 2, PAGE * head_dim)
    hidden_out = (residual + residual_scale * moe).astype(jnp.bfloat16)
    return (hidden_out, page_rows)


def solution(mesh):
    seq_count, exp_count = mesh.devices.shape
    split_mesh = Mesh(
        mesh.devices.reshape(2, seq_count // 2, exp_count), ("half", "hseq", "exp")
    )
    return jax.shard_map(
        body,
        mesh=split_mesh,
        in_specs=(
            P(SEQ_AXES, None),
            P(),
            P(None, "exp"),
            P(None, "exp"),
            P(None, "exp"),
            P("exp", None),
            P(SEQ_AXES, "exp"),
            P(),
            P(SEQ_AXES, None, None),
            P(SEQ_AXES, None, None),
            P(("half", "hseq", "exp"), None),
            P(("half", "hseq", "exp"), None),
            P(),
        ),
        out_specs=(P(("half", "hseq", "exp"), None), P(SEQ_AXES, "exp", None, None)),
        check_vma=False,
    )
```

```python
import functools
import math

import jax
import jax.numpy as jnp
from jax import lax
from jax.experimental import pallas as pl
from jax.experimental.pallas import tpu as pltpu
from jax.sharding import Mesh, PartitionSpec as P

HEADS = 24
KV_HEADS = 8
HEAD_DIM = 64
EXPERTS = 32
PAGE = 8
SEQ_AXES = ("half", "hseq")


norm_epsilon = 1e-06
attention_scale = 0.015625
residual_scale = 0.22
masked_score = -1e30


def rms_norm(values, gain_row):
    widened = values.astype(jnp.float32)
    spread = lax.rsqrt(jnp.mean(widened * widened, axis=-1, keepdims=True) + norm_epsilon)
    return (widened * spread * gain_row).astype(jnp.bfloat16)


def partial_kernel(
    flags_ref, q_ref, k_ref, v_ref, acc_ref, m_ref, l_ref, m_sc, l_sc, acc_sc, *, mode, cache_rows,
    group_rows
):
    step = pl.program_id(1)
    last = pl.num_programs(1) - 1
    query_first = flags_ref[0]
    chunk = k_ref.shape[1]
    new_rows = chunk - cache_rows
    new_first = step * new_rows

    @pl.when(step == 0)
    def _():
        m_sc[...] = jnp.full(m_sc.shape, masked_score, jnp.float32)
        l_sc[...] = jnp.zeros(l_sc.shape, jnp.float32)
        acc_sc[...] = jnp.zeros(acc_sc.shape, jnp.float32)

    def update(first, count, causal):
        q = q_ref[0]
        k = k_ref[0, pl.ds(first, count), :]
        v = v_ref[0, pl.ds(first, count), :]
        scores = lax.dot_general(
            q, k, (((1,), (1,)), ((), ())), preferred_element_type=jnp.float32
        ) * attention_scale
        if causal:
            rows = q.shape[0]
            query_pos = query_first + lax.broadcasted_iota(jnp.int32, (rows, count), 0) % group_rows
            column = lax.broadcasted_iota(jnp.int32, (rows, count), 1) + first
            visible = (column < cache_rows) | (new_first + column - cache_rows <= query_pos)
            scores = jnp.where(visible, scores, masked_score)
        m_prev = m_sc[...]
        m_new = jnp.maximum(m_prev, jnp.max(scores, axis=1, keepdims=True))
        weights = jnp.exp(scores - m_new)
        if causal:
            weights = jnp.where(visible, weights, 0.0)
        factor = jnp.exp(m_prev - m_new)
        l_sc[...] = l_sc[...] * factor + jnp.sum(weights, axis=1, keepdims=True)
        acc_sc[...] = acc_sc[...] * factor + jnp.dot(
            weights.astype(jnp.bfloat16), v, preferred_element_type=jnp.float32
        )
        m_sc[...] = m_new

    if mode == "all":
        update(0, chunk, True)
    elif mode == "cache":
        update(0, cache_rows, False)
    else:

        @pl.when(new_first <= query_first + group_rows - 1)
        def _():
            update(cache_rows, new_rows, True)

    @pl.when(step == last)
    def _():
        acc_ref[0] = acc_sc[...]
        m_ref[0] = m_sc[...]
        l_ref[0] = l_sc[...]


def attend_partial(flags, q, kv_all, mode, cache_rows, group_rows):
    heads, rows, dim = q.shape
    devices, _, _, chunk, _ = kv_all.shape
    kernel = functools.partial(partial_kernel, mode=mode, cache_rows=cache_rows, group_rows=group_rows)
    kv_block = (None, None, 1, chunk, dim)
    row_block = pl.BlockSpec((1, rows, 1), lambda h, s, f: (h, 0, 0))
    return pl.pallas_call(
        kernel,
        out_shape=(
            jax.ShapeDtypeStruct((heads, rows, dim), jnp.float32),
            jax.ShapeDtypeStruct((heads, rows, 1), jnp.float32),
            jax.ShapeDtypeStruct((heads, rows, 1), jnp.float32),
        ),
        grid_spec=pltpu.PrefetchScalarGridSpec(
            num_scalar_prefetch=1,
            grid=(heads, devices),
            in_specs=[
                pl.BlockSpec((1, rows, dim), lambda h, s, f: (h, 0, 0)),
                pl.BlockSpec(kv_block, lambda h, s, f: (s, 0, h, 0, 0)),
                pl.BlockSpec(kv_block, lambda h, s, f: (s, 1, h, 0, 0)),
            ],
            out_specs=[pl.BlockSpec((1, rows, dim), lambda h, s, f: (h, 0, 0)), row_block, row_block],
            scratch_shapes=[
                pltpu.VMEM((rows, 1), jnp.float32),
                pltpu.VMEM((rows, 1), jnp.float32),
                pltpu.VMEM((rows, dim), jnp.float32),
            ],
        ),
        compiler_params=pltpu.CompilerParams(dimension_semantics=("arbitrary", "arbitrary")),
    )(flags, q, kv_all, kv_all)


def pl_cdiv(a, b):
    return -(-a // b)


def block_size(piece_rows):
    return math.gcd(piece_rows, 512)


def body(
    hidden_in,
    attn_gain,
    q_weight,
    k_weight,
    v_weight,
    o_weight,
    cache_kv,
    moe_gain,
    expert_in,
    expert_out,
    routes,
    route_prob,
    page_slot,
):
    halves = lax.axis_size("half")
    half_size = lax.axis_size("hseq")
    seq_count = halves * half_size
    half_index = lax.axis_index("half")
    half_pos = lax.axis_index("hseq")
    seq_index = half_index * half_size + half_pos
    exp_index = lax.axis_index("exp")
    tokens_here = hidden_in.shape[0]
    head_dim = HEAD_DIM
    kv_local = k_weight.shape[1] // head_dim
    group_size = HEADS // KV_HEADS
    holds_first = half_index == 0
    normed = rms_norm(hidden_in, attn_gain)
    queries = jnp.dot(normed, q_weight, preferred_element_type=jnp.float32).astype(jnp.bfloat16)
    keys_new = jnp.dot(normed, k_weight, preferred_element_type=jnp.float32).astype(jnp.bfloat16)
    values_new = jnp.dot(normed, v_weight, preferred_element_type=jnp.float32).astype(jnp.bfloat16)
    pair_width = 2 * kv_local * head_dim
    split_new = jnp.stack(
        [
            keys_new.reshape(tokens_here, kv_local, head_dim),
            values_new.reshape(tokens_here, kv_local, head_dim),
        ],
        axis=2,
    )
    pairs_new = split_new.reshape(tokens_here, pair_width)
    blocks_here = tokens_here // PAGE
    rounds = blocks_here // seq_count
    outgoing = pairs_new.reshape(rounds, seq_count, PAGE * pair_width).transpose(1, 0, 2)
    outgoing = outgoing.reshape(seq_count, -1)
    kv_own = split_new.transpose(2, 1, 0, 3)
    cache_rows = cache_kv.shape[0]
    cache_own = cache_kv.reshape(cache_rows, kv_local, 2, head_dim).transpose(2, 1, 0, 3)
    kv_piece = jnp.concatenate([cache_own, kv_own], axis=2)
    kv_all = lax.all_to_all(
        jnp.broadcast_to(kv_piece[None], (half_size,) + kv_piece.shape),
        "hseq",
        split_axis=0,
        concat_axis=0,
        tiled=True,
    )
    query_rows = queries.reshape(tokens_here, kv_local, group_size, head_dim)
    query_rows = query_rows.transpose(1, 2, 0, 3).reshape(kv_local, group_size * tokens_here, head_dim)
    partner_rows = lax.ppermute(query_rows, "half", perm=[(0, 1)])
    flags = jnp.reshape(half_pos * tokens_here, (1,)).astype(jnp.int32)
    shapes = dict(cache_rows=cache_rows, group_rows=tokens_here)

    def empty_partial(rows_in):
        heads, rows, _ = rows_in.shape
        return (
            jnp.zeros((heads, rows, head_dim), jnp.float32),
            jnp.full((heads, rows, 1), masked_score, jnp.float32),
            jnp.zeros((heads, rows, 1), jnp.float32),
        )

    far_part = lax.cond(
        holds_first,
        empty_partial,
        lambda rows_in: attend_partial(flags, rows_in, kv_all, "cache", **shapes),
        partner_rows,
    )
    own_part = lax.cond(
        holds_first,
        lambda rows_in: attend_partial(flags, rows_in, kv_all, "all", **shapes),
        lambda rows_in: attend_partial(flags, rows_in, kv_all, "new", **shapes),
        query_rows,
    )
    back_acc, back_best, back_total = lax.ppermute(far_part, "half", perm=[(1, 0)])
    back_best = jnp.where(holds_first, back_best, masked_score)
    back_total = jnp.where(holds_first, back_total, 0.0)
    back_acc = jnp.where(holds_first, back_acc, 0.0)
    own_acc, own_best, own_total = own_part
    best = jnp.maximum(own_best, back_best)
    own_scale = jnp.exp(own_best - best)
    back_scale = jnp.exp(back_best - best)
    attended = (own_acc * own_scale + back_acc * back_scale) / (
        own_total * own_scale + back_total * back_scale
    )
    attended = attended.astype(jnp.bfloat16).reshape(kv_local, group_size, tokens_here, head_dim)
    attended = attended.transpose(2, 0, 1, 3).reshape(tokens_here, -1)
    exp_count = lax.axis_size("exp")
    projected = jnp.dot(attended, o_weight, preferred_element_type=jnp.float32).astype(jnp.bfloat16)
    pieces = lax.all_to_all(
        projected.reshape(exp_count, -1, projected.shape[1]), "exp", split_axis=0, concat_axis=0, tiled=True
    )
    mixed_rows = jnp.sum(pieces.astype(jnp.float32), axis=0)
    moe_rows = mixed_rows.shape[0]
    residual = (
        lax.dynamic_slice_in_dim(hidden_in, exp_index * moe_rows, moe_rows, 0).astype(jnp.float32)
        + residual_scale * mixed_rows
    )
    moe_in = rms_norm(residual, moe_gain)
    top_count = routes.shape[1]
    experts_here = expert_in.shape[0]
    capacity = 2 * moe_rows * top_count // EXPERTS
    share = route_prob / jnp.sum(route_prob, axis=-1, keepdims=True)
    expert_ids = jnp.arange(EXPERTS, dtype=jnp.int32)
    route_hits = routes[:, :, None] == expert_ids[None, None, :]
    full_weight = jnp.sum(jnp.where(route_hits, share[:, :, None], 0.0), axis=1)
    full_hi = full_weight.astype(jnp.bfloat16)
    full_lo = (full_weight - full_hi.astype(jnp.float32)).astype(jnp.bfloat16)
    full_named = jnp.any(route_hits, axis=1).astype(jnp.bfloat16)
    moe_width = moe_in.shape[1]
    side_width = 128 * pl_cdiv(3 * EXPERTS, 128)
    side = jnp.concatenate(
        [
            full_named,
            full_hi,
            full_lo,
            jnp.zeros((moe_rows, side_width - 3 * EXPERTS), jnp.bfloat16),
        ],
        axis=1,
    )
    packed_all = lax.all_gather(
        jnp.concatenate([moe_in, side], axis=1), SEQ_AXES, axis=0, tiled=True
    )
    rows_all = packed_all[:, :moe_width]
    total_rows = rows_all.shape[0]
    local_first = seq_index * experts_here
    side_all = packed_all[:, moe_width:]
    named = (
        lax.dynamic_slice_in_dim(side_all, local_first, experts_here, 1) > 0
    )
    weight_hi = lax.dynamic_slice_in_dim(side_all, EXPERTS + local_first, experts_here, 1)
    weight_lo = lax.dynamic_slice_in_dim(side_all, 2 * EXPERTS + local_first, experts_here, 1)
    named_blocks = named.reshape(seq_count, moe_rows, experts_here).astype(jnp.int32)
    rank = jnp.cumsum(named_blocks, axis=1) - named_blocks
    slot = (jnp.arange(seq_count, dtype=jnp.int32)[:, None, None] * capacity + rank).reshape(
        total_rows, experts_here
    )
    slots_total = seq_count * capacity
    picks = named[:, :, None] & (
        slot[:, :, None] == jnp.arange(slots_total, dtype=jnp.int32)[None, None, :]
    )
    onehot = picks.astype(jnp.bfloat16)
    rows_in = jnp.einsum(
        "nec,nd->ecd", onehot, rows_all, preferred_element_type=jnp.float32
    ).astype(jnp.bfloat16)
    hidden = jnp.einsum("ecd,edf->ecf", rows_in, expert_in, preferred_element_type=jnp.float32)
    half_width = hidden.shape[-1] // 2
    active = (jax.nn.silu(hidden[..., :half_width]) * hidden[..., half_width:]).astype(jnp.bfloat16)
    produced = jnp.einsum(
        "ecf,efd->ecd", active, expert_out, preferred_element_type=jnp.float32
    ).astype(jnp.bfloat16)
    scaled_hi = jnp.where(picks, weight_hi[:, :, None], jnp.zeros_like(onehot))
    scaled_lo = jnp.where(picks, weight_lo[:, :, None], jnp.zeros_like(onehot))
    partial = jnp.einsum(
        "nec,ecd->nd", scaled_hi, produced, preferred_element_type=jnp.float32
    ) + jnp.einsum("nec,ecd->nd", scaled_lo, produced, preferred_element_type=jnp.float32)
    model_width = partial.shape[1]
    page_lines = pl_cdiv(outgoing.shape[1], model_width)
    page_part = jnp.pad(outgoing, ((0, 0), (0, page_lines * model_width - outgoing.shape[1])))
    both = jnp.concatenate(
        [
            partial.astype(jnp.bfloat16).reshape(seq_count, moe_rows, model_width),
            page_part.reshape(seq_count, page_lines, model_width),
        ],
        axis=1,
    )
    returned = lax.all_to_all(both, SEQ_AXES, split_axis=0, concat_axis=0, tiled=True)
    moe = jnp.sum(returned[:, :moe_rows].astype(jnp.float32), axis=0)
    received = returned[:, moe_rows:].reshape(seq_count, -1)[:, : outgoing.shape[1]]
    received = received.reshape(seq_count, rounds, -1).transpose(1, 0, 2)
    block_ids = (
        jnp.arange(seq_count, dtype=jnp.int32)[None, :] * blocks_here
        + jnp.arange(rounds, dtype=jnp.int32)[:, None] * seq_count
        + seq_index
    ).reshape(-1)
    table_ids = jnp.arange(page_slot.shape[0], dtype=jnp.int32)
    page_slots = jnp.sum(
        jnp.where(block_ids[:, None] == table_ids[None, :], page_slot[None, :], 0), axis=1
    )
    local_pages = (
        jnp.zeros((blocks_here, PAGE * pair_width), jnp.bfloat16)
        .at[page_slots]
        .set(received.reshape(blocks_here, -1))
    )
    page_rows = local_pages.reshape(blocks_here, PAGE, kv_local, 2, head_dim).transpose(
        0, 2, 3, 1, 4
    )
    page_rows = page_rows.reshape(blocks_here, kv_local, 2, PAGE * head_dim)
    hidden_out = (residual + residual_scale * moe).astype(jnp.bfloat16)
    return (hidden_out, page_rows)


def solution(mesh):
    seq_count, exp_count = mesh.devices.shape
    split_mesh = Mesh(
        mesh.devices.reshape(2, seq_count // 2, exp_count), ("half", "hseq", "exp")
    )
    return jax.shard_map(
        body,
        mesh=split_mesh,
        in_specs=(
            P(SEQ_AXES, None),
            P(),
            P(None, "exp"),
            P(None, "exp"),
            P(None, "exp"),
            P("exp", None),
            P(SEQ_AXES, "exp"),
            P(),
            P(SEQ_AXES, None, None),
            P(SEQ_AXES, None, None),
            P(("half", "hseq", "exp"), None),
            P(("half", "hseq", "exp"), None),
            P(),
        ),
        out_specs=(P(("half", "hseq", "exp"), None), P(SEQ_AXES, "exp", None, None)),
        check_vma=False,
    )
```

```python
import functools
import math

import jax
import jax.numpy as jnp
from jax import lax
from jax.experimental import pallas as pl
from jax.experimental.pallas import tpu as pltpu
from jax.sharding import Mesh, PartitionSpec as P

HEADS = 24
KV_HEADS = 8
HEAD_DIM = 64
EXPERTS = 32
PAGE = 8
SEQ_AXES = ("half", "hseq")


norm_epsilon = 1e-06
attention_scale = 0.015625
residual_scale = 0.22
masked_score = -1e30


def rms_norm(values, gain_row):
    widened = values.astype(jnp.float32)
    spread = lax.rsqrt(jnp.mean(widened * widened, axis=-1, keepdims=True) + norm_epsilon)
    return (widened * spread * gain_row).astype(jnp.bfloat16)


def partial_kernel(
    flags_ref, q_ref, k_ref, v_ref, acc_ref, m_ref, l_ref, m_sc, l_sc, acc_sc, *, mode, cache_rows,
    group_rows
):
    step = pl.program_id(1)
    last = pl.num_programs(1) - 1
    query_first = flags_ref[0]
    chunk = k_ref.shape[1]
    new_rows = chunk - cache_rows
    new_first = step * new_rows

    @pl.when(step == 0)
    def _():
        m_sc[...] = jnp.full(m_sc.shape, masked_score, jnp.float32)
        l_sc[...] = jnp.zeros(l_sc.shape, jnp.float32)
        acc_sc[...] = jnp.zeros(acc_sc.shape, jnp.float32)

    def update(first, count, causal):
        q = q_ref[0]
        k = k_ref[0, pl.ds(first, count), :]
        v = v_ref[0, pl.ds(first, count), :]
        scores = lax.dot_general(
            q, k, (((1,), (1,)), ((), ())), preferred_element_type=jnp.float32
        ) * attention_scale
        if causal:
            rows = q.shape[0]
            query_pos = query_first + lax.broadcasted_iota(jnp.int32, (rows, count), 0) % group_rows
            column = lax.broadcasted_iota(jnp.int32, (rows, count), 1) + first
            visible = (column < cache_rows) | (new_first + column - cache_rows <= query_pos)
            scores = jnp.where(visible, scores, masked_score)
        m_prev = m_sc[...]
        m_new = jnp.maximum(m_prev, jnp.max(scores, axis=1, keepdims=True))
        weights = jnp.exp(scores - m_new)
        if causal:
            weights = jnp.where(visible, weights, 0.0)
        factor = jnp.exp(m_prev - m_new)
        l_sc[...] = l_sc[...] * factor + jnp.sum(weights, axis=1, keepdims=True)
        acc_sc[...] = acc_sc[...] * factor + jnp.dot(
            weights.astype(jnp.bfloat16), v, preferred_element_type=jnp.float32
        )
        m_sc[...] = m_new

    if mode == "all":
        update(0, chunk, True)
    elif mode == "cache":
        update(0, cache_rows, False)
    else:

        @pl.when(new_first <= query_first + group_rows - 1)
        def _():
            update(cache_rows, new_rows, True)

    @pl.when(step == last)
    def _():
        acc_ref[0] = acc_sc[...]
        m_ref[0] = m_sc[...]
        l_ref[0] = l_sc[...]


def attend_partial(flags, q, kv_all, mode, cache_rows, group_rows):
    heads, rows, dim = q.shape
    devices, _, _, chunk, _ = kv_all.shape
    kernel = functools.partial(partial_kernel, mode=mode, cache_rows=cache_rows, group_rows=group_rows)
    kv_block = (None, None, 1, chunk, dim)
    row_block = pl.BlockSpec((1, rows, 1), lambda h, s, f: (h, 0, 0))
    return pl.pallas_call(
        kernel,
        out_shape=(
            jax.ShapeDtypeStruct((heads, rows, dim), jnp.float32),
            jax.ShapeDtypeStruct((heads, rows, 1), jnp.float32),
            jax.ShapeDtypeStruct((heads, rows, 1), jnp.float32),
        ),
        grid_spec=pltpu.PrefetchScalarGridSpec(
            num_scalar_prefetch=1,
            grid=(heads, devices),
            in_specs=[
                pl.BlockSpec((1, rows, dim), lambda h, s, f: (h, 0, 0)),
                pl.BlockSpec(kv_block, lambda h, s, f: (s, 0, h, 0, 0)),
                pl.BlockSpec(kv_block, lambda h, s, f: (s, 1, h, 0, 0)),
            ],
            out_specs=[pl.BlockSpec((1, rows, dim), lambda h, s, f: (h, 0, 0)), row_block, row_block],
            scratch_shapes=[
                pltpu.VMEM((rows, 1), jnp.float32),
                pltpu.VMEM((rows, 1), jnp.float32),
                pltpu.VMEM((rows, dim), jnp.float32),
            ],
        ),
        compiler_params=pltpu.CompilerParams(dimension_semantics=("arbitrary", "arbitrary")),
    )(flags, q, kv_all, kv_all)


def pl_cdiv(a, b):
    return -(-a // b)


def block_size(piece_rows):
    return math.gcd(piece_rows, 512)


def body(
    hidden_in,
    attn_gain,
    q_weight,
    k_weight,
    v_weight,
    o_weight,
    cache_kv,
    moe_gain,
    expert_in,
    expert_out,
    routes,
    route_prob,
    page_slot,
):
    halves = lax.axis_size("half")
    half_size = lax.axis_size("hseq")
    seq_count = halves * half_size
    half_index = lax.axis_index("half")
    half_pos = lax.axis_index("hseq")
    seq_index = half_index * half_size + half_pos
    exp_index = lax.axis_index("exp")
    tokens_here = hidden_in.shape[0]
    head_dim = HEAD_DIM
    kv_local = k_weight.shape[1] // head_dim
    group_size = HEADS // KV_HEADS
    holds_first = half_index == 0
    normed = rms_norm(hidden_in, attn_gain)
    queries = jnp.dot(normed, q_weight, preferred_element_type=jnp.float32).astype(jnp.bfloat16)
    keys_new = jnp.dot(normed, k_weight, preferred_element_type=jnp.float32).astype(jnp.bfloat16)
    values_new = jnp.dot(normed, v_weight, preferred_element_type=jnp.float32).astype(jnp.bfloat16)
    pair_width = 2 * kv_local * head_dim
    split_new = jnp.stack(
        [
            keys_new.reshape(tokens_here, kv_local, head_dim),
            values_new.reshape(tokens_here, kv_local, head_dim),
        ],
        axis=2,
    )
    pairs_new = split_new.reshape(tokens_here, pair_width)
    blocks_here = tokens_here // PAGE
    rounds = blocks_here // seq_count
    outgoing = pairs_new.reshape(rounds, seq_count, PAGE * pair_width)
    received = lax.all_to_all(outgoing, SEQ_AXES, split_axis=1, concat_axis=1, tiled=True)
    block_ids = (
        jnp.arange(seq_count, dtype=jnp.int32)[None, :] * blocks_here
        + jnp.arange(rounds, dtype=jnp.int32)[:, None] * seq_count
        + seq_index
    ).reshape(-1)
    table_ids = jnp.arange(page_slot.shape[0], dtype=jnp.int32)
    page_slots = jnp.sum(
        jnp.where(block_ids[:, None] == table_ids[None, :], page_slot[None, :], 0), axis=1
    )
    local_pages = (
        jnp.zeros((blocks_here, PAGE * pair_width), jnp.bfloat16)
        .at[page_slots]
        .set(received.reshape(blocks_here, -1))
    )
    page_rows = local_pages.reshape(blocks_here, PAGE, kv_local, 2, head_dim).transpose(
        0, 2, 3, 1, 4
    )
    page_rows = page_rows.reshape(blocks_here, kv_local, 2, PAGE * head_dim)
    kv_own = split_new.transpose(2, 1, 0, 3)
    cache_rows = cache_kv.shape[0]
    cache_own = cache_kv.reshape(cache_rows, kv_local, 2, head_dim).transpose(2, 1, 0, 3)
    kv_piece = jnp.concatenate([cache_own, kv_own], axis=2)
    kv_all = lax.all_to_all(
        jnp.broadcast_to(kv_piece[None], (half_size,) + kv_piece.shape),
        "hseq",
        split_axis=0,
        concat_axis=0,
        tiled=True,
    )
    query_rows = queries.reshape(tokens_here, kv_local, group_size, head_dim)
    query_rows = query_rows.transpose(1, 2, 0, 3).reshape(kv_local, group_size * tokens_here, head_dim)
    partner_rows = lax.ppermute(query_rows, "half", perm=[(0, 1)])
    flags = jnp.reshape(half_pos * tokens_here, (1,)).astype(jnp.int32)
    shapes = dict(cache_rows=cache_rows, group_rows=tokens_here)

    def empty_partial(rows_in):
        heads, rows, _ = rows_in.shape
        return (
            jnp.zeros((heads, rows, head_dim), jnp.float32),
            jnp.full((heads, rows, 1), masked_score, jnp.float32),
            jnp.zeros((heads, rows, 1), jnp.float32),
        )

    far_part = lax.cond(
        holds_first,
        empty_partial,
        lambda rows_in: attend_partial(flags, rows_in, kv_all, "cache", **shapes),
        partner_rows,
    )
    own_part = lax.cond(
        holds_first,
        lambda rows_in: attend_partial(flags, rows_in, kv_all, "all", **shapes),
        lambda rows_in: attend_partial(flags, rows_in, kv_all, "new", **shapes),
        query_rows,
    )
    back_acc, back_best, back_total = lax.ppermute(far_part, "half", perm=[(1, 0)])
    back_best = jnp.where(holds_first, back_best, masked_score)
    back_total = jnp.where(holds_first, back_total, 0.0)
    back_acc = jnp.where(holds_first, back_acc, 0.0)
    own_acc, own_best, own_total = own_part
    best = jnp.maximum(own_best, back_best)
    own_scale = jnp.exp(own_best - best)
    back_scale = jnp.exp(back_best - best)
    attended = (own_acc * own_scale + back_acc * back_scale) / (
        own_total * own_scale + back_total * back_scale
    )
    attended = attended.astype(jnp.bfloat16).reshape(kv_local, group_size, tokens_here, head_dim)
    attended = attended.transpose(2, 0, 1, 3).reshape(tokens_here, -1)
    exp_count = lax.axis_size("exp")
    projected = jnp.dot(attended, o_weight, preferred_element_type=jnp.float32).astype(jnp.bfloat16)
    pieces = lax.all_to_all(
        projected.reshape(exp_count, -1, projected.shape[1]), "exp", split_axis=0, concat_axis=0, tiled=True
    )
    mixed_rows = jnp.sum(pieces.astype(jnp.float32), axis=0)
    moe_rows = mixed_rows.shape[0]
    residual = (
        lax.dynamic_slice_in_dim(hidden_in, exp_index * moe_rows, moe_rows, 0).astype(jnp.float32)
        + residual_scale * mixed_rows
    )
    moe_in = rms_norm(residual, moe_gain)
    top_count = routes.shape[1]
    experts_here = expert_in.shape[0]
    capacity = 2 * moe_rows * top_count // EXPERTS
    share = route_prob / jnp.sum(route_prob, axis=-1, keepdims=True)
    expert_ids = jnp.arange(EXPERTS, dtype=jnp.int32)
    route_hits = routes[:, :, None] == expert_ids[None, None, :]
    full_weight = jnp.sum(jnp.where(route_hits, share[:, :, None], 0.0), axis=1)
    full_hi = full_weight.astype(jnp.bfloat16)
    full_lo = (full_weight - full_hi.astype(jnp.float32)).astype(jnp.bfloat16)
    full_named = jnp.any(route_hits, axis=1).astype(jnp.bfloat16)
    model_width = moe_in.shape[1]
    side_width = 128 * pl_cdiv(3 * EXPERTS, 128)
    side = jnp.concatenate(
        [
            full_named,
            full_hi,
            full_lo,
            jnp.zeros((moe_rows, side_width - 3 * EXPERTS), jnp.bfloat16),
        ],
        axis=1,
    )
    packed = jnp.concatenate([moe_in, side], axis=1)
    crossed = lax.ppermute(packed, "half", perm=[(0, 1), (1, 0)])
    pair = jnp.where(
        holds_first, jnp.stack([packed, crossed]), jnp.stack([crossed, packed])
    )
    fanned = lax.all_to_all(
        jnp.broadcast_to(pair[None], (half_size,) + pair.shape),
        "hseq",
        split_axis=0,
        concat_axis=0,
        tiled=True,
    )
    packed_all = fanned.transpose(1, 0, 2, 3).reshape(seq_count * moe_rows, -1)
    rows_all = packed_all[:, :model_width]
    total_rows = rows_all.shape[0]
    local_first = seq_index * experts_here
    side_all = packed_all[:, model_width:]
    named = (
        lax.dynamic_slice_in_dim(side_all, local_first, experts_here, 1) > 0
    )
    weight_hi = lax.dynamic_slice_in_dim(side_all, EXPERTS + local_first, experts_here, 1)
    weight_lo = lax.dynamic_slice_in_dim(side_all, 2 * EXPERTS + local_first, experts_here, 1)
    named_blocks = named.reshape(seq_count, moe_rows, experts_here).astype(jnp.int32)
    rank = jnp.cumsum(named_blocks, axis=1) - named_blocks
    slot = (jnp.arange(seq_count, dtype=jnp.int32)[:, None, None] * capacity + rank).reshape(
        total_rows, experts_here
    )
    slots_total = seq_count * capacity
    picks = named[:, :, None] & (
        slot[:, :, None] == jnp.arange(slots_total, dtype=jnp.int32)[None, None, :]
    )
    onehot = picks.astype(jnp.bfloat16)
    rows_in = jnp.einsum(
        "nec,nd->ecd", onehot, rows_all, preferred_element_type=jnp.float32
    ).astype(jnp.bfloat16)
    hidden = jnp.einsum("ecd,edf->ecf", rows_in, expert_in, preferred_element_type=jnp.float32)
    half_width = hidden.shape[-1] // 2
    active = (jax.nn.silu(hidden[..., :half_width]) * hidden[..., half_width:]).astype(jnp.bfloat16)
    produced = jnp.einsum(
        "ecf,efd->ecd", active, expert_out, preferred_element_type=jnp.float32
    ).astype(jnp.bfloat16)
    scaled_hi = jnp.where(picks, weight_hi[:, :, None], jnp.zeros_like(onehot))
    scaled_lo = jnp.where(picks, weight_lo[:, :, None], jnp.zeros_like(onehot))
    partial = jnp.einsum(
        "nec,ecd->nd", scaled_hi, produced, preferred_element_type=jnp.float32
    ) + jnp.einsum("nec,ecd->nd", scaled_lo, produced, preferred_element_type=jnp.float32)
    returned = lax.all_to_all(
        partial.astype(jnp.bfloat16).reshape(seq_count, moe_rows, -1),
        SEQ_AXES,
        split_axis=0,
        concat_axis=0,
        tiled=True,
    )
    moe = jnp.sum(returned.astype(jnp.float32), axis=0)
    hidden_out = (residual + residual_scale * moe).astype(jnp.bfloat16)
    return (hidden_out, page_rows)


def solution(mesh):
    seq_count, exp_count = mesh.devices.shape
    split_mesh = Mesh(
        mesh.devices.reshape(2, seq_count // 2, exp_count), ("half", "hseq", "exp")
    )
    return jax.shard_map(
        body,
        mesh=split_mesh,
        in_specs=(
            P(SEQ_AXES, None),
            P(),
            P(None, "exp"),
            P(None, "exp"),
            P(None, "exp"),
            P("exp", None),
            P(SEQ_AXES, "exp"),
            P(),
            P(SEQ_AXES, None, None),
            P(SEQ_AXES, None, None),
            P(("half", "hseq", "exp"), None),
            P(("half", "hseq", "exp"), None),
            P(),
        ),
        out_specs=(P(("half", "hseq", "exp"), None), P(SEQ_AXES, "exp", None, None)),
        check_vma=False,
    )
```

```python
import functools
import math

import jax
import jax.numpy as jnp
from jax import lax
from jax.experimental import pallas as pl
from jax.experimental.pallas import tpu as pltpu
from jax.sharding import Mesh, PartitionSpec as P

HEADS = 24
KV_HEADS = 8
HEAD_DIM = 64
EXPERTS = 32
PAGE = 8
SEQ_AXES = ("half", "hseq")


norm_epsilon = 1e-06
attention_scale = 0.015625
residual_scale = 0.22
masked_score = -1e30


def rms_norm(values, gain_row):
    widened = values.astype(jnp.float32)
    spread = lax.rsqrt(jnp.mean(widened * widened, axis=-1, keepdims=True) + norm_epsilon)
    return (widened * spread * gain_row).astype(jnp.bfloat16)


def partial_kernel(
    flags_ref, q_ref, k_ref, v_ref, acc_ref, m_ref, l_ref, m_sc, l_sc, acc_sc, *, mode, cache_rows,
    group_rows
):
    step = pl.program_id(1)
    last = pl.num_programs(1) - 1
    query_first = flags_ref[0]
    chunk = k_ref.shape[1]
    new_rows = chunk - cache_rows
    new_first = step * new_rows

    @pl.when(step == 0)
    def _():
        m_sc[...] = jnp.full(m_sc.shape, masked_score, jnp.float32)
        l_sc[...] = jnp.zeros(l_sc.shape, jnp.float32)
        acc_sc[...] = jnp.zeros(acc_sc.shape, jnp.float32)

    def update(first, count, causal):
        q = q_ref[0]
        k = k_ref[0, pl.ds(first, count), :]
        v = v_ref[0, pl.ds(first, count), :]
        scores = lax.dot_general(
            q, k, (((1,), (1,)), ((), ())), preferred_element_type=jnp.float32
        ) * attention_scale
        if causal:
            rows = q.shape[0]
            query_pos = query_first + lax.broadcasted_iota(jnp.int32, (rows, count), 0) % group_rows
            column = lax.broadcasted_iota(jnp.int32, (rows, count), 1) + first
            visible = (column < cache_rows) | (new_first + column - cache_rows <= query_pos)
            scores = jnp.where(visible, scores, masked_score)
        m_prev = m_sc[...]
        m_new = jnp.maximum(m_prev, jnp.max(scores, axis=1, keepdims=True))
        weights = jnp.exp(scores - m_new)
        if causal:
            weights = jnp.where(visible, weights, 0.0)
        factor = jnp.exp(m_prev - m_new)
        l_sc[...] = l_sc[...] * factor + jnp.sum(weights, axis=1, keepdims=True)
        acc_sc[...] = acc_sc[...] * factor + jnp.dot(
            weights.astype(jnp.bfloat16), v, preferred_element_type=jnp.float32
        )
        m_sc[...] = m_new

    if mode == "all":
        update(0, chunk, True)
    elif mode == "cache":
        update(0, cache_rows, False)
    else:

        @pl.when(new_first <= query_first + group_rows - 1)
        def _():
            update(cache_rows, new_rows, True)

    @pl.when(step == last)
    def _():
        acc_ref[0] = acc_sc[...]
        m_ref[0] = m_sc[...]
        l_ref[0] = l_sc[...]


def attend_partial(flags, q, kv_all, mode, cache_rows, group_rows):
    heads, rows, dim = q.shape
    devices, _, _, chunk, _ = kv_all.shape
    kernel = functools.partial(partial_kernel, mode=mode, cache_rows=cache_rows, group_rows=group_rows)
    kv_block = (None, None, 1, chunk, dim)
    row_block = pl.BlockSpec((1, rows, 1), lambda h, s, f: (h, 0, 0))
    return pl.pallas_call(
        kernel,
        out_shape=(
            jax.ShapeDtypeStruct((heads, rows, dim), jnp.float32),
            jax.ShapeDtypeStruct((heads, rows, 1), jnp.float32),
            jax.ShapeDtypeStruct((heads, rows, 1), jnp.float32),
        ),
        grid_spec=pltpu.PrefetchScalarGridSpec(
            num_scalar_prefetch=1,
            grid=(heads, devices),
            in_specs=[
                pl.BlockSpec((1, rows, dim), lambda h, s, f: (h, 0, 0)),
                pl.BlockSpec(kv_block, lambda h, s, f: (s, 0, h, 0, 0)),
                pl.BlockSpec(kv_block, lambda h, s, f: (s, 1, h, 0, 0)),
            ],
            out_specs=[pl.BlockSpec((1, rows, dim), lambda h, s, f: (h, 0, 0)), row_block, row_block],
            scratch_shapes=[
                pltpu.VMEM((rows, 1), jnp.float32),
                pltpu.VMEM((rows, 1), jnp.float32),
                pltpu.VMEM((rows, dim), jnp.float32),
            ],
        ),
        compiler_params=pltpu.CompilerParams(dimension_semantics=("arbitrary", "arbitrary")),
    )(flags, q, kv_all, kv_all)


def pl_cdiv(a, b):
    return -(-a // b)


def block_size(piece_rows):
    return math.gcd(piece_rows, 512)


def body(
    hidden_in,
    attn_gain,
    q_weight,
    k_weight,
    v_weight,
    o_weight,
    cache_kv,
    moe_gain,
    expert_in,
    expert_out,
    routes,
    route_prob,
    page_slot,
):
    halves = lax.axis_size("half")
    half_size = lax.axis_size("hseq")
    seq_count = halves * half_size
    half_index = lax.axis_index("half")
    half_pos = lax.axis_index("hseq")
    seq_index = half_index * half_size + half_pos
    exp_index = lax.axis_index("exp")
    tokens_here = hidden_in.shape[0]
    head_dim = HEAD_DIM
    kv_local = k_weight.shape[1] // head_dim
    group_size = HEADS // KV_HEADS
    holds_first = half_index == 0
    normed = rms_norm(hidden_in, attn_gain)
    queries = jnp.dot(normed, q_weight, preferred_element_type=jnp.float32).astype(jnp.bfloat16)
    keys_new = jnp.dot(normed, k_weight, preferred_element_type=jnp.float32).astype(jnp.bfloat16)
    values_new = jnp.dot(normed, v_weight, preferred_element_type=jnp.float32).astype(jnp.bfloat16)
    pair_width = 2 * kv_local * head_dim
    split_new = jnp.stack(
        [
            keys_new.reshape(tokens_here, kv_local, head_dim),
            values_new.reshape(tokens_here, kv_local, head_dim),
        ],
        axis=2,
    )
    pairs_new = split_new.reshape(tokens_here, pair_width)
    blocks_here = tokens_here // PAGE
    rounds = blocks_here // seq_count
    outgoing = pairs_new.reshape(rounds, seq_count, PAGE * pair_width)
    received = lax.all_to_all(outgoing, SEQ_AXES, split_axis=1, concat_axis=1, tiled=True)
    block_ids = (
        jnp.arange(seq_count, dtype=jnp.int32)[None, :] * blocks_here
        + jnp.arange(rounds, dtype=jnp.int32)[:, None] * seq_count
        + seq_index
    ).reshape(-1)
    table_ids = jnp.arange(page_slot.shape[0], dtype=jnp.int32)
    page_slots = jnp.sum(
        jnp.where(block_ids[:, None] == table_ids[None, :], page_slot[None, :], 0), axis=1
    )
    local_pages = (
        jnp.zeros((blocks_here, PAGE * pair_width), jnp.bfloat16)
        .at[page_slots]
        .set(received.reshape(blocks_here, -1))
    )
    page_rows = local_pages.reshape(blocks_here, PAGE, kv_local, 2, head_dim).transpose(
        0, 2, 3, 1, 4
    )
    page_rows = page_rows.reshape(blocks_here, kv_local, 2, PAGE * head_dim)
    kv_own = split_new.transpose(2, 1, 0, 3)
    cache_rows = cache_kv.shape[0]
    cache_own = cache_kv.reshape(cache_rows, kv_local, 2, head_dim).transpose(2, 1, 0, 3)
    kv_piece = jnp.concatenate([cache_own, kv_own], axis=2)
    kv_all = lax.all_to_all(
        jnp.broadcast_to(kv_piece[None], (half_size,) + kv_piece.shape),
        "hseq",
        split_axis=0,
        concat_axis=0,
        tiled=True,
    )
    query_rows = queries.reshape(tokens_here, kv_local, group_size, head_dim)
    query_rows = query_rows.transpose(1, 2, 0, 3).reshape(kv_local, group_size * tokens_here, head_dim)
    partner_rows = lax.ppermute(query_rows, "half", perm=[(0, 1)])
    flags = jnp.reshape(half_pos * tokens_here, (1,)).astype(jnp.int32)
    shapes = dict(cache_rows=cache_rows, group_rows=tokens_here)

    def empty_partial(rows_in):
        heads, rows, _ = rows_in.shape
        return (
            jnp.zeros((heads, rows, head_dim), jnp.float32),
            jnp.full((heads, rows, 1), masked_score, jnp.float32),
            jnp.zeros((heads, rows, 1), jnp.float32),
        )

    far_part = lax.cond(
        holds_first,
        empty_partial,
        lambda rows_in: attend_partial(flags, rows_in, kv_all, "cache", **shapes),
        partner_rows,
    )
    own_part = lax.cond(
        holds_first,
        lambda rows_in: attend_partial(flags, rows_in, kv_all, "all", **shapes),
        lambda rows_in: attend_partial(flags, rows_in, kv_all, "new", **shapes),
        query_rows,
    )
    back_acc, back_best, back_total = lax.ppermute(far_part, "half", perm=[(1, 0)])
    back_best = jnp.where(holds_first, back_best, masked_score)
    back_total = jnp.where(holds_first, back_total, 0.0)
    back_acc = jnp.where(holds_first, back_acc, 0.0)
    own_acc, own_best, own_total = own_part
    best = jnp.maximum(own_best, back_best)
    own_scale = jnp.exp(own_best - best)
    back_scale = jnp.exp(back_best - best)
    attended = (own_acc * own_scale + back_acc * back_scale) / (
        own_total * own_scale + back_total * back_scale
    )
    attended = attended.astype(jnp.bfloat16).reshape(kv_local, group_size, tokens_here, head_dim)
    attended = attended.transpose(2, 0, 1, 3).reshape(tokens_here, -1)
    exp_count = lax.axis_size("exp")
    projected = jnp.dot(attended, o_weight, preferred_element_type=jnp.float32).astype(jnp.bfloat16)
    pieces = lax.all_to_all(
        projected.reshape(exp_count, -1, projected.shape[1]), "exp", split_axis=0, concat_axis=0, tiled=True
    )
    mixed_rows = jnp.sum(pieces.astype(jnp.float32), axis=0)
    moe_rows = mixed_rows.shape[0]
    residual = (
        lax.dynamic_slice_in_dim(hidden_in, exp_index * moe_rows, moe_rows, 0).astype(jnp.float32)
        + residual_scale * mixed_rows
    )
    moe_in = rms_norm(residual, moe_gain)
    top_count = routes.shape[1]
    experts_here = expert_in.shape[0]
    capacity = 2 * moe_rows * top_count // EXPERTS
    share = route_prob / jnp.sum(route_prob, axis=-1, keepdims=True)
    expert_ids = jnp.arange(EXPERTS, dtype=jnp.int32)
    route_hits = routes[:, :, None] == expert_ids[None, None, :]
    full_weight = jnp.sum(jnp.where(route_hits, share[:, :, None], 0.0), axis=1)
    full_hi = full_weight.astype(jnp.bfloat16)
    full_lo = (full_weight - full_hi.astype(jnp.float32)).astype(jnp.bfloat16)
    full_named = jnp.any(route_hits, axis=1).astype(jnp.bfloat16)
    model_width = moe_in.shape[1]
    side_width = 128 * pl_cdiv(3 * EXPERTS, 128)
    side = jnp.concatenate(
        [
            full_named,
            full_hi,
            full_lo,
            jnp.zeros((moe_rows, side_width - 3 * EXPERTS), jnp.bfloat16),
        ],
        axis=1,
    )
    packed = jnp.concatenate([moe_in, side], axis=1)
    crossed = lax.ppermute(packed, "half", perm=[(0, 1), (1, 0)])
    pair = jnp.where(
        holds_first, jnp.stack([packed, crossed]), jnp.stack([crossed, packed])
    )
    fanned = lax.all_to_all(
        jnp.broadcast_to(pair[None], (half_size,) + pair.shape),
        "hseq",
        split_axis=0,
        concat_axis=0,
        tiled=True,
    )
    packed_all = fanned.transpose(1, 0, 2, 3).reshape(seq_count * moe_rows, -1)
    rows_all = packed_all[:, :model_width]
    total_rows = rows_all.shape[0]
    local_first = seq_index * experts_here
    side_all = packed_all[:, model_width:]
    named = (
        lax.dynamic_slice_in_dim(side_all, local_first, experts_here, 1) > 0
    )
    weight_hi = lax.dynamic_slice_in_dim(side_all, EXPERTS + local_first, experts_here, 1)
    weight_lo = lax.dynamic_slice_in_dim(side_all, 2 * EXPERTS + local_first, experts_here, 1)
    named_blocks = named.reshape(seq_count, moe_rows, experts_here).astype(jnp.int32)
    rank = jnp.cumsum(named_blocks, axis=1) - named_blocks
    slot = (jnp.arange(seq_count, dtype=jnp.int32)[:, None, None] * capacity + rank).reshape(
        total_rows, experts_here
    )
    slots_total = seq_count * capacity
    picks = named[:, :, None] & (
        slot[:, :, None] == jnp.arange(slots_total, dtype=jnp.int32)[None, None, :]
    )
    onehot = picks.astype(jnp.bfloat16)
    rows_in = jnp.einsum(
        "nec,nd->ecd", onehot, rows_all, preferred_element_type=jnp.float32
    ).astype(jnp.bfloat16)
    hidden = jnp.einsum("ecd,edf->ecf", rows_in, expert_in, preferred_element_type=jnp.float32)
    half_width = hidden.shape[-1] // 2
    active = (jax.nn.silu(hidden[..., :half_width]) * hidden[..., half_width:]).astype(jnp.bfloat16)
    produced = jnp.einsum(
        "ecf,efd->ecd", active, expert_out, preferred_element_type=jnp.float32
    ).astype(jnp.bfloat16)
    scaled_hi = jnp.where(picks, weight_hi[:, :, None], jnp.zeros_like(onehot))
    scaled_lo = jnp.where(picks, weight_lo[:, :, None], jnp.zeros_like(onehot))
    partial = jnp.einsum(
        "nec,ecd->nd", scaled_hi, produced, preferred_element_type=jnp.float32
    ) + jnp.einsum("nec,ecd->nd", scaled_lo, produced, preferred_element_type=jnp.float32)
    by_dest = partial.astype(jnp.bfloat16).reshape(halves, half_size, moe_rows, -1)
    from_half = lax.all_to_all(
        by_dest.transpose(1, 0, 2, 3), "hseq", split_axis=0, concat_axis=0, tiled=True
    )
    half_sums = jnp.sum(from_half.astype(jnp.float32), axis=0)
    own_sum = jnp.where(holds_first, half_sums[0], half_sums[1])
    other_sum = jnp.where(holds_first, half_sums[1], half_sums[0])
    from_partner = lax.ppermute(other_sum.astype(jnp.bfloat16), "half", perm=[(0, 1), (1, 0)])
    moe = own_sum + from_partner.astype(jnp.float32)
    hidden_out = (residual + residual_scale * moe).astype(jnp.bfloat16)
    return (hidden_out, page_rows)


def solution(mesh):
    seq_count, exp_count = mesh.devices.shape
    split_mesh = Mesh(
        mesh.devices.reshape(2, seq_count // 2, exp_count), ("half", "hseq", "exp")
    )
    return jax.shard_map(
        body,
        mesh=split_mesh,
        in_specs=(
            P(SEQ_AXES, None),
            P(),
            P(None, "exp"),
            P(None, "exp"),
            P(None, "exp"),
            P("exp", None),
            P(SEQ_AXES, "exp"),
            P(),
            P(SEQ_AXES, None, None),
            P(SEQ_AXES, None, None),
            P(("half", "hseq", "exp"), None),
            P(("half", "hseq", "exp"), None),
            P(),
        ),
        out_specs=(P(("half", "hseq", "exp"), None), P(SEQ_AXES, "exp", None, None)),
        check_vma=False,
    )
```

```python
import functools
import math

import jax
import jax.numpy as jnp
from jax import lax
from jax.experimental import pallas as pl
from jax.experimental.pallas import tpu as pltpu
from jax.sharding import Mesh, PartitionSpec as P

HEADS = 24
KV_HEADS = 8
HEAD_DIM = 64
EXPERTS = 32
PAGE = 8
SEQ_AXES = ("half", "hseq")


norm_epsilon = 1e-06
attention_scale = 0.015625
residual_scale = 0.22
masked_score = -1e30


def rms_norm(values, gain_row):
    widened = values.astype(jnp.float32)
    spread = lax.rsqrt(jnp.mean(widened * widened, axis=-1, keepdims=True) + norm_epsilon)
    return (widened * spread * gain_row).astype(jnp.bfloat16)


def partial_kernel(
    flags_ref, q_ref, k_ref, v_ref, acc_ref, m_ref, l_ref, m_sc, l_sc, acc_sc, *, mode, cache_rows,
    group_rows
):
    step = pl.program_id(1)
    last = pl.num_programs(1) - 1
    query_first = flags_ref[0]
    chunk = k_ref.shape[1]
    new_rows = chunk - cache_rows
    new_first = step * new_rows

    @pl.when(step == 0)
    def _():
        m_sc[...] = jnp.full(m_sc.shape, masked_score, jnp.float32)
        l_sc[...] = jnp.zeros(l_sc.shape, jnp.float32)
        acc_sc[...] = jnp.zeros(acc_sc.shape, jnp.float32)

    def update(first, count, causal):
        q = q_ref[0]
        k = k_ref[0, pl.ds(first, count), :]
        v = v_ref[0, pl.ds(first, count), :]
        scores = lax.dot_general(
            q, k, (((1,), (1,)), ((), ())), preferred_element_type=jnp.float32
        ) * attention_scale
        if causal:
            rows = q.shape[0]
            query_pos = query_first + lax.broadcasted_iota(jnp.int32, (rows, count), 0) % group_rows
            column = lax.broadcasted_iota(jnp.int32, (rows, count), 1) + first
            visible = (column < cache_rows) | (new_first + column - cache_rows <= query_pos)
            scores = jnp.where(visible, scores, masked_score)
        m_prev = m_sc[...]
        m_new = jnp.maximum(m_prev, jnp.max(scores, axis=1, keepdims=True))
        weights = jnp.exp(scores - m_new)
        if causal:
            weights = jnp.where(visible, weights, 0.0)
        factor = jnp.exp(m_prev - m_new)
        l_sc[...] = l_sc[...] * factor + jnp.sum(weights, axis=1, keepdims=True)
        acc_sc[...] = acc_sc[...] * factor + jnp.dot(
            weights.astype(jnp.bfloat16), v, preferred_element_type=jnp.float32
        )
        m_sc[...] = m_new

    if mode == "all":
        update(0, chunk, True)
    elif mode == "cache":
        update(0, cache_rows, False)
    else:

        @pl.when(new_first <= query_first + group_rows - 1)
        def _():
            update(cache_rows, new_rows, True)

    @pl.when(step == last)
    def _():
        acc_ref[0] = acc_sc[...]
        m_ref[0] = m_sc[...]
        l_ref[0] = l_sc[...]


def attend_partial(flags, q, kv_all, mode, cache_rows, group_rows):
    heads, rows, dim = q.shape
    devices, _, _, chunk, _ = kv_all.shape
    kernel = functools.partial(partial_kernel, mode=mode, cache_rows=cache_rows, group_rows=group_rows)
    kv_block = (None, None, 1, chunk, dim)
    row_block = pl.BlockSpec((1, rows, 1), lambda h, s, f: (h, 0, 0))
    return pl.pallas_call(
        kernel,
        out_shape=(
            jax.ShapeDtypeStruct((heads, rows, dim), jnp.float32),
            jax.ShapeDtypeStruct((heads, rows, 1), jnp.float32),
            jax.ShapeDtypeStruct((heads, rows, 1), jnp.float32),
        ),
        grid_spec=pltpu.PrefetchScalarGridSpec(
            num_scalar_prefetch=1,
            grid=(heads, devices),
            in_specs=[
                pl.BlockSpec((1, rows, dim), lambda h, s, f: (h, 0, 0)),
                pl.BlockSpec(kv_block, lambda h, s, f: (s, 0, h, 0, 0)),
                pl.BlockSpec(kv_block, lambda h, s, f: (s, 1, h, 0, 0)),
            ],
            out_specs=[pl.BlockSpec((1, rows, dim), lambda h, s, f: (h, 0, 0)), row_block, row_block],
            scratch_shapes=[
                pltpu.VMEM((rows, 1), jnp.float32),
                pltpu.VMEM((rows, 1), jnp.float32),
                pltpu.VMEM((rows, dim), jnp.float32),
            ],
        ),
        compiler_params=pltpu.CompilerParams(dimension_semantics=("arbitrary", "arbitrary")),
    )(flags, q, kv_all, kv_all)


def pl_cdiv(a, b):
    return -(-a // b)


def block_size(piece_rows):
    return math.gcd(piece_rows, 512)


def body(
    hidden_in,
    attn_gain,
    q_weight,
    k_weight,
    v_weight,
    o_weight,
    cache_kv,
    moe_gain,
    expert_in,
    expert_out,
    routes,
    route_prob,
    page_slot,
):
    halves = lax.axis_size("half")
    half_size = lax.axis_size("hseq")
    seq_count = halves * half_size
    half_index = lax.axis_index("half")
    half_pos = lax.axis_index("hseq")
    seq_index = half_index * half_size + half_pos
    exp_index = lax.axis_index("exp")
    tokens_here = hidden_in.shape[0]
    head_dim = HEAD_DIM
    kv_local = k_weight.shape[1] // head_dim
    group_size = HEADS // KV_HEADS
    holds_first = half_index == 0
    normed = rms_norm(hidden_in, attn_gain)
    queries = jnp.dot(normed, q_weight, preferred_element_type=jnp.float32).astype(jnp.bfloat16)
    keys_new = jnp.dot(normed, k_weight, preferred_element_type=jnp.float32).astype(jnp.bfloat16)
    values_new = jnp.dot(normed, v_weight, preferred_element_type=jnp.float32).astype(jnp.bfloat16)
    pair_width = 2 * kv_local * head_dim
    split_new = jnp.stack(
        [
            keys_new.reshape(tokens_here, kv_local, head_dim),
            values_new.reshape(tokens_here, kv_local, head_dim),
        ],
        axis=2,
    )
    pairs_new = split_new.reshape(tokens_here, pair_width)
    blocks_here = tokens_here // PAGE
    rounds = blocks_here // seq_count
    outgoing = pairs_new.reshape(rounds, seq_count, PAGE * pair_width)
    received = lax.all_to_all(outgoing, SEQ_AXES, split_axis=1, concat_axis=1, tiled=True)
    block_ids = (
        jnp.arange(seq_count, dtype=jnp.int32)[None, :] * blocks_here
        + jnp.arange(rounds, dtype=jnp.int32)[:, None] * seq_count
        + seq_index
    ).reshape(-1)
    table_ids = jnp.arange(page_slot.shape[0], dtype=jnp.int32)
    page_slots = jnp.sum(
        jnp.where(block_ids[:, None] == table_ids[None, :], page_slot[None, :], 0), axis=1
    )
    local_pages = (
        jnp.zeros((blocks_here, PAGE * pair_width), jnp.bfloat16)
        .at[page_slots]
        .set(received.reshape(blocks_here, -1))
    )
    page_rows = local_pages.reshape(blocks_here, PAGE, kv_local, 2, head_dim).transpose(
        0, 2, 3, 1, 4
    )
    page_rows = page_rows.reshape(blocks_here, kv_local, 2, PAGE * head_dim)
    kv_own = split_new.transpose(2, 1, 0, 3)
    cache_rows = cache_kv.shape[0]
    cache_own = cache_kv.reshape(cache_rows, kv_local, 2, head_dim).transpose(2, 1, 0, 3)
    kv_piece = jnp.concatenate([cache_own, kv_own], axis=2)
    kv_all = lax.all_to_all(
        jnp.broadcast_to(kv_piece[None], (half_size,) + kv_piece.shape),
        "hseq",
        split_axis=0,
        concat_axis=0,
        tiled=True,
    )
    query_rows = queries.reshape(tokens_here, kv_local, group_size, head_dim)
    query_rows = query_rows.transpose(1, 2, 0, 3).reshape(kv_local, group_size * tokens_here, head_dim)
    partner_rows = lax.ppermute(query_rows, "half", perm=[(0, 1)])
    received, partner_rows = lax.optimization_barrier((received, partner_rows))
    flags = jnp.reshape(half_pos * tokens_here, (1,)).astype(jnp.int32)
    shapes = dict(cache_rows=cache_rows, group_rows=tokens_here)

    def empty_partial(rows_in):
        heads, rows, _ = rows_in.shape
        return (
            jnp.zeros((heads, rows, head_dim), jnp.float32),
            jnp.full((heads, rows, 1), masked_score, jnp.float32),
            jnp.zeros((heads, rows, 1), jnp.float32),
        )

    far_part = lax.cond(
        holds_first,
        empty_partial,
        lambda rows_in: attend_partial(flags, rows_in, kv_all, "cache", **shapes),
        partner_rows,
    )
    own_part = lax.cond(
        holds_first,
        lambda rows_in: attend_partial(flags, rows_in, kv_all, "all", **shapes),
        lambda rows_in: attend_partial(flags, rows_in, kv_all, "new", **shapes),
        query_rows,
    )
    back_acc, back_best, back_total = lax.ppermute(far_part, "half", perm=[(1, 0)])
    back_best = jnp.where(holds_first, back_best, masked_score)
    back_total = jnp.where(holds_first, back_total, 0.0)
    back_acc = jnp.where(holds_first, back_acc, 0.0)
    own_acc, own_best, own_total = own_part
    best = jnp.maximum(own_best, back_best)
    own_scale = jnp.exp(own_best - best)
    back_scale = jnp.exp(back_best - best)
    attended = (own_acc * own_scale + back_acc * back_scale) / (
        own_total * own_scale + back_total * back_scale
    )
    attended = attended.astype(jnp.bfloat16).reshape(kv_local, group_size, tokens_here, head_dim)
    attended = attended.transpose(2, 0, 1, 3).reshape(tokens_here, -1)
    exp_count = lax.axis_size("exp")
    projected = jnp.dot(attended, o_weight, preferred_element_type=jnp.float32).astype(jnp.bfloat16)
    pieces = lax.all_to_all(
        projected.reshape(exp_count, -1, projected.shape[1]), "exp", split_axis=0, concat_axis=0, tiled=True
    )
    mixed_rows = jnp.sum(pieces.astype(jnp.float32), axis=0)
    moe_rows = mixed_rows.shape[0]
    residual = (
        lax.dynamic_slice_in_dim(hidden_in, exp_index * moe_rows, moe_rows, 0).astype(jnp.float32)
        + residual_scale * mixed_rows
    )
    moe_in = rms_norm(residual, moe_gain)
    top_count = routes.shape[1]
    experts_here = expert_in.shape[0]
    capacity = 2 * moe_rows * top_count // EXPERTS
    share = route_prob / jnp.sum(route_prob, axis=-1, keepdims=True)
    expert_ids = jnp.arange(EXPERTS, dtype=jnp.int32)
    route_hits = routes[:, :, None] == expert_ids[None, None, :]
    full_weight = jnp.sum(jnp.where(route_hits, share[:, :, None], 0.0), axis=1)
    full_hi = full_weight.astype(jnp.bfloat16)
    full_lo = (full_weight - full_hi.astype(jnp.float32)).astype(jnp.bfloat16)
    full_named = jnp.any(route_hits, axis=1).astype(jnp.bfloat16)
    model_width = moe_in.shape[1]
    side_width = 128 * pl_cdiv(3 * EXPERTS, 128)
    side = jnp.concatenate(
        [
            full_named,
            full_hi,
            full_lo,
            jnp.zeros((moe_rows, side_width - 3 * EXPERTS), jnp.bfloat16),
        ],
        axis=1,
    )
    packed = jnp.concatenate([moe_in, side], axis=1)
    crossed = lax.ppermute(packed, "half", perm=[(0, 1), (1, 0)])
    pair = jnp.where(
        holds_first, jnp.stack([packed, crossed]), jnp.stack([crossed, packed])
    )
    fanned = lax.all_to_all(
        jnp.broadcast_to(pair[None], (half_size,) + pair.shape),
        "hseq",
        split_axis=0,
        concat_axis=0,
        tiled=True,
    )
    packed_all = fanned.transpose(1, 0, 2, 3).reshape(seq_count * moe_rows, -1)
    rows_all = packed_all[:, :model_width]
    total_rows = rows_all.shape[0]
    local_first = seq_index * experts_here
    side_all = packed_all[:, model_width:]
    named = (
        lax.dynamic_slice_in_dim(side_all, local_first, experts_here, 1) > 0
    )
    weight_hi = lax.dynamic_slice_in_dim(side_all, EXPERTS + local_first, experts_here, 1)
    weight_lo = lax.dynamic_slice_in_dim(side_all, 2 * EXPERTS + local_first, experts_here, 1)
    named_blocks = named.reshape(seq_count, moe_rows, experts_here).astype(jnp.int32)
    rank = jnp.cumsum(named_blocks, axis=1) - named_blocks
    slot = (jnp.arange(seq_count, dtype=jnp.int32)[:, None, None] * capacity + rank).reshape(
        total_rows, experts_here
    )
    slots_total = seq_count * capacity
    picks = named[:, :, None] & (
        slot[:, :, None] == jnp.arange(slots_total, dtype=jnp.int32)[None, None, :]
    )
    onehot = picks.astype(jnp.bfloat16)
    rows_in = jnp.einsum(
        "nec,nd->ecd", onehot, rows_all, preferred_element_type=jnp.float32
    ).astype(jnp.bfloat16)
    hidden = jnp.einsum("ecd,edf->ecf", rows_in, expert_in, preferred_element_type=jnp.float32)
    half_width = hidden.shape[-1] // 2
    active = (jax.nn.silu(hidden[..., :half_width]) * hidden[..., half_width:]).astype(jnp.bfloat16)
    produced = jnp.einsum(
        "ecf,efd->ecd", active, expert_out, preferred_element_type=jnp.float32
    ).astype(jnp.bfloat16)
    scaled_hi = jnp.where(picks, weight_hi[:, :, None], jnp.zeros_like(onehot))
    scaled_lo = jnp.where(picks, weight_lo[:, :, None], jnp.zeros_like(onehot))
    partial = jnp.einsum(
        "nec,ecd->nd", scaled_hi, produced, preferred_element_type=jnp.float32
    ) + jnp.einsum("nec,ecd->nd", scaled_lo, produced, preferred_element_type=jnp.float32)
    by_dest = partial.astype(jnp.bfloat16).reshape(halves, half_size, moe_rows, -1)
    from_half = lax.all_to_all(
        by_dest.transpose(1, 0, 2, 3), "hseq", split_axis=0, concat_axis=0, tiled=True
    )
    half_sums = jnp.sum(from_half.astype(jnp.float32), axis=0)
    own_sum = jnp.where(holds_first, half_sums[0], half_sums[1])
    other_sum = jnp.where(holds_first, half_sums[1], half_sums[0])
    from_partner = lax.ppermute(other_sum.astype(jnp.bfloat16), "half", perm=[(0, 1), (1, 0)])
    moe = own_sum + from_partner.astype(jnp.float32)
    hidden_out = (residual + residual_scale * moe).astype(jnp.bfloat16)
    return (hidden_out, page_rows)


def solution(mesh):
    seq_count, exp_count = mesh.devices.shape
    split_mesh = Mesh(
        mesh.devices.reshape(2, seq_count // 2, exp_count), ("half", "hseq", "exp")
    )
    return jax.shard_map(
        body,
        mesh=split_mesh,
        in_specs=(
            P(SEQ_AXES, None),
            P(),
            P(None, "exp"),
            P(None, "exp"),
            P(None, "exp"),
            P("exp", None),
            P(SEQ_AXES, "exp"),
            P(),
            P(SEQ_AXES, None, None),
            P(SEQ_AXES, None, None),
            P(("half", "hseq", "exp"), None),
            P(("half", "hseq", "exp"), None),
            P(),
        ),
        out_specs=(P(("half", "hseq", "exp"), None), P(SEQ_AXES, "exp", None, None)),
        check_vma=False,
    )
```

```python
import functools
import math

import jax
import jax.numpy as jnp
from jax import lax
from jax.experimental import pallas as pl
from jax.experimental.pallas import tpu as pltpu
from jax.sharding import Mesh, PartitionSpec as P

HEADS = 24
KV_HEADS = 8
HEAD_DIM = 64
EXPERTS = 32
PAGE = 8
SEQ_AXES = ("half", "hseq")


norm_epsilon = 1e-06
attention_scale = 0.015625
residual_scale = 0.22
masked_score = -1e30


def rms_norm(values, gain_row):
    widened = values.astype(jnp.float32)
    spread = lax.rsqrt(jnp.mean(widened * widened, axis=-1, keepdims=True) + norm_epsilon)
    return (widened * spread * gain_row).astype(jnp.bfloat16)


def partial_kernel(
    flags_ref, q_ref, k_ref, v_ref, acc_ref, m_ref, l_ref, m_sc, l_sc, acc_sc, *, mode, cache_rows,
    group_rows
):
    step = pl.program_id(1)
    last = pl.num_programs(1) - 1
    query_first = flags_ref[0]
    chunk = k_ref.shape[1]
    new_rows = chunk - cache_rows
    new_first = step * new_rows

    @pl.when(step == 0)
    def _():
        m_sc[...] = jnp.full(m_sc.shape, masked_score, jnp.float32)
        l_sc[...] = jnp.zeros(l_sc.shape, jnp.float32)
        acc_sc[...] = jnp.zeros(acc_sc.shape, jnp.float32)

    def update(first, count, causal):
        q = q_ref[0]
        k = k_ref[0, pl.ds(first, count), :]
        v = v_ref[0, pl.ds(first, count), :]
        scores = lax.dot_general(
            q, k, (((1,), (1,)), ((), ())), preferred_element_type=jnp.float32
        ) * attention_scale
        if causal:
            rows = q.shape[0]
            query_pos = query_first + lax.broadcasted_iota(jnp.int32, (rows, count), 0) % group_rows
            column = lax.broadcasted_iota(jnp.int32, (rows, count), 1) + first
            visible = (column < cache_rows) | (new_first + column - cache_rows <= query_pos)
            scores = jnp.where(visible, scores, masked_score)
        m_prev = m_sc[...]
        m_new = jnp.maximum(m_prev, jnp.max(scores, axis=1, keepdims=True))
        weights = jnp.exp(scores - m_new)
        if causal:
            weights = jnp.where(visible, weights, 0.0)
        factor = jnp.exp(m_prev - m_new)
        l_sc[...] = l_sc[...] * factor + jnp.sum(weights, axis=1, keepdims=True)
        acc_sc[...] = acc_sc[...] * factor + jnp.dot(
            weights.astype(jnp.bfloat16), v, preferred_element_type=jnp.float32
        )
        m_sc[...] = m_new

    if mode == "all":
        update(0, chunk, True)
    elif mode == "cache":
        update(0, cache_rows, False)
    else:

        @pl.when(new_first <= query_first + group_rows - 1)
        def _():
            update(cache_rows, new_rows, True)

    @pl.when(step == last)
    def _():
        acc_ref[0] = acc_sc[...]
        m_ref[0] = m_sc[...]
        l_ref[0] = l_sc[...]


def attend_partial(flags, q, kv_all, mode, cache_rows, group_rows):
    heads, rows, dim = q.shape
    devices, _, _, chunk, _ = kv_all.shape
    kernel = functools.partial(partial_kernel, mode=mode, cache_rows=cache_rows, group_rows=group_rows)
    kv_block = (None, None, 1, chunk, dim)
    row_block = pl.BlockSpec((1, rows, 1), lambda h, s, f: (h, 0, 0))
    return pl.pallas_call(
        kernel,
        out_shape=(
            jax.ShapeDtypeStruct((heads, rows, dim), jnp.float32),
            jax.ShapeDtypeStruct((heads, rows, 1), jnp.float32),
            jax.ShapeDtypeStruct((heads, rows, 1), jnp.float32),
        ),
        grid_spec=pltpu.PrefetchScalarGridSpec(
            num_scalar_prefetch=1,
            grid=(heads, devices),
            in_specs=[
                pl.BlockSpec((1, rows, dim), lambda h, s, f: (h, 0, 0)),
                pl.BlockSpec(kv_block, lambda h, s, f: (s, 0, h, 0, 0)),
                pl.BlockSpec(kv_block, lambda h, s, f: (s, 1, h, 0, 0)),
            ],
            out_specs=[pl.BlockSpec((1, rows, dim), lambda h, s, f: (h, 0, 0)), row_block, row_block],
            scratch_shapes=[
                pltpu.VMEM((rows, 1), jnp.float32),
                pltpu.VMEM((rows, 1), jnp.float32),
                pltpu.VMEM((rows, dim), jnp.float32),
            ],
        ),
        compiler_params=pltpu.CompilerParams(dimension_semantics=("arbitrary", "arbitrary")),
    )(flags, q, kv_all, kv_all)


def pl_cdiv(a, b):
    return -(-a // b)


def block_size(piece_rows):
    return math.gcd(piece_rows, 512)


def body(
    hidden_in,
    attn_gain,
    q_weight,
    k_weight,
    v_weight,
    o_weight,
    cache_kv,
    moe_gain,
    expert_in,
    expert_out,
    routes,
    route_prob,
    page_slot,
):
    halves = lax.axis_size("half")
    half_size = lax.axis_size("hseq")
    seq_count = halves * half_size
    half_index = lax.axis_index("half")
    half_pos = lax.axis_index("hseq")
    seq_index = half_index * half_size + half_pos
    exp_index = lax.axis_index("exp")
    tokens_here = hidden_in.shape[0]
    head_dim = HEAD_DIM
    kv_local = k_weight.shape[1] // head_dim
    group_size = HEADS // KV_HEADS
    holds_first = half_index == 0
    normed = rms_norm(hidden_in, attn_gain)
    queries = jnp.dot(normed, q_weight, preferred_element_type=jnp.float32).astype(jnp.bfloat16)
    keys_new = jnp.dot(normed, k_weight, preferred_element_type=jnp.float32).astype(jnp.bfloat16)
    values_new = jnp.dot(normed, v_weight, preferred_element_type=jnp.float32).astype(jnp.bfloat16)
    pair_width = 2 * kv_local * head_dim
    split_new = jnp.stack(
        [
            keys_new.reshape(tokens_here, kv_local, head_dim),
            values_new.reshape(tokens_here, kv_local, head_dim),
        ],
        axis=2,
    )
    pairs_new = split_new.reshape(tokens_here, pair_width)
    blocks_here = tokens_here // PAGE
    rounds = blocks_here // seq_count
    outgoing = pairs_new.reshape(rounds, seq_count, PAGE * pair_width)
    received = lax.all_to_all(outgoing, SEQ_AXES, split_axis=1, concat_axis=1, tiled=True)
    block_ids = (
        jnp.arange(seq_count, dtype=jnp.int32)[None, :] * blocks_here
        + jnp.arange(rounds, dtype=jnp.int32)[:, None] * seq_count
        + seq_index
    ).reshape(-1)
    table_ids = jnp.arange(page_slot.shape[0], dtype=jnp.int32)
    page_slots = jnp.sum(
        jnp.where(block_ids[:, None] == table_ids[None, :], page_slot[None, :], 0), axis=1
    )
    local_pages = (
        jnp.zeros((blocks_here, PAGE * pair_width), jnp.bfloat16)
        .at[page_slots]
        .set(received.reshape(blocks_here, -1))
    )
    page_rows = local_pages.reshape(blocks_here, PAGE, kv_local, 2, head_dim).transpose(
        0, 2, 3, 1, 4
    )
    page_rows = page_rows.reshape(blocks_here, kv_local, 2, PAGE * head_dim)
    kv_own = split_new.transpose(2, 1, 0, 3)
    cache_rows = cache_kv.shape[0]
    cache_own = cache_kv.reshape(cache_rows, kv_local, 2, head_dim).transpose(2, 1, 0, 3)
    kv_piece = jnp.concatenate([cache_own, kv_own], axis=2)
    kv_all = lax.all_to_all(
        jnp.broadcast_to(kv_piece[None], (half_size,) + kv_piece.shape),
        "hseq",
        split_axis=0,
        concat_axis=0,
        tiled=True,
    )
    query_rows = queries.reshape(tokens_here, kv_local, group_size, head_dim)
    query_rows = query_rows.transpose(1, 2, 0, 3).reshape(kv_local, group_size * tokens_here, head_dim)
    partner_rows = lax.ppermute(query_rows, "half", perm=[(0, 1)])
    flags = jnp.reshape(half_pos * tokens_here, (1,)).astype(jnp.int32)
    shapes = dict(cache_rows=cache_rows, group_rows=tokens_here)

    def empty_partial(rows_in):
        heads, rows, _ = rows_in.shape
        return (
            jnp.zeros((heads, rows, head_dim), jnp.float32),
            jnp.full((heads, rows, 1), masked_score, jnp.float32),
            jnp.zeros((heads, rows, 1), jnp.float32),
        )

    far_part = lax.cond(
        holds_first,
        empty_partial,
        lambda rows_in: attend_partial(flags, rows_in, kv_all, "cache", **shapes),
        partner_rows,
    )
    own_part = lax.cond(
        holds_first,
        lambda rows_in: attend_partial(flags, rows_in, kv_all, "all", **shapes),
        lambda rows_in: attend_partial(flags, rows_in, kv_all, "new", **shapes),
        query_rows,
    )
    back_acc, back_best, back_total = lax.ppermute(far_part, "half", perm=[(1, 0)])
    back_best = jnp.where(holds_first, back_best, masked_score)
    back_total = jnp.where(holds_first, back_total, 0.0)
    back_acc = jnp.where(holds_first, back_acc, 0.0)
    own_acc, own_best, own_total = own_part
    best = jnp.maximum(own_best, back_best)
    own_scale = jnp.exp(own_best - best)
    back_scale = jnp.exp(back_best - best)
    attended = (own_acc * own_scale + back_acc * back_scale) / (
        own_total * own_scale + back_total * back_scale
    )
    attended = attended.astype(jnp.bfloat16).reshape(kv_local, group_size, tokens_here, head_dim)
    attended = attended.transpose(2, 0, 1, 3).reshape(tokens_here, -1)
    exp_count = lax.axis_size("exp")
    projected = jnp.dot(attended, o_weight, preferred_element_type=jnp.float32).astype(jnp.bfloat16)
    pieces = lax.all_to_all(
        projected.reshape(exp_count, -1, projected.shape[1]), "exp", split_axis=0, concat_axis=0, tiled=True
    )
    mixed_rows = jnp.sum(pieces.astype(jnp.float32), axis=0)
    moe_rows = mixed_rows.shape[0]
    residual = (
        lax.dynamic_slice_in_dim(hidden_in, exp_index * moe_rows, moe_rows, 0).astype(jnp.float32)
        + residual_scale * mixed_rows
    )
    moe_in = rms_norm(residual, moe_gain)
    top_count = routes.shape[1]
    experts_here = expert_in.shape[0]
    capacity = 2 * moe_rows * top_count // EXPERTS
    share = route_prob / jnp.sum(route_prob, axis=-1, keepdims=True)
    expert_ids = jnp.arange(EXPERTS, dtype=jnp.int32)
    route_hits = routes[:, :, None] == expert_ids[None, None, :]
    full_weight = jnp.sum(jnp.where(route_hits, share[:, :, None], 0.0), axis=1)
    full_hi = full_weight.astype(jnp.bfloat16)
    full_lo = (full_weight - full_hi.astype(jnp.float32)).astype(jnp.bfloat16)
    full_named = jnp.any(route_hits, axis=1).astype(jnp.bfloat16)
    model_width = moe_in.shape[1]
    side_width = 128 * pl_cdiv(3 * EXPERTS, 128)
    side = jnp.concatenate(
        [
            full_named,
            full_hi,
            full_lo,
            jnp.zeros((moe_rows, side_width - 3 * EXPERTS), jnp.bfloat16),
        ],
        axis=1,
    )
    packed = jnp.concatenate([moe_in, side], axis=1)
    crossed = lax.ppermute(packed, "half", perm=[(0, 1), (1, 0)])
    pair = jnp.where(
        holds_first, jnp.stack([packed, crossed]), jnp.stack([crossed, packed])
    )
    fanned = lax.all_to_all(
        jnp.broadcast_to(pair[None], (half_size,) + pair.shape),
        "hseq",
        split_axis=0,
        concat_axis=0,
        tiled=True,
    )
    packed_all = fanned.transpose(1, 0, 2, 3).reshape(seq_count * moe_rows, -1)
    rows_all = packed_all[:, :model_width]
    total_rows = rows_all.shape[0]
    local_first = seq_index * experts_here
    side_all = packed_all[:, model_width:]
    named = (
        lax.dynamic_slice_in_dim(side_all, local_first, experts_here, 1) > 0
    )
    weight_hi = lax.dynamic_slice_in_dim(side_all, EXPERTS + local_first, experts_here, 1)
    weight_lo = lax.dynamic_slice_in_dim(side_all, 2 * EXPERTS + local_first, experts_here, 1)
    named_blocks = named.reshape(seq_count, moe_rows, experts_here).astype(jnp.int32)
    earlier_rows = (
        jnp.arange(moe_rows, dtype=jnp.int32)[None, :] < jnp.arange(moe_rows, dtype=jnp.int32)[:, None]
    ).astype(jnp.bfloat16)
    rank = jnp.einsum(
        "ij,bjx->bix", earlier_rows, named_blocks.astype(jnp.bfloat16), preferred_element_type=jnp.float32
    ).astype(jnp.int32)
    slot = (jnp.arange(seq_count, dtype=jnp.int32)[:, None, None] * capacity + rank).reshape(
        total_rows, experts_here
    )
    slots_total = seq_count * capacity
    picks = named[:, :, None] & (
        slot[:, :, None] == jnp.arange(slots_total, dtype=jnp.int32)[None, None, :]
    )
    onehot = picks.astype(jnp.bfloat16)
    rows_in = jnp.einsum(
        "nec,nd->ecd", onehot, rows_all, preferred_element_type=jnp.float32
    ).astype(jnp.bfloat16)
    hidden = jnp.einsum("ecd,edf->ecf", rows_in, expert_in, preferred_element_type=jnp.float32)
    half_width = hidden.shape[-1] // 2
    active = (jax.nn.silu(hidden[..., :half_width]) * hidden[..., half_width:]).astype(jnp.bfloat16)
    produced = jnp.einsum(
        "ecf,efd->ecd", active, expert_out, preferred_element_type=jnp.float32
    ).astype(jnp.bfloat16)
    scaled_hi = jnp.where(picks, weight_hi[:, :, None], jnp.zeros_like(onehot))
    scaled_lo = jnp.where(picks, weight_lo[:, :, None], jnp.zeros_like(onehot))
    partial = jnp.einsum(
        "nec,ecd->nd", scaled_hi, produced, preferred_element_type=jnp.float32
    ) + jnp.einsum("nec,ecd->nd", scaled_lo, produced, preferred_element_type=jnp.float32)
    by_dest = partial.astype(jnp.bfloat16).reshape(halves, half_size, moe_rows, -1)
    from_half = lax.all_to_all(
        by_dest.transpose(1, 0, 2, 3), "hseq", split_axis=0, concat_axis=0, tiled=True
    )
    half_sums = jnp.sum(from_half.astype(jnp.float32), axis=0)
    own_sum = jnp.where(holds_first, half_sums[0], half_sums[1])
    other_sum = jnp.where(holds_first, half_sums[1], half_sums[0])
    from_partner = lax.ppermute(other_sum.astype(jnp.bfloat16), "half", perm=[(0, 1), (1, 0)])
    moe = own_sum + from_partner.astype(jnp.float32)
    hidden_out = (residual + residual_scale * moe).astype(jnp.bfloat16)
    return (hidden_out, page_rows)


def solution(mesh):
    seq_count, exp_count = mesh.devices.shape
    split_mesh = Mesh(
        mesh.devices.reshape(2, seq_count // 2, exp_count), ("half", "hseq", "exp")
    )
    return jax.shard_map(
        body,
        mesh=split_mesh,
        in_specs=(
            P(SEQ_AXES, None),
            P(),
            P(None, "exp"),
            P(None, "exp"),
            P(None, "exp"),
            P("exp", None),
            P(SEQ_AXES, "exp"),
            P(),
            P(SEQ_AXES, None, None),
            P(SEQ_AXES, None, None),
            P(("half", "hseq", "exp"), None),
            P(("half", "hseq", "exp"), None),
            P(),
        ),
        out_specs=(P(("half", "hseq", "exp"), None), P(SEQ_AXES, "exp", None, None)),
        check_vma=False,
    )
```

```python
import functools
import math

import jax
import jax.numpy as jnp
from jax import lax
from jax.experimental import pallas as pl
from jax.experimental.pallas import tpu as pltpu
from jax.sharding import Mesh, PartitionSpec as P

HEADS = 24
KV_HEADS = 8
HEAD_DIM = 64
EXPERTS = 32
PAGE = 8
SEQ_AXES = ("half", "hseq")


norm_epsilon = 1e-06
attention_scale = 0.015625
residual_scale = 0.22
masked_score = -1e30


def rms_norm(values, gain_row):
    widened = values.astype(jnp.float32)
    spread = lax.rsqrt(jnp.mean(widened * widened, axis=-1, keepdims=True) + norm_epsilon)
    return (widened * spread * gain_row).astype(jnp.bfloat16)


def partial_kernel(
    flags_ref, q_ref, k_ref, v_ref, acc_ref, m_ref, l_ref, m_sc, l_sc, acc_sc, *, mode, cache_rows,
    group_rows
):
    step = pl.program_id(1)
    last = pl.num_programs(1) - 1
    query_first = flags_ref[0]
    chunk = k_ref.shape[1]
    new_rows = chunk - cache_rows
    new_first = step * new_rows

    @pl.when(step == 0)
    def _():
        m_sc[...] = jnp.full(m_sc.shape, masked_score, jnp.float32)
        l_sc[...] = jnp.zeros(l_sc.shape, jnp.float32)
        acc_sc[...] = jnp.zeros(acc_sc.shape, jnp.float32)

    def update(first, count, causal):
        q = q_ref[0]
        k = k_ref[0, pl.ds(first, count), :]
        v = v_ref[0, pl.ds(first, count), :]
        scores = lax.dot_general(
            q, k, (((1,), (1,)), ((), ())), preferred_element_type=jnp.float32
        ) * attention_scale
        if causal:
            rows = q.shape[0]
            query_pos = query_first + lax.broadcasted_iota(jnp.int32, (rows, count), 0) % group_rows
            column = lax.broadcasted_iota(jnp.int32, (rows, count), 1) + first
            visible = (column < cache_rows) | (new_first + column - cache_rows <= query_pos)
            scores = jnp.where(visible, scores, masked_score)
        m_prev = m_sc[...]
        m_new = jnp.maximum(m_prev, jnp.max(scores, axis=1, keepdims=True))
        weights = jnp.exp(scores - m_new)
        if causal:
            weights = jnp.where(visible, weights, 0.0)
        factor = jnp.exp(m_prev - m_new)
        l_sc[...] = l_sc[...] * factor + jnp.sum(weights, axis=1, keepdims=True)
        acc_sc[...] = acc_sc[...] * factor + jnp.dot(
            weights.astype(jnp.bfloat16), v, preferred_element_type=jnp.float32
        )
        m_sc[...] = m_new

    if mode == "all":
        update(0, chunk, True)
    elif mode == "cache":
        update(0, cache_rows, False)
    else:

        @pl.when(new_first <= query_first + group_rows - 1)
        def _():
            update(cache_rows, new_rows, True)

    @pl.when(step == last)
    def _():
        acc_ref[0] = acc_sc[...]
        m_ref[0] = m_sc[...]
        l_ref[0] = l_sc[...]


def attend_partial(flags, q, kv_all, mode, cache_rows, group_rows):
    heads, rows, dim = q.shape
    devices, _, _, chunk, _ = kv_all.shape
    kernel = functools.partial(partial_kernel, mode=mode, cache_rows=cache_rows, group_rows=group_rows)
    kv_block = (None, None, 1, chunk, dim)
    row_block = pl.BlockSpec((1, rows, 1), lambda h, s, f: (h, 0, 0))
    return pl.pallas_call(
        kernel,
        out_shape=(
            jax.ShapeDtypeStruct((heads, rows, dim), jnp.float32),
            jax.ShapeDtypeStruct((heads, rows, 1), jnp.float32),
            jax.ShapeDtypeStruct((heads, rows, 1), jnp.float32),
        ),
        grid_spec=pltpu.PrefetchScalarGridSpec(
            num_scalar_prefetch=1,
            grid=(heads, devices),
            in_specs=[
                pl.BlockSpec((1, rows, dim), lambda h, s, f: (h, 0, 0)),
                pl.BlockSpec(kv_block, lambda h, s, f: (s, 0, h, 0, 0)),
                pl.BlockSpec(kv_block, lambda h, s, f: (s, 1, h, 0, 0)),
            ],
            out_specs=[pl.BlockSpec((1, rows, dim), lambda h, s, f: (h, 0, 0)), row_block, row_block],
            scratch_shapes=[
                pltpu.VMEM((rows, 1), jnp.float32),
                pltpu.VMEM((rows, 1), jnp.float32),
                pltpu.VMEM((rows, dim), jnp.float32),
            ],
        ),
        compiler_params=pltpu.CompilerParams(dimension_semantics=("arbitrary", "arbitrary")),
    )(flags, q, kv_all, kv_all)


def pl_cdiv(a, b):
    return -(-a // b)


def block_size(piece_rows):
    return math.gcd(piece_rows, 512)


def body(
    hidden_in,
    attn_gain,
    q_weight,
    k_weight,
    v_weight,
    o_weight,
    cache_kv,
    moe_gain,
    expert_in,
    expert_out,
    routes,
    route_prob,
    page_slot,
):
    halves = lax.axis_size("half")
    half_size = lax.axis_size("hseq")
    seq_count = halves * half_size
    half_index = lax.axis_index("half")
    half_pos = lax.axis_index("hseq")
    seq_index = half_index * half_size + half_pos
    exp_index = lax.axis_index("exp")
    tokens_here = hidden_in.shape[0]
    head_dim = HEAD_DIM
    kv_local = k_weight.shape[1] // head_dim
    group_size = HEADS // KV_HEADS
    holds_first = half_index == 0
    normed = rms_norm(hidden_in, attn_gain)
    queries = jnp.dot(normed, q_weight, preferred_element_type=jnp.float32).astype(jnp.bfloat16)
    keys_new = jnp.dot(normed, k_weight, preferred_element_type=jnp.float32).astype(jnp.bfloat16)
    values_new = jnp.dot(normed, v_weight, preferred_element_type=jnp.float32).astype(jnp.bfloat16)
    pair_width = 2 * kv_local * head_dim
    split_new = jnp.stack(
        [
            keys_new.reshape(tokens_here, kv_local, head_dim),
            values_new.reshape(tokens_here, kv_local, head_dim),
        ],
        axis=2,
    )
    pairs_new = split_new.reshape(tokens_here, pair_width)
    blocks_here = tokens_here // PAGE
    rounds = blocks_here // seq_count
    outgoing = pairs_new.reshape(rounds, seq_count, PAGE * pair_width).transpose(1, 0, 2)
    outgoing = outgoing.reshape(seq_count, -1)
    kv_own = split_new.transpose(2, 1, 0, 3)
    cache_rows = cache_kv.shape[0]
    cache_own = cache_kv.reshape(cache_rows, kv_local, 2, head_dim).transpose(2, 1, 0, 3)
    kv_piece = jnp.concatenate([cache_own, kv_own], axis=2)
    kv_all = lax.all_to_all(
        jnp.broadcast_to(kv_piece[None], (half_size,) + kv_piece.shape),
        "hseq",
        split_axis=0,
        concat_axis=0,
        tiled=True,
    )
    query_rows = queries.reshape(tokens_here, kv_local, group_size, head_dim)
    query_rows = query_rows.transpose(1, 2, 0, 3).reshape(kv_local, group_size * tokens_here, head_dim)
    partner_rows = lax.ppermute(query_rows, "half", perm=[(0, 1)])
    flags = jnp.reshape(half_pos * tokens_here, (1,)).astype(jnp.int32)
    shapes = dict(cache_rows=cache_rows, group_rows=tokens_here)

    def empty_partial(rows_in):
        heads, rows, _ = rows_in.shape
        return (
            jnp.zeros((heads, rows, head_dim), jnp.float32),
            jnp.full((heads, rows, 1), masked_score, jnp.float32),
            jnp.zeros((heads, rows, 1), jnp.float32),
        )

    far_part = lax.cond(
        holds_first,
        empty_partial,
        lambda rows_in: attend_partial(flags, rows_in, kv_all, "cache", **shapes),
        partner_rows,
    )
    own_part = lax.cond(
        holds_first,
        lambda rows_in: attend_partial(flags, rows_in, kv_all, "all", **shapes),
        lambda rows_in: attend_partial(flags, rows_in, kv_all, "new", **shapes),
        query_rows,
    )
    back_acc, back_best, back_total = lax.ppermute(far_part, "half", perm=[(1, 0)])
    back_best = jnp.where(holds_first, back_best, masked_score)
    back_total = jnp.where(holds_first, back_total, 0.0)
    back_acc = jnp.where(holds_first, back_acc, 0.0)
    own_acc, own_best, own_total = own_part
    best = jnp.maximum(own_best, back_best)
    own_scale = jnp.exp(own_best - best)
    back_scale = jnp.exp(back_best - best)
    attended = (own_acc * own_scale + back_acc * back_scale) / (
        own_total * own_scale + back_total * back_scale
    )
    attended = attended.astype(jnp.bfloat16).reshape(kv_local, group_size, tokens_here, head_dim)
    attended = attended.transpose(2, 0, 1, 3).reshape(tokens_here, -1)
    exp_count = lax.axis_size("exp")
    projected = jnp.dot(attended, o_weight, preferred_element_type=jnp.float32).astype(jnp.bfloat16)
    pieces = lax.all_to_all(
        projected.reshape(exp_count, -1, projected.shape[1]), "exp", split_axis=0, concat_axis=0, tiled=True
    )
    mixed_rows = jnp.sum(pieces.astype(jnp.float32), axis=0)
    moe_rows = mixed_rows.shape[0]
    residual = (
        lax.dynamic_slice_in_dim(hidden_in, exp_index * moe_rows, moe_rows, 0).astype(jnp.float32)
        + residual_scale * mixed_rows
    )
    moe_in = rms_norm(residual, moe_gain)
    top_count = routes.shape[1]
    experts_here = expert_in.shape[0]
    capacity = 2 * moe_rows * top_count // EXPERTS
    share = route_prob / jnp.sum(route_prob, axis=-1, keepdims=True)
    expert_ids = jnp.arange(EXPERTS, dtype=jnp.int32)
    route_hits = routes[:, :, None] == expert_ids[None, None, :]
    full_weight = jnp.sum(jnp.where(route_hits, share[:, :, None], 0.0), axis=1)
    full_hi = full_weight.astype(jnp.bfloat16)
    full_lo = (full_weight - full_hi.astype(jnp.float32)).astype(jnp.bfloat16)
    full_named = jnp.any(route_hits, axis=1).astype(jnp.bfloat16)
    model_width = moe_in.shape[1]
    side_width = 128 * pl_cdiv(3 * EXPERTS, 128)
    side = jnp.concatenate(
        [
            full_named,
            full_hi,
            full_lo,
            jnp.zeros((moe_rows, side_width - 3 * EXPERTS), jnp.bfloat16),
        ],
        axis=1,
    )
    packed = jnp.concatenate([moe_in, side], axis=1)
    crossed = lax.ppermute(packed, "half", perm=[(0, 1), (1, 0)])
    pair = jnp.where(
        holds_first, jnp.stack([packed, crossed]), jnp.stack([crossed, packed])
    )
    fanned = lax.all_to_all(
        jnp.broadcast_to(pair[None], (half_size,) + pair.shape),
        "hseq",
        split_axis=0,
        concat_axis=0,
        tiled=True,
    )
    packed_all = fanned.transpose(1, 0, 2, 3).reshape(seq_count * moe_rows, -1)
    rows_all = packed_all[:, :model_width]
    total_rows = rows_all.shape[0]
    local_first = seq_index * experts_here
    side_all = packed_all[:, model_width:]
    named = (
        lax.dynamic_slice_in_dim(side_all, local_first, experts_here, 1) > 0
    )
    weight_hi = lax.dynamic_slice_in_dim(side_all, EXPERTS + local_first, experts_here, 1)
    weight_lo = lax.dynamic_slice_in_dim(side_all, 2 * EXPERTS + local_first, experts_here, 1)
    named_blocks = named.reshape(seq_count, moe_rows, experts_here).astype(jnp.int32)
    earlier_rows = (
        jnp.arange(moe_rows, dtype=jnp.int32)[None, :] < jnp.arange(moe_rows, dtype=jnp.int32)[:, None]
    ).astype(jnp.bfloat16)
    rank = jnp.einsum(
        "ij,bjx->bix", earlier_rows, named_blocks.astype(jnp.bfloat16), preferred_element_type=jnp.float32
    ).astype(jnp.int32)
    slot = (jnp.arange(seq_count, dtype=jnp.int32)[:, None, None] * capacity + rank).reshape(
        total_rows, experts_here
    )
    slots_total = seq_count * capacity
    picks = named[:, :, None] & (
        slot[:, :, None] == jnp.arange(slots_total, dtype=jnp.int32)[None, None, :]
    )
    onehot = picks.astype(jnp.bfloat16)
    rows_in = jnp.einsum(
        "nec,nd->ecd", onehot, rows_all, preferred_element_type=jnp.float32
    ).astype(jnp.bfloat16)
    hidden = jnp.einsum("ecd,edf->ecf", rows_in, expert_in, preferred_element_type=jnp.float32)
    half_width = hidden.shape[-1] // 2
    active = (jax.nn.silu(hidden[..., :half_width]) * hidden[..., half_width:]).astype(jnp.bfloat16)
    produced = jnp.einsum(
        "ecf,efd->ecd", active, expert_out, preferred_element_type=jnp.float32
    ).astype(jnp.bfloat16)
    scaled_hi = jnp.where(picks, weight_hi[:, :, None], jnp.zeros_like(onehot))
    scaled_lo = jnp.where(picks, weight_lo[:, :, None], jnp.zeros_like(onehot))
    partial = jnp.einsum(
        "nec,ecd->nd", scaled_hi, produced, preferred_element_type=jnp.float32
    ) + jnp.einsum("nec,ecd->nd", scaled_lo, produced, preferred_element_type=jnp.float32)
    model_width = partial.shape[1]
    page_lines = pl_cdiv(outgoing.shape[1], model_width)
    page_part = jnp.pad(outgoing, ((0, 0), (0, page_lines * model_width - outgoing.shape[1])))
    page_part = page_part.reshape(halves, half_size, page_lines, model_width)
    by_dest = jnp.concatenate(
        [
            partial.astype(jnp.bfloat16).reshape(halves, half_size, moe_rows, model_width),
            page_part,
        ],
        axis=2,
    )
    from_half = lax.all_to_all(
        by_dest.transpose(1, 0, 2, 3), "hseq", split_axis=0, concat_axis=0, tiled=True
    )
    half_sums = jnp.sum(from_half[:, :, :moe_rows].astype(jnp.float32), axis=0)
    pages_in = from_half[:, :, moe_rows:]
    own_sum = jnp.where(holds_first, half_sums[0], half_sums[1])
    other_sum = jnp.where(holds_first, half_sums[1], half_sums[0])
    own_pages = jnp.where(holds_first, pages_in[:, 0], pages_in[:, 1])
    other_pages = jnp.where(holds_first, pages_in[:, 1], pages_in[:, 0])
    forward = jnp.concatenate(
        [other_sum.astype(jnp.bfloat16), other_pages.reshape(-1, model_width)], axis=0
    )
    from_partner = lax.ppermute(forward, "half", perm=[(0, 1), (1, 0)])
    moe = own_sum + from_partner[:moe_rows].astype(jnp.float32)
    partner_pages = from_partner[moe_rows:].reshape(half_size, page_lines, model_width)
    pages_by_source = jnp.where(
        holds_first,
        jnp.concatenate([own_pages, partner_pages], axis=0),
        jnp.concatenate([partner_pages, own_pages], axis=0),
    )
    received = pages_by_source.reshape(seq_count, -1)[:, : outgoing.shape[1]]
    received = received.reshape(seq_count, rounds, -1).transpose(1, 0, 2)
    block_ids = (
        jnp.arange(seq_count, dtype=jnp.int32)[None, :] * blocks_here
        + jnp.arange(rounds, dtype=jnp.int32)[:, None] * seq_count
        + seq_index
    ).reshape(-1)
    table_ids = jnp.arange(page_slot.shape[0], dtype=jnp.int32)
    page_slots = jnp.sum(
        jnp.where(block_ids[:, None] == table_ids[None, :], page_slot[None, :], 0), axis=1
    )
    local_pages = (
        jnp.zeros((blocks_here, PAGE * pair_width), jnp.bfloat16)
        .at[page_slots]
        .set(received.reshape(blocks_here, -1))
    )
    page_rows = local_pages.reshape(blocks_here, PAGE, kv_local, 2, head_dim).transpose(
        0, 2, 3, 1, 4
    )
    page_rows = page_rows.reshape(blocks_here, kv_local, 2, PAGE * head_dim)
    hidden_out = (residual + residual_scale * moe).astype(jnp.bfloat16)
    return (hidden_out, page_rows)


def solution(mesh):
    seq_count, exp_count = mesh.devices.shape
    split_mesh = Mesh(
        mesh.devices.reshape(2, seq_count // 2, exp_count), ("half", "hseq", "exp")
    )
    return jax.shard_map(
        body,
        mesh=split_mesh,
        in_specs=(
            P(SEQ_AXES, None),
            P(),
            P(None, "exp"),
            P(None, "exp"),
            P(None, "exp"),
            P("exp", None),
            P(SEQ_AXES, "exp"),
            P(),
            P(SEQ_AXES, None, None),
            P(SEQ_AXES, None, None),
            P(("half", "hseq", "exp"), None),
            P(("half", "hseq", "exp"), None),
            P(),
        ),
        out_specs=(P(("half", "hseq", "exp"), None), P(SEQ_AXES, "exp", None, None)),
        check_vma=False,
    )
```

```python
import functools
import math

import jax
import jax.numpy as jnp
from jax import lax
from jax.experimental import pallas as pl
from jax.experimental.pallas import tpu as pltpu
from jax.sharding import Mesh, PartitionSpec as P

HEADS = 24
KV_HEADS = 8
HEAD_DIM = 64
EXPERTS = 32
PAGE = 8
SEQ_AXES = ("half", "hseq")


norm_epsilon = 1e-06
attention_scale = 0.015625
residual_scale = 0.22
masked_score = -1e30


def rms_norm(values, gain_row):
    widened = values.astype(jnp.float32)
    spread = lax.rsqrt(jnp.mean(widened * widened, axis=-1, keepdims=True) + norm_epsilon)
    return (widened * spread * gain_row).astype(jnp.bfloat16)


def partial_kernel(
    flags_ref, q_ref, k_ref, v_ref, acc_ref, m_ref, l_ref, m_sc, l_sc, acc_sc, *, mode, cache_rows,
    group_rows
):
    step = pl.program_id(1)
    last = pl.num_programs(1) - 1
    query_first = flags_ref[0]
    chunk = k_ref.shape[1]
    new_rows = chunk - cache_rows
    new_first = step * new_rows

    @pl.when(step == 0)
    def _():
        m_sc[...] = jnp.full(m_sc.shape, masked_score, jnp.float32)
        l_sc[...] = jnp.zeros(l_sc.shape, jnp.float32)
        acc_sc[...] = jnp.zeros(acc_sc.shape, jnp.float32)

    def update(first, count, causal):
        q = q_ref[0]
        k = k_ref[0, pl.ds(first, count), :]
        v = v_ref[0, pl.ds(first, count), :]
        scores = lax.dot_general(
            q, k, (((1,), (1,)), ((), ())), preferred_element_type=jnp.float32
        ) * attention_scale
        if causal:
            rows = q.shape[0]
            query_pos = query_first + lax.broadcasted_iota(jnp.int32, (rows, count), 0) % group_rows
            column = lax.broadcasted_iota(jnp.int32, (rows, count), 1) + first
            visible = (column < cache_rows) | (new_first + column - cache_rows <= query_pos)
            scores = jnp.where(visible, scores, masked_score)
        m_prev = m_sc[...]
        m_new = jnp.maximum(m_prev, jnp.max(scores, axis=1, keepdims=True))
        weights = jnp.exp(scores - m_new)
        if causal:
            weights = jnp.where(visible, weights, 0.0)
        factor = jnp.exp(m_prev - m_new)
        l_sc[...] = l_sc[...] * factor + jnp.sum(weights, axis=1, keepdims=True)
        acc_sc[...] = acc_sc[...] * factor + jnp.dot(
            weights.astype(jnp.bfloat16), v, preferred_element_type=jnp.float32
        )
        m_sc[...] = m_new

    if mode == "all":
        update(0, chunk, True)
    elif mode == "cache":
        update(0, cache_rows, False)
    else:

        @pl.when(new_first <= query_first + group_rows - 1)
        def _():
            update(cache_rows, new_rows, True)

    @pl.when(step == last)
    def _():
        acc_ref[0] = acc_sc[...]
        m_ref[0] = m_sc[...]
        l_ref[0] = l_sc[...]


def attend_partial(flags, q, kv_all, mode, cache_rows, group_rows):
    heads, rows, dim = q.shape
    devices, _, _, chunk, _ = kv_all.shape
    kernel = functools.partial(partial_kernel, mode=mode, cache_rows=cache_rows, group_rows=group_rows)
    kv_block = (None, None, 1, chunk, dim)
    row_block = pl.BlockSpec((1, rows, 1), lambda h, s, f: (h, 0, 0))
    return pl.pallas_call(
        kernel,
        out_shape=(
            jax.ShapeDtypeStruct((heads, rows, dim), jnp.float32),
            jax.ShapeDtypeStruct((heads, rows, 1), jnp.float32),
            jax.ShapeDtypeStruct((heads, rows, 1), jnp.float32),
        ),
        grid_spec=pltpu.PrefetchScalarGridSpec(
            num_scalar_prefetch=1,
            grid=(heads, devices),
            in_specs=[
                pl.BlockSpec((1, rows, dim), lambda h, s, f: (h, 0, 0)),
                pl.BlockSpec(kv_block, lambda h, s, f: (s, 0, h, 0, 0)),
                pl.BlockSpec(kv_block, lambda h, s, f: (s, 1, h, 0, 0)),
            ],
            out_specs=[pl.BlockSpec((1, rows, dim), lambda h, s, f: (h, 0, 0)), row_block, row_block],
            scratch_shapes=[
                pltpu.VMEM((rows, 1), jnp.float32),
                pltpu.VMEM((rows, 1), jnp.float32),
                pltpu.VMEM((rows, dim), jnp.float32),
            ],
        ),
        compiler_params=pltpu.CompilerParams(dimension_semantics=("arbitrary", "arbitrary")),
    )(flags, q, kv_all, kv_all)


def pl_cdiv(a, b):
    return -(-a // b)


def block_size(piece_rows):
    return math.gcd(piece_rows, 512)


def body(
    hidden_in,
    attn_gain,
    q_weight,
    k_weight,
    v_weight,
    o_weight,
    cache_kv,
    moe_gain,
    expert_in,
    expert_out,
    routes,
    route_prob,
    page_slot,
):
    halves = lax.axis_size("half")
    half_size = lax.axis_size("hseq")
    seq_count = halves * half_size
    half_index = lax.axis_index("half")
    half_pos = lax.axis_index("hseq")
    seq_index = half_index * half_size + half_pos
    exp_index = lax.axis_index("exp")
    tokens_here = hidden_in.shape[0]
    head_dim = HEAD_DIM
    kv_local = k_weight.shape[1] // head_dim
    group_size = HEADS // KV_HEADS
    holds_first = half_index == 0
    normed = rms_norm(hidden_in, attn_gain)
    queries = jnp.dot(normed, q_weight, preferred_element_type=jnp.float32).astype(jnp.bfloat16)
    keys_new = jnp.dot(normed, k_weight, preferred_element_type=jnp.float32).astype(jnp.bfloat16)
    values_new = jnp.dot(normed, v_weight, preferred_element_type=jnp.float32).astype(jnp.bfloat16)
    pair_width = 2 * kv_local * head_dim
    split_new = jnp.stack(
        [
            keys_new.reshape(tokens_here, kv_local, head_dim),
            values_new.reshape(tokens_here, kv_local, head_dim),
        ],
        axis=2,
    )
    pairs_new = split_new.reshape(tokens_here, pair_width)
    blocks_here = tokens_here // PAGE
    rounds = blocks_here // seq_count
    outgoing = pairs_new.reshape(rounds, seq_count, PAGE * pair_width)
    received = lax.all_to_all(outgoing, SEQ_AXES, split_axis=1, concat_axis=1, tiled=True)
    block_ids = (
        jnp.arange(seq_count, dtype=jnp.int32)[None, :] * blocks_here
        + jnp.arange(rounds, dtype=jnp.int32)[:, None] * seq_count
        + seq_index
    ).reshape(-1)
    table_ids = jnp.arange(page_slot.shape[0], dtype=jnp.int32)
    page_slots = jnp.sum(
        jnp.where(block_ids[:, None] == table_ids[None, :], page_slot[None, :], 0), axis=1
    )
    local_pages = (
        jnp.zeros((blocks_here, PAGE * pair_width), jnp.bfloat16)
        .at[page_slots]
        .set(received.reshape(blocks_here, -1))
    )
    page_rows = local_pages.reshape(blocks_here, PAGE, kv_local, 2, head_dim).transpose(
        0, 2, 3, 1, 4
    )
    page_rows = page_rows.reshape(blocks_here, kv_local, 2, PAGE * head_dim)
    kv_own = split_new.transpose(2, 1, 0, 3)
    cache_rows = cache_kv.shape[0]
    cache_own = cache_kv.reshape(cache_rows, kv_local, 2, head_dim).transpose(2, 1, 0, 3)
    kv_piece = jnp.concatenate([cache_own, kv_own], axis=2)
    kv_all = lax.all_to_all(
        jnp.broadcast_to(kv_piece[None], (half_size,) + kv_piece.shape),
        "hseq",
        split_axis=0,
        concat_axis=0,
        tiled=True,
    )
    query_rows = queries.reshape(tokens_here, kv_local, group_size, head_dim)
    query_rows = query_rows.transpose(1, 2, 0, 3).reshape(kv_local, group_size * tokens_here, head_dim)
    partner_rows = lax.ppermute(query_rows, "half", perm=[(0, 1)])
    flags = jnp.reshape(half_pos * tokens_here, (1,)).astype(jnp.int32)
    shapes = dict(cache_rows=cache_rows, group_rows=tokens_here)

    def empty_partial(rows_in):
        heads, rows, _ = rows_in.shape
        return (
            jnp.zeros((heads, rows, head_dim), jnp.float32),
            jnp.full((heads, rows, 1), masked_score, jnp.float32),
            jnp.zeros((heads, rows, 1), jnp.float32),
        )

    far_part = lax.cond(
        holds_first,
        empty_partial,
        lambda rows_in: attend_partial(flags, rows_in, kv_all, "cache", **shapes),
        partner_rows,
    )
    own_part = lax.cond(
        holds_first,
        lambda rows_in: attend_partial(flags, rows_in, kv_all, "all", **shapes),
        lambda rows_in: attend_partial(flags, rows_in, kv_all, "new", **shapes),
        query_rows,
    )
    back_acc, back_best, back_total = lax.ppermute(far_part, "half", perm=[(1, 0)])
    back_best = jnp.where(holds_first, back_best, masked_score)
    back_total = jnp.where(holds_first, back_total, 0.0)
    back_acc = jnp.where(holds_first, back_acc, 0.0)
    own_acc, own_best, own_total = own_part
    best = jnp.maximum(own_best, back_best)
    own_scale = jnp.exp(own_best - best)
    back_scale = jnp.exp(back_best - best)
    attended = (own_acc * own_scale + back_acc * back_scale) / (
        own_total * own_scale + back_total * back_scale
    )
    attended = attended.astype(jnp.bfloat16).reshape(kv_local, group_size, tokens_here, head_dim)
    attended = attended.transpose(2, 0, 1, 3).reshape(tokens_here, -1)
    exp_count = lax.axis_size("exp")
    projected = jnp.dot(attended, o_weight, preferred_element_type=jnp.float32).astype(jnp.bfloat16)
    pieces = lax.all_to_all(
        projected.reshape(exp_count, -1, projected.shape[1]), "exp", split_axis=0, concat_axis=0, tiled=True
    )
    mixed_rows = jnp.sum(pieces.astype(jnp.float32), axis=0)
    moe_rows = mixed_rows.shape[0]
    residual = (
        lax.dynamic_slice_in_dim(hidden_in, exp_index * moe_rows, moe_rows, 0).astype(jnp.float32)
        + residual_scale * mixed_rows
    )
    moe_in = rms_norm(residual, moe_gain)
    top_count = routes.shape[1]
    experts_here = expert_in.shape[0]
    capacity = 2 * moe_rows * top_count // EXPERTS
    share = route_prob / jnp.sum(route_prob, axis=-1, keepdims=True)
    expert_ids = jnp.arange(EXPERTS, dtype=jnp.int32)
    route_hits = routes[:, :, None] == expert_ids[None, None, :]
    full_weight = jnp.sum(jnp.where(route_hits, share[:, :, None], 0.0), axis=1)
    full_hi = full_weight.astype(jnp.bfloat16)
    full_lo = (full_weight - full_hi.astype(jnp.float32)).astype(jnp.bfloat16)
    full_named = jnp.any(route_hits, axis=1).astype(jnp.bfloat16)
    model_width = moe_in.shape[1]
    side_width = 128 * pl_cdiv(3 * EXPERTS, 128)
    side = jnp.concatenate(
        [
            full_named,
            full_hi,
            full_lo,
            jnp.zeros((moe_rows, side_width - 3 * EXPERTS), jnp.bfloat16),
        ],
        axis=1,
    )
    packed = jnp.concatenate([moe_in, side], axis=1)
    crossed = lax.ppermute(packed, "half", perm=[(0, 1), (1, 0)])
    pair = jnp.where(
        holds_first, jnp.stack([packed, crossed]), jnp.stack([crossed, packed])
    )
    fanned = lax.all_to_all(
        jnp.broadcast_to(pair[None], (half_size,) + pair.shape),
        "hseq",
        split_axis=0,
        concat_axis=0,
        tiled=True,
    )
    packed_all = fanned.transpose(1, 0, 2, 3).reshape(seq_count * moe_rows, -1)
    rows_all = packed_all[:, :model_width]
    total_rows = rows_all.shape[0]
    local_first = seq_index * experts_here
    side_all = packed_all[:, model_width:]
    named = (
        lax.dynamic_slice_in_dim(side_all, local_first, experts_here, 1) > 0
    )
    weight_hi = lax.dynamic_slice_in_dim(side_all, EXPERTS + local_first, experts_here, 1)
    weight_lo = lax.dynamic_slice_in_dim(side_all, 2 * EXPERTS + local_first, experts_here, 1)
    named_blocks = named.reshape(seq_count, moe_rows, experts_here).astype(jnp.int32)
    earlier_rows = (
        jnp.arange(moe_rows, dtype=jnp.int32)[None, :] < jnp.arange(moe_rows, dtype=jnp.int32)[:, None]
    ).astype(jnp.bfloat16)
    rank = jnp.einsum(
        "ij,bjx->bix", earlier_rows, named_blocks.astype(jnp.bfloat16), preferred_element_type=jnp.float32
    ).astype(jnp.int32)
    slot = (jnp.arange(seq_count, dtype=jnp.int32)[:, None, None] * capacity + rank).reshape(
        total_rows, experts_here
    )
    slots_total = seq_count * capacity
    picks = named[:, :, None] & (
        slot[:, :, None] == jnp.arange(slots_total, dtype=jnp.int32)[None, None, :]
    )
    onehot = picks.astype(jnp.bfloat16)
    rows_in = jnp.einsum(
        "nec,nd->ecd", onehot, rows_all, preferred_element_type=jnp.float32
    ).astype(jnp.bfloat16)
    hidden = jnp.einsum("ecd,edf->ecf", rows_in, expert_in, preferred_element_type=jnp.float32)
    half_width = hidden.shape[-1] // 2
    active = (jax.nn.silu(hidden[..., :half_width]) * hidden[..., half_width:]).astype(jnp.bfloat16)
    produced = jnp.einsum(
        "ecf,efd->ecd", active, expert_out, preferred_element_type=jnp.float32
    ).astype(jnp.bfloat16)
    scaled_hi = jnp.where(picks, weight_hi[:, :, None], jnp.zeros_like(onehot))
    scaled_lo = jnp.where(picks, weight_lo[:, :, None], jnp.zeros_like(onehot))
    partial = jnp.einsum(
        "nec,ecd->nd", scaled_hi, produced, preferred_element_type=jnp.float32
    ) + jnp.einsum("nec,ecd->nd", scaled_lo, produced, preferred_element_type=jnp.float32)
    received, partial = lax.optimization_barrier((received, partial))
    by_dest = partial.astype(jnp.bfloat16).reshape(halves, half_size, moe_rows, -1)
    from_half = lax.all_to_all(
        by_dest.transpose(1, 0, 2, 3), "hseq", split_axis=0, concat_axis=0, tiled=True
    )
    half_sums = jnp.sum(from_half.astype(jnp.float32), axis=0)
    own_sum = jnp.where(holds_first, half_sums[0], half_sums[1])
    other_sum = jnp.where(holds_first, half_sums[1], half_sums[0])
    from_partner = lax.ppermute(other_sum.astype(jnp.bfloat16), "half", perm=[(0, 1), (1, 0)])
    moe = own_sum + from_partner.astype(jnp.float32)
    hidden_out = (residual + residual_scale * moe).astype(jnp.bfloat16)
    return (hidden_out, page_rows)


def solution(mesh):
    seq_count, exp_count = mesh.devices.shape
    split_mesh = Mesh(
        mesh.devices.reshape(2, seq_count // 2, exp_count), ("half", "hseq", "exp")
    )
    return jax.shard_map(
        body,
        mesh=split_mesh,
        in_specs=(
            P(SEQ_AXES, None),
            P(),
            P(None, "exp"),
            P(None, "exp"),
            P(None, "exp"),
            P("exp", None),
            P(SEQ_AXES, "exp"),
            P(),
            P(SEQ_AXES, None, None),
            P(SEQ_AXES, None, None),
            P(("half", "hseq", "exp"), None),
            P(("half", "hseq", "exp"), None),
            P(),
        ),
        out_specs=(P(("half", "hseq", "exp"), None), P(SEQ_AXES, "exp", None, None)),
        check_vma=False,
    )
```

```python
import functools
import math

import jax
import jax.numpy as jnp
from jax import lax
from jax.experimental import pallas as pl
from jax.experimental.pallas import tpu as pltpu
from jax.sharding import Mesh, PartitionSpec as P

HEADS = 24
KV_HEADS = 8
HEAD_DIM = 64
EXPERTS = 32
PAGE = 8
SEQ_AXES = ("half", "hseq")


norm_epsilon = 1e-06
attention_scale = 0.015625
residual_scale = 0.22
masked_score = -1e30


def rms_norm(values, gain_row):
    widened = values.astype(jnp.float32)
    spread = lax.rsqrt(jnp.mean(widened * widened, axis=-1, keepdims=True) + norm_epsilon)
    return (widened * spread * gain_row).astype(jnp.bfloat16)


def partial_kernel(
    flags_ref, q_ref, k_ref, v_ref, acc_ref, m_ref, l_ref, m_sc, l_sc, acc_sc, *, mode, cache_rows,
    group_rows
):
    step = pl.program_id(1)
    last = pl.num_programs(1) - 1
    query_first = flags_ref[0]
    chunk = k_ref.shape[1]
    new_rows = chunk - cache_rows
    new_first = step * new_rows

    @pl.when(step == 0)
    def _():
        m_sc[...] = jnp.full(m_sc.shape, masked_score, jnp.float32)
        l_sc[...] = jnp.zeros(l_sc.shape, jnp.float32)
        acc_sc[...] = jnp.zeros(acc_sc.shape, jnp.float32)

    def update(first, count, causal):
        q = q_ref[0]
        k = k_ref[0, pl.ds(first, count), :]
        v = v_ref[0, pl.ds(first, count), :]
        scores = lax.dot_general(
            q, k, (((1,), (1,)), ((), ())), preferred_element_type=jnp.float32
        ) * attention_scale
        if causal:
            rows = q.shape[0]
            query_pos = query_first + lax.broadcasted_iota(jnp.int32, (rows, count), 0) % group_rows
            column = lax.broadcasted_iota(jnp.int32, (rows, count), 1) + first
            visible = (column < cache_rows) | (new_first + column - cache_rows <= query_pos)
            scores = jnp.where(visible, scores, masked_score)
        m_prev = m_sc[...]
        m_new = jnp.maximum(m_prev, jnp.max(scores, axis=1, keepdims=True))
        weights = jnp.exp(scores - m_new)
        if causal:
            weights = jnp.where(visible, weights, 0.0)
        factor = jnp.exp(m_prev - m_new)
        l_sc[...] = l_sc[...] * factor + jnp.sum(weights, axis=1, keepdims=True)
        acc_sc[...] = acc_sc[...] * factor + jnp.dot(
            weights.astype(jnp.bfloat16), v, preferred_element_type=jnp.float32
        )
        m_sc[...] = m_new

    if mode == "all":
        update(0, chunk, True)
    elif mode == "cache":
        update(0, cache_rows, False)
    else:

        @pl.when(new_first <= query_first + group_rows - 1)
        def _():
            update(cache_rows, new_rows, True)

    @pl.when(step == last)
    def _():
        acc_ref[0] = acc_sc[...]
        m_ref[0] = m_sc[...]
        l_ref[0] = l_sc[...]


def attend_partial(flags, q, kv_all, mode, cache_rows, group_rows):
    heads, rows, dim = q.shape
    devices, _, _, chunk, _ = kv_all.shape
    kernel = functools.partial(partial_kernel, mode=mode, cache_rows=cache_rows, group_rows=group_rows)
    kv_block = (None, None, 1, chunk, dim)
    row_block = pl.BlockSpec((1, rows, 1), lambda h, s, f: (h, 0, 0))
    return pl.pallas_call(
        kernel,
        out_shape=(
            jax.ShapeDtypeStruct((heads, rows, dim), jnp.float32),
            jax.ShapeDtypeStruct((heads, rows, 1), jnp.float32),
            jax.ShapeDtypeStruct((heads, rows, 1), jnp.float32),
        ),
        grid_spec=pltpu.PrefetchScalarGridSpec(
            num_scalar_prefetch=1,
            grid=(heads, devices),
            in_specs=[
                pl.BlockSpec((1, rows, dim), lambda h, s, f: (h, 0, 0)),
                pl.BlockSpec(kv_block, lambda h, s, f: (s, 0, h, 0, 0)),
                pl.BlockSpec(kv_block, lambda h, s, f: (s, 1, h, 0, 0)),
            ],
            out_specs=[pl.BlockSpec((1, rows, dim), lambda h, s, f: (h, 0, 0)), row_block, row_block],
            scratch_shapes=[
                pltpu.VMEM((rows, 1), jnp.float32),
                pltpu.VMEM((rows, 1), jnp.float32),
                pltpu.VMEM((rows, dim), jnp.float32),
            ],
        ),
        compiler_params=pltpu.CompilerParams(dimension_semantics=("arbitrary", "arbitrary")),
    )(flags, q, kv_all, kv_all)


def pl_cdiv(a, b):
    return -(-a // b)


def block_size(piece_rows):
    return math.gcd(piece_rows, 512)


def body(
    hidden_in,
    attn_gain,
    q_weight,
    k_weight,
    v_weight,
    o_weight,
    cache_kv,
    moe_gain,
    expert_in,
    expert_out,
    routes,
    route_prob,
    page_slot,
):
    halves = lax.axis_size("half")
    half_size = lax.axis_size("hseq")
    seq_count = halves * half_size
    half_index = lax.axis_index("half")
    half_pos = lax.axis_index("hseq")
    seq_index = half_index * half_size + half_pos
    exp_index = lax.axis_index("exp")
    tokens_here = hidden_in.shape[0]
    head_dim = HEAD_DIM
    kv_local = k_weight.shape[1] // head_dim
    group_size = HEADS // KV_HEADS
    holds_first = half_index == 0
    normed = rms_norm(hidden_in, attn_gain)
    queries = jnp.dot(normed, q_weight, preferred_element_type=jnp.float32).astype(jnp.bfloat16)
    keys_new = jnp.dot(normed, k_weight, preferred_element_type=jnp.float32).astype(jnp.bfloat16)
    values_new = jnp.dot(normed, v_weight, preferred_element_type=jnp.float32).astype(jnp.bfloat16)
    pair_width = 2 * kv_local * head_dim
    split_new = jnp.stack(
        [
            keys_new.reshape(tokens_here, kv_local, head_dim),
            values_new.reshape(tokens_here, kv_local, head_dim),
        ],
        axis=2,
    )
    pairs_new = split_new.reshape(tokens_here, pair_width)
    blocks_here = tokens_here // PAGE
    rounds = blocks_here // seq_count
    outgoing = pairs_new.reshape(rounds, seq_count, PAGE * pair_width)
    received = lax.all_to_all(outgoing, SEQ_AXES, split_axis=1, concat_axis=1, tiled=True)
    block_ids = (
        jnp.arange(seq_count, dtype=jnp.int32)[None, :] * blocks_here
        + jnp.arange(rounds, dtype=jnp.int32)[:, None] * seq_count
        + seq_index
    ).reshape(-1)
    table_ids = jnp.arange(page_slot.shape[0], dtype=jnp.int32)
    page_slots = jnp.sum(
        jnp.where(block_ids[:, None] == table_ids[None, :], page_slot[None, :], 0), axis=1
    )
    local_pages = (
        jnp.zeros((blocks_here, PAGE * pair_width), jnp.bfloat16)
        .at[page_slots]
        .set(received.reshape(blocks_here, -1))
    )
    page_rows = local_pages.reshape(blocks_here, PAGE, kv_local, 2, head_dim).transpose(
        0, 2, 3, 1, 4
    )
    page_rows = page_rows.reshape(blocks_here, kv_local, 2, PAGE * head_dim)
    kv_own = split_new.transpose(2, 1, 0, 3)
    cache_rows = cache_kv.shape[0]
    cache_own = cache_kv.reshape(cache_rows, kv_local, 2, head_dim).transpose(2, 1, 0, 3)
    kv_piece = jnp.concatenate([cache_own, kv_own], axis=2)
    kv_all = lax.all_to_all(
        jnp.broadcast_to(kv_piece[None], (half_size,) + kv_piece.shape),
        "hseq",
        split_axis=0,
        concat_axis=0,
        tiled=True,
    )
    query_rows = queries.reshape(tokens_here, kv_local, group_size, head_dim)
    query_rows = query_rows.transpose(1, 2, 0, 3).reshape(kv_local, group_size * tokens_here, head_dim)
    partner_rows = lax.ppermute(query_rows, "half", perm=[(0, 1)])
    flags = jnp.reshape(half_pos * tokens_here, (1,)).astype(jnp.int32)
    shapes = dict(cache_rows=cache_rows, group_rows=tokens_here)

    def empty_partial(rows_in):
        heads, rows, _ = rows_in.shape
        return jnp.concatenate(
            [
                jnp.zeros((heads, rows, head_dim), jnp.float32),
                jnp.full((heads, rows, 1), masked_score, jnp.float32),
                jnp.zeros((heads, rows, 1), jnp.float32),
            ],
            axis=2,
        )

    far_part = lax.cond(
        holds_first,
        empty_partial,
        lambda rows_in: jnp.concatenate(
            attend_partial(flags, rows_in, kv_all, "cache", **shapes), axis=2
        ),
        partner_rows,
    )
    own_part = lax.cond(
        holds_first,
        lambda rows_in: attend_partial(flags, rows_in, kv_all, "all", **shapes),
        lambda rows_in: attend_partial(flags, rows_in, kv_all, "new", **shapes),
        query_rows,
    )
    back = lax.ppermute(far_part, "half", perm=[(1, 0)])
    back_acc = back[..., :head_dim]
    back_best = back[..., head_dim : head_dim + 1]
    back_total = back[..., head_dim + 1 :]
    back_best = jnp.where(holds_first, back_best, masked_score)
    back_total = jnp.where(holds_first, back_total, 0.0)
    back_acc = jnp.where(holds_first, back_acc, 0.0)
    own_acc, own_best, own_total = own_part
    best = jnp.maximum(own_best, back_best)
    own_scale = jnp.exp(own_best - best)
    back_scale = jnp.exp(back_best - best)
    attended = (own_acc * own_scale + back_acc * back_scale) / (
        own_total * own_scale + back_total * back_scale
    )
    attended = attended.astype(jnp.bfloat16).reshape(kv_local, group_size, tokens_here, head_dim)
    attended = attended.transpose(2, 0, 1, 3).reshape(tokens_here, -1)
    exp_count = lax.axis_size("exp")
    projected = jnp.dot(attended, o_weight, preferred_element_type=jnp.float32).astype(jnp.bfloat16)
    pieces = lax.all_to_all(
        projected.reshape(exp_count, -1, projected.shape[1]), "exp", split_axis=0, concat_axis=0, tiled=True
    )
    mixed_rows = jnp.sum(pieces.astype(jnp.float32), axis=0)
    moe_rows = mixed_rows.shape[0]
    residual = (
        lax.dynamic_slice_in_dim(hidden_in, exp_index * moe_rows, moe_rows, 0).astype(jnp.float32)
        + residual_scale * mixed_rows
    )
    moe_in = rms_norm(residual, moe_gain)
    top_count = routes.shape[1]
    experts_here = expert_in.shape[0]
    capacity = 2 * moe_rows * top_count // EXPERTS
    share = route_prob / jnp.sum(route_prob, axis=-1, keepdims=True)
    expert_ids = jnp.arange(EXPERTS, dtype=jnp.int32)
    route_hits = routes[:, :, None] == expert_ids[None, None, :]
    full_weight = jnp.sum(jnp.where(route_hits, share[:, :, None], 0.0), axis=1)
    full_hi = full_weight.astype(jnp.bfloat16)
    full_lo = (full_weight - full_hi.astype(jnp.float32)).astype(jnp.bfloat16)
    full_named = jnp.any(route_hits, axis=1).astype(jnp.bfloat16)
    model_width = moe_in.shape[1]
    side_width = 128 * pl_cdiv(3 * EXPERTS, 128)
    side = jnp.concatenate(
        [
            full_named,
            full_hi,
            full_lo,
            jnp.zeros((moe_rows, side_width - 3 * EXPERTS), jnp.bfloat16),
        ],
        axis=1,
    )
    packed = jnp.concatenate([moe_in, side], axis=1)
    crossed = lax.ppermute(packed, "half", perm=[(0, 1), (1, 0)])
    pair = jnp.where(
        holds_first, jnp.stack([packed, crossed]), jnp.stack([crossed, packed])
    )
    fanned = lax.all_to_all(
        jnp.broadcast_to(pair[None], (half_size,) + pair.shape),
        "hseq",
        split_axis=0,
        concat_axis=0,
        tiled=True,
    )
    packed_all = fanned.transpose(1, 0, 2, 3).reshape(seq_count * moe_rows, -1)
    rows_all = packed_all[:, :model_width]
    total_rows = rows_all.shape[0]
    local_first = seq_index * experts_here
    side_all = packed_all[:, model_width:]
    named = (
        lax.dynamic_slice_in_dim(side_all, local_first, experts_here, 1) > 0
    )
    weight_hi = lax.dynamic_slice_in_dim(side_all, EXPERTS + local_first, experts_here, 1)
    weight_lo = lax.dynamic_slice_in_dim(side_all, 2 * EXPERTS + local_first, experts_here, 1)
    named_blocks = named.reshape(seq_count, moe_rows, experts_here).astype(jnp.int32)
    earlier_rows = (
        jnp.arange(moe_rows, dtype=jnp.int32)[None, :] < jnp.arange(moe_rows, dtype=jnp.int32)[:, None]
    ).astype(jnp.bfloat16)
    rank = jnp.einsum(
        "ij,bjx->bix", earlier_rows, named_blocks.astype(jnp.bfloat16), preferred_element_type=jnp.float32
    ).astype(jnp.int32)
    slot = (jnp.arange(seq_count, dtype=jnp.int32)[:, None, None] * capacity + rank).reshape(
        total_rows, experts_here
    )
    slots_total = seq_count * capacity
    picks = named[:, :, None] & (
        slot[:, :, None] == jnp.arange(slots_total, dtype=jnp.int32)[None, None, :]
    )
    onehot = picks.astype(jnp.bfloat16)
    rows_in = jnp.einsum(
        "nec,nd->ecd", onehot, rows_all, preferred_element_type=jnp.float32
    ).astype(jnp.bfloat16)
    hidden = jnp.einsum("ecd,edf->ecf", rows_in, expert_in, preferred_element_type=jnp.float32)
    half_width = hidden.shape[-1] // 2
    active = (jax.nn.silu(hidden[..., :half_width]) * hidden[..., half_width:]).astype(jnp.bfloat16)
    produced = jnp.einsum(
        "ecf,efd->ecd", active, expert_out, preferred_element_type=jnp.float32
    ).astype(jnp.bfloat16)
    scaled_hi = jnp.where(picks, weight_hi[:, :, None], jnp.zeros_like(onehot))
    scaled_lo = jnp.where(picks, weight_lo[:, :, None], jnp.zeros_like(onehot))
    partial = jnp.einsum(
        "nec,ecd->nd", scaled_hi, produced, preferred_element_type=jnp.float32
    ) + jnp.einsum("nec,ecd->nd", scaled_lo, produced, preferred_element_type=jnp.float32)
    by_dest = partial.astype(jnp.bfloat16).reshape(halves, half_size, moe_rows, -1)
    from_half = lax.all_to_all(
        by_dest.transpose(1, 0, 2, 3), "hseq", split_axis=0, concat_axis=0, tiled=True
    )
    half_sums = jnp.sum(from_half.astype(jnp.float32), axis=0)
    own_sum = jnp.where(holds_first, half_sums[0], half_sums[1])
    other_sum = jnp.where(holds_first, half_sums[1], half_sums[0])
    from_partner = lax.ppermute(other_sum.astype(jnp.bfloat16), "half", perm=[(0, 1), (1, 0)])
    moe = own_sum + from_partner.astype(jnp.float32)
    hidden_out = (residual + residual_scale * moe).astype(jnp.bfloat16)
    return (hidden_out, page_rows)


def solution(mesh):
    seq_count, exp_count = mesh.devices.shape
    split_mesh = Mesh(
        mesh.devices.reshape(2, seq_count // 2, exp_count), ("half", "hseq", "exp")
    )
    return jax.shard_map(
        body,
        mesh=split_mesh,
        in_specs=(
            P(SEQ_AXES, None),
            P(),
            P(None, "exp"),
            P(None, "exp"),
            P(None, "exp"),
            P("exp", None),
            P(SEQ_AXES, "exp"),
            P(),
            P(SEQ_AXES, None, None),
            P(SEQ_AXES, None, None),
            P(("half", "hseq", "exp"), None),
            P(("half", "hseq", "exp"), None),
            P(),
        ),
        out_specs=(P(("half", "hseq", "exp"), None), P(SEQ_AXES, "exp", None, None)),
        check_vma=False,
    )
```

```python
import functools
import math

import jax
import jax.numpy as jnp
from jax import lax
from jax.experimental import pallas as pl
from jax.experimental.pallas import tpu as pltpu
from jax.sharding import Mesh, PartitionSpec as P

HEADS = 24
KV_HEADS = 8
HEAD_DIM = 64
EXPERTS = 32
PAGE = 8
SEQ_AXES = ("half", "hseq")


norm_epsilon = 1e-06
attention_scale = 0.015625
residual_scale = 0.22
masked_score = -1e30


def rms_norm(values, gain_row):
    widened = values.astype(jnp.float32)
    spread = lax.rsqrt(jnp.mean(widened * widened, axis=-1, keepdims=True) + norm_epsilon)
    return (widened * spread * gain_row).astype(jnp.bfloat16)


def partial_kernel(
    flags_ref, q_ref, k_ref, v_ref, acc_ref, m_ref, l_ref, m_sc, l_sc, acc_sc, *, mode, cache_rows,
    group_rows
):
    step = pl.program_id(1)
    last = pl.num_programs(1) - 1
    query_first = flags_ref[0]
    chunk = k_ref.shape[1]
    new_rows = chunk - cache_rows
    new_first = step * new_rows

    @pl.when(step == 0)
    def _():
        m_sc[...] = jnp.full(m_sc.shape, masked_score, jnp.float32)
        l_sc[...] = jnp.zeros(l_sc.shape, jnp.float32)
        acc_sc[...] = jnp.zeros(acc_sc.shape, jnp.float32)

    def update(first, count, causal):
        q = q_ref[0]
        k = k_ref[0, pl.ds(first, count), :]
        v = v_ref[0, pl.ds(first, count), :]
        scores = lax.dot_general(
            q, k, (((1,), (1,)), ((), ())), preferred_element_type=jnp.float32
        ) * attention_scale
        if causal:
            rows = q.shape[0]
            query_pos = query_first + lax.broadcasted_iota(jnp.int32, (rows, count), 0) % group_rows
            column = lax.broadcasted_iota(jnp.int32, (rows, count), 1) + first
            visible = (column < cache_rows) | (new_first + column - cache_rows <= query_pos)
            scores = jnp.where(visible, scores, masked_score)
        m_prev = m_sc[...]
        m_new = jnp.maximum(m_prev, jnp.max(scores, axis=1, keepdims=True))
        weights = jnp.exp(scores - m_new)
        if causal:
            weights = jnp.where(visible, weights, 0.0)
        factor = jnp.exp(m_prev - m_new)
        l_sc[...] = l_sc[...] * factor + jnp.sum(weights, axis=1, keepdims=True)
        acc_sc[...] = acc_sc[...] * factor + jnp.dot(
            weights.astype(jnp.bfloat16), v, preferred_element_type=jnp.float32
        )
        m_sc[...] = m_new

    if mode == "all":
        update(0, chunk, True)
    elif mode == "cache":
        update(0, cache_rows, False)
    else:

        @pl.when(new_first <= query_first + group_rows - 1)
        def _():
            update(cache_rows, new_rows, True)

    @pl.when(step == last)
    def _():
        acc_ref[0] = acc_sc[...]
        m_ref[0] = m_sc[...]
        l_ref[0] = l_sc[...]


def attend_partial(flags, q, kv_all, mode, cache_rows, group_rows):
    heads, rows, dim = q.shape
    devices, _, _, chunk, _ = kv_all.shape
    kernel = functools.partial(partial_kernel, mode=mode, cache_rows=cache_rows, group_rows=group_rows)
    kv_block = (None, None, 1, chunk, dim)
    row_block = pl.BlockSpec((1, rows, 1), lambda h, s, f: (h, 0, 0))
    return pl.pallas_call(
        kernel,
        out_shape=(
            jax.ShapeDtypeStruct((heads, rows, dim), jnp.float32),
            jax.ShapeDtypeStruct((heads, rows, 1), jnp.float32),
            jax.ShapeDtypeStruct((heads, rows, 1), jnp.float32),
        ),
        grid_spec=pltpu.PrefetchScalarGridSpec(
            num_scalar_prefetch=1,
            grid=(heads, devices),
            in_specs=[
                pl.BlockSpec((1, rows, dim), lambda h, s, f: (h, 0, 0)),
                pl.BlockSpec(kv_block, lambda h, s, f: (s, 0, h, 0, 0)),
                pl.BlockSpec(kv_block, lambda h, s, f: (s, 1, h, 0, 0)),
            ],
            out_specs=[pl.BlockSpec((1, rows, dim), lambda h, s, f: (h, 0, 0)), row_block, row_block],
            scratch_shapes=[
                pltpu.VMEM((rows, 1), jnp.float32),
                pltpu.VMEM((rows, 1), jnp.float32),
                pltpu.VMEM((rows, dim), jnp.float32),
            ],
        ),
        compiler_params=pltpu.CompilerParams(dimension_semantics=("arbitrary", "arbitrary")),
    )(flags, q, kv_all, kv_all)


def pl_cdiv(a, b):
    return -(-a // b)


def block_size(piece_rows):
    return math.gcd(piece_rows, 512)


def body(
    hidden_in,
    attn_gain,
    q_weight,
    k_weight,
    v_weight,
    o_weight,
    cache_kv,
    moe_gain,
    expert_in,
    expert_out,
    routes,
    route_prob,
    page_slot,
):
    halves = lax.axis_size("half")
    half_size = lax.axis_size("hseq")
    seq_count = halves * half_size
    half_index = lax.axis_index("half")
    half_pos = lax.axis_index("hseq")
    seq_index = half_index * half_size + half_pos
    exp_index = lax.axis_index("exp")
    tokens_here = hidden_in.shape[0]
    head_dim = HEAD_DIM
    kv_local = k_weight.shape[1] // head_dim
    group_size = HEADS // KV_HEADS
    holds_first = half_index == 0
    normed = rms_norm(hidden_in, attn_gain)
    queries = jnp.dot(normed, q_weight, preferred_element_type=jnp.float32).astype(jnp.bfloat16)
    keys_new = jnp.dot(normed, k_weight, preferred_element_type=jnp.float32).astype(jnp.bfloat16)
    values_new = jnp.dot(normed, v_weight, preferred_element_type=jnp.float32).astype(jnp.bfloat16)
    pair_width = 2 * kv_local * head_dim
    split_new = jnp.stack(
        [
            keys_new.reshape(tokens_here, kv_local, head_dim),
            values_new.reshape(tokens_here, kv_local, head_dim),
        ],
        axis=2,
    )
    pairs_new = split_new.reshape(tokens_here, pair_width)
    blocks_here = tokens_here // PAGE
    rounds = blocks_here // seq_count
    outgoing = pairs_new.reshape(rounds, seq_count, PAGE * pair_width)
    received = lax.all_to_all(outgoing, SEQ_AXES, split_axis=1, concat_axis=1, tiled=True)
    block_ids = (
        jnp.arange(seq_count, dtype=jnp.int32)[None, :] * blocks_here
        + jnp.arange(rounds, dtype=jnp.int32)[:, None] * seq_count
        + seq_index
    ).reshape(-1)
    table_ids = jnp.arange(page_slot.shape[0], dtype=jnp.int32)
    page_slots = jnp.sum(
        jnp.where(block_ids[:, None] == table_ids[None, :], page_slot[None, :], 0), axis=1
    )
    local_pages = (
        jnp.zeros((blocks_here, PAGE * pair_width), jnp.bfloat16)
        .at[page_slots]
        .set(received.reshape(blocks_here, -1))
    )
    page_rows = local_pages.reshape(blocks_here, PAGE, kv_local, 2, head_dim).transpose(
        0, 2, 3, 1, 4
    )
    page_rows = page_rows.reshape(blocks_here, kv_local, 2, PAGE * head_dim)
    kv_own = split_new.transpose(2, 1, 0, 3)
    cache_rows = cache_kv.shape[0]
    cache_own = cache_kv.reshape(cache_rows, kv_local, 2, head_dim).transpose(2, 1, 0, 3)
    kv_piece = jnp.concatenate([cache_own, kv_own], axis=2)
    kv_all = lax.all_to_all(
        jnp.broadcast_to(kv_piece[None], (half_size,) + kv_piece.shape),
        "hseq",
        split_axis=0,
        concat_axis=0,
        tiled=True,
    )
    query_rows = queries.reshape(tokens_here, kv_local, group_size, head_dim)
    query_rows = query_rows.transpose(1, 2, 0, 3).reshape(kv_local, group_size * tokens_here, head_dim)
    partner_rows = lax.ppermute(query_rows, "half", perm=[(0, 1)])
    flags = jnp.reshape(half_pos * tokens_here, (1,)).astype(jnp.int32)
    shapes = dict(cache_rows=cache_rows, group_rows=tokens_here)

    def pack_partial(part):
        acc, best, total = part
        pieces = [acc.astype(jnp.bfloat16)]
        for value in (best, total):
            high = value.astype(jnp.bfloat16)
            rest = value - high.astype(jnp.float32)
            middle = rest.astype(jnp.bfloat16)
            low = (rest - middle.astype(jnp.float32)).astype(jnp.bfloat16)
            pieces += [high, middle, low]
        return jnp.concatenate(pieces, axis=2)

    def empty_partial(rows_in):
        heads, rows, _ = rows_in.shape
        return pack_partial(
            (
                jnp.zeros((heads, rows, head_dim), jnp.float32),
                jnp.full((heads, rows, 1), masked_score, jnp.float32),
                jnp.zeros((heads, rows, 1), jnp.float32),
            )
        )

    far_part = lax.cond(
        holds_first,
        empty_partial,
        lambda rows_in: pack_partial(attend_partial(flags, rows_in, kv_all, "cache", **shapes)),
        partner_rows,
    )
    own_part = lax.cond(
        holds_first,
        lambda rows_in: attend_partial(flags, rows_in, kv_all, "all", **shapes),
        lambda rows_in: attend_partial(flags, rows_in, kv_all, "new", **shapes),
        query_rows,
    )
    back = lax.ppermute(far_part, "half", perm=[(1, 0)]).astype(jnp.float32)
    back_acc = back[..., :head_dim]
    back_best = jnp.sum(back[..., head_dim : head_dim + 3], axis=2, keepdims=True)
    back_total = jnp.sum(back[..., head_dim + 3 : head_dim + 6], axis=2, keepdims=True)
    back_best = jnp.where(holds_first, back_best, masked_score)
    back_total = jnp.where(holds_first, back_total, 0.0)
    back_acc = jnp.where(holds_first, back_acc, 0.0)
    own_acc, own_best, own_total = own_part
    best = jnp.maximum(own_best, back_best)
    own_scale = jnp.exp(own_best - best)
    back_scale = jnp.exp(back_best - best)
    attended = (own_acc * own_scale + back_acc * back_scale) / (
        own_total * own_scale + back_total * back_scale
    )
    attended = attended.astype(jnp.bfloat16).reshape(kv_local, group_size, tokens_here, head_dim)
    attended = attended.transpose(2, 0, 1, 3).reshape(tokens_here, -1)
    exp_count = lax.axis_size("exp")
    projected = jnp.dot(attended, o_weight, preferred_element_type=jnp.float32).astype(jnp.bfloat16)
    pieces = lax.all_to_all(
        projected.reshape(exp_count, -1, projected.shape[1]), "exp", split_axis=0, concat_axis=0, tiled=True
    )
    mixed_rows = jnp.sum(pieces.astype(jnp.float32), axis=0)
    moe_rows = mixed_rows.shape[0]
    residual = (
        lax.dynamic_slice_in_dim(hidden_in, exp_index * moe_rows, moe_rows, 0).astype(jnp.float32)
        + residual_scale * mixed_rows
    )
    moe_in = rms_norm(residual, moe_gain)
    top_count = routes.shape[1]
    experts_here = expert_in.shape[0]
    capacity = 2 * moe_rows * top_count // EXPERTS
    share = route_prob / jnp.sum(route_prob, axis=-1, keepdims=True)
    expert_ids = jnp.arange(EXPERTS, dtype=jnp.int32)
    route_hits = routes[:, :, None] == expert_ids[None, None, :]
    full_weight = jnp.sum(jnp.where(route_hits, share[:, :, None], 0.0), axis=1)
    full_hi = full_weight.astype(jnp.bfloat16)
    full_lo = (full_weight - full_hi.astype(jnp.float32)).astype(jnp.bfloat16)
    full_named = jnp.any(route_hits, axis=1).astype(jnp.bfloat16)
    model_width = moe_in.shape[1]
    side_width = 128 * pl_cdiv(3 * EXPERTS, 128)
    side = jnp.concatenate(
        [
            full_named,
            full_hi,
            full_lo,
            jnp.zeros((moe_rows, side_width - 3 * EXPERTS), jnp.bfloat16),
        ],
        axis=1,
    )
    packed = jnp.concatenate([moe_in, side], axis=1)
    crossed = lax.ppermute(packed, "half", perm=[(0, 1), (1, 0)])
    pair = jnp.where(
        holds_first, jnp.stack([packed, crossed]), jnp.stack([crossed, packed])
    )
    fanned = lax.all_to_all(
        jnp.broadcast_to(pair[None], (half_size,) + pair.shape),
        "hseq",
        split_axis=0,
        concat_axis=0,
        tiled=True,
    )
    packed_all = fanned.transpose(1, 0, 2, 3).reshape(seq_count * moe_rows, -1)
    rows_all = packed_all[:, :model_width]
    total_rows = rows_all.shape[0]
    local_first = seq_index * experts_here
    side_all = packed_all[:, model_width:]
    named = (
        lax.dynamic_slice_in_dim(side_all, local_first, experts_here, 1) > 0
    )
    weight_hi = lax.dynamic_slice_in_dim(side_all, EXPERTS + local_first, experts_here, 1)
    weight_lo = lax.dynamic_slice_in_dim(side_all, 2 * EXPERTS + local_first, experts_here, 1)
    named_blocks = named.reshape(seq_count, moe_rows, experts_here).astype(jnp.int32)
    earlier_rows = (
        jnp.arange(moe_rows, dtype=jnp.int32)[None, :] < jnp.arange(moe_rows, dtype=jnp.int32)[:, None]
    ).astype(jnp.bfloat16)
    rank = jnp.einsum(
        "ij,bjx->bix", earlier_rows, named_blocks.astype(jnp.bfloat16), preferred_element_type=jnp.float32
    ).astype(jnp.int32)
    slot = (jnp.arange(seq_count, dtype=jnp.int32)[:, None, None] * capacity + rank).reshape(
        total_rows, experts_here
    )
    slots_total = seq_count * capacity
    picks = named[:, :, None] & (
        slot[:, :, None] == jnp.arange(slots_total, dtype=jnp.int32)[None, None, :]
    )
    onehot = picks.astype(jnp.bfloat16)
    rows_in = jnp.einsum(
        "nec,nd->ecd", onehot, rows_all, preferred_element_type=jnp.float32
    ).astype(jnp.bfloat16)
    hidden = jnp.einsum("ecd,edf->ecf", rows_in, expert_in, preferred_element_type=jnp.float32)
    half_width = hidden.shape[-1] // 2
    active = (jax.nn.silu(hidden[..., :half_width]) * hidden[..., half_width:]).astype(jnp.bfloat16)
    produced = jnp.einsum(
        "ecf,efd->ecd", active, expert_out, preferred_element_type=jnp.float32
    ).astype(jnp.bfloat16)
    scaled_hi = jnp.where(picks, weight_hi[:, :, None], jnp.zeros_like(onehot))
    scaled_lo = jnp.where(picks, weight_lo[:, :, None], jnp.zeros_like(onehot))
    partial = jnp.einsum(
        "nec,ecd->nd", scaled_hi, produced, preferred_element_type=jnp.float32
    ) + jnp.einsum("nec,ecd->nd", scaled_lo, produced, preferred_element_type=jnp.float32)
    by_dest = partial.astype(jnp.bfloat16).reshape(halves, half_size, moe_rows, -1)
    from_half = lax.all_to_all(
        by_dest.transpose(1, 0, 2, 3), "hseq", split_axis=0, concat_axis=0, tiled=True
    )
    half_sums = jnp.sum(from_half.astype(jnp.float32), axis=0)
    own_sum = jnp.where(holds_first, half_sums[0], half_sums[1])
    other_sum = jnp.where(holds_first, half_sums[1], half_sums[0])
    from_partner = lax.ppermute(other_sum.astype(jnp.bfloat16), "half", perm=[(0, 1), (1, 0)])
    moe = own_sum + from_partner.astype(jnp.float32)
    hidden_out = (residual + residual_scale * moe).astype(jnp.bfloat16)
    return (hidden_out, page_rows)


def solution(mesh):
    seq_count, exp_count = mesh.devices.shape
    split_mesh = Mesh(
        mesh.devices.reshape(2, seq_count // 2, exp_count), ("half", "hseq", "exp")
    )
    return jax.shard_map(
        body,
        mesh=split_mesh,
        in_specs=(
            P(SEQ_AXES, None),
            P(),
            P(None, "exp"),
            P(None, "exp"),
            P(None, "exp"),
            P("exp", None),
            P(SEQ_AXES, "exp"),
            P(),
            P(SEQ_AXES, None, None),
            P(SEQ_AXES, None, None),
            P(("half", "hseq", "exp"), None),
            P(("half", "hseq", "exp"), None),
            P(),
        ),
        out_specs=(P(("half", "hseq", "exp"), None), P(SEQ_AXES, "exp", None, None)),
        check_vma=False,
    )
```

```python
import functools
import math

import jax
import jax.numpy as jnp
from jax import lax
from jax.experimental import pallas as pl
from jax.experimental.pallas import tpu as pltpu
from jax.sharding import Mesh, PartitionSpec as P

HEADS = 24
KV_HEADS = 8
HEAD_DIM = 64
EXPERTS = 32
PAGE = 8
SEQ_AXES = ("half", "hseq")


norm_epsilon = 1e-06
attention_scale = 0.015625
residual_scale = 0.22
masked_score = -1e30


def rms_norm(values, gain_row):
    widened = values.astype(jnp.float32)
    spread = lax.rsqrt(jnp.mean(widened * widened, axis=-1, keepdims=True) + norm_epsilon)
    return (widened * spread * gain_row).astype(jnp.bfloat16)


def partial_kernel(
    flags_ref, q_ref, k_ref, v_ref, acc_ref, m_ref, l_ref, m_sc, l_sc, acc_sc, *, mode, cache_rows,
    group_rows
):
    step = pl.program_id(1)
    last = pl.num_programs(1) - 1
    query_first = flags_ref[0]
    chunk = k_ref.shape[1]
    new_rows = chunk - cache_rows
    new_first = step * new_rows

    @pl.when(step == 0)
    def _():
        m_sc[...] = jnp.full(m_sc.shape, masked_score, jnp.float32)
        l_sc[...] = jnp.zeros(l_sc.shape, jnp.float32)
        acc_sc[...] = jnp.zeros(acc_sc.shape, jnp.float32)

    def update(first, count, causal):
        q = q_ref[0]
        k = k_ref[0, pl.ds(first, count), :]
        v = v_ref[0, pl.ds(first, count), :]
        scores = lax.dot_general(
            q, k, (((1,), (1,)), ((), ())), preferred_element_type=jnp.float32
        ) * attention_scale
        if causal:
            rows = q.shape[0]
            query_pos = query_first + lax.broadcasted_iota(jnp.int32, (rows, count), 0) % group_rows
            column = lax.broadcasted_iota(jnp.int32, (rows, count), 1) + first
            visible = (column < cache_rows) | (new_first + column - cache_rows <= query_pos)
            scores = jnp.where(visible, scores, masked_score)
        m_prev = m_sc[...]
        m_new = jnp.maximum(m_prev, jnp.max(scores, axis=1, keepdims=True))
        weights = jnp.exp(scores - m_new)
        if causal:
            weights = jnp.where(visible, weights, 0.0)
        factor = jnp.exp(m_prev - m_new)
        l_sc[...] = l_sc[...] * factor + jnp.sum(weights, axis=1, keepdims=True)
        acc_sc[...] = acc_sc[...] * factor + jnp.dot(
            weights.astype(jnp.bfloat16), v, preferred_element_type=jnp.float32
        )
        m_sc[...] = m_new

    if mode == "all":
        update(0, chunk, True)
    elif mode == "cache":
        update(0, cache_rows, False)
    else:

        @pl.when(new_first <= query_first + group_rows - 1)
        def _():
            update(cache_rows, new_rows, True)

    @pl.when(step == last)
    def _():
        acc_ref[0] = acc_sc[...]
        m_ref[0] = m_sc[...]
        l_ref[0] = l_sc[...]


def attend_partial(flags, q, kv_all, mode, cache_rows, group_rows):
    heads, rows, dim = q.shape
    devices, _, _, chunk, _ = kv_all.shape
    kernel = functools.partial(partial_kernel, mode=mode, cache_rows=cache_rows, group_rows=group_rows)
    kv_block = (None, None, 1, chunk, dim)
    row_block = pl.BlockSpec((1, rows, 1), lambda h, s, f: (h, 0, 0))
    return pl.pallas_call(
        kernel,
        out_shape=(
            jax.ShapeDtypeStruct((heads, rows, dim), jnp.float32),
            jax.ShapeDtypeStruct((heads, rows, 1), jnp.float32),
            jax.ShapeDtypeStruct((heads, rows, 1), jnp.float32),
        ),
        grid_spec=pltpu.PrefetchScalarGridSpec(
            num_scalar_prefetch=1,
            grid=(heads, devices),
            in_specs=[
                pl.BlockSpec((1, rows, dim), lambda h, s, f: (h, 0, 0)),
                pl.BlockSpec(kv_block, lambda h, s, f: (s, 0, h, 0, 0)),
                pl.BlockSpec(kv_block, lambda h, s, f: (s, 1, h, 0, 0)),
            ],
            out_specs=[pl.BlockSpec((1, rows, dim), lambda h, s, f: (h, 0, 0)), row_block, row_block],
            scratch_shapes=[
                pltpu.VMEM((rows, 1), jnp.float32),
                pltpu.VMEM((rows, 1), jnp.float32),
                pltpu.VMEM((rows, dim), jnp.float32),
            ],
        ),
        compiler_params=pltpu.CompilerParams(dimension_semantics=("arbitrary", "arbitrary")),
    )(flags, q, kv_all, kv_all)


def pl_cdiv(a, b):
    return -(-a // b)


def block_size(piece_rows):
    return math.gcd(piece_rows, 512)


def body(
    hidden_in,
    attn_gain,
    q_weight,
    k_weight,
    v_weight,
    o_weight,
    cache_kv,
    moe_gain,
    expert_in,
    expert_out,
    routes,
    route_prob,
    page_slot,
):
    halves = lax.axis_size("half")
    half_size = lax.axis_size("hseq")
    seq_count = halves * half_size
    half_index = lax.axis_index("half")
    half_pos = lax.axis_index("hseq")
    seq_index = half_index * half_size + half_pos
    exp_index = lax.axis_index("exp")
    tokens_here = hidden_in.shape[0]
    head_dim = HEAD_DIM
    kv_local = k_weight.shape[1] // head_dim
    group_size = HEADS // KV_HEADS
    holds_first = half_index == 0
    normed = rms_norm(hidden_in, attn_gain)
    queries = jnp.dot(normed, q_weight, preferred_element_type=jnp.float32).astype(jnp.bfloat16)
    keys_new = jnp.dot(normed, k_weight, preferred_element_type=jnp.float32).astype(jnp.bfloat16)
    values_new = jnp.dot(normed, v_weight, preferred_element_type=jnp.float32).astype(jnp.bfloat16)
    pair_width = 2 * kv_local * head_dim
    split_new = jnp.stack(
        [
            keys_new.reshape(tokens_here, kv_local, head_dim),
            values_new.reshape(tokens_here, kv_local, head_dim),
        ],
        axis=2,
    )
    pairs_new = split_new.reshape(tokens_here, pair_width)
    blocks_here = tokens_here // PAGE
    rounds = blocks_here // seq_count
    outgoing = pairs_new.reshape(rounds, seq_count, PAGE * pair_width)
    received = lax.all_to_all(outgoing, SEQ_AXES, split_axis=1, concat_axis=1, tiled=True)
    block_ids = (
        jnp.arange(seq_count, dtype=jnp.int32)[None, :] * blocks_here
        + jnp.arange(rounds, dtype=jnp.int32)[:, None] * seq_count
        + seq_index
    ).reshape(-1)
    table_ids = jnp.arange(page_slot.shape[0], dtype=jnp.int32)
    page_slots = jnp.sum(
        jnp.where(block_ids[:, None] == table_ids[None, :], page_slot[None, :], 0), axis=1
    )
    local_pages = (
        jnp.zeros((blocks_here, PAGE * pair_width), jnp.bfloat16)
        .at[page_slots]
        .set(received.reshape(blocks_here, -1))
    )
    page_rows = local_pages.reshape(blocks_here, PAGE, kv_local, 2, head_dim).transpose(
        0, 2, 3, 1, 4
    )
    page_rows = page_rows.reshape(blocks_here, kv_local, 2, PAGE * head_dim)
    kv_own = split_new.transpose(2, 1, 0, 3)
    cache_rows = cache_kv.shape[0]
    cache_own = cache_kv.reshape(cache_rows, kv_local, 2, head_dim).transpose(2, 1, 0, 3)
    kv_piece = jnp.concatenate([cache_own, kv_own], axis=2)
    query_rows = queries.reshape(tokens_here, kv_local, group_size, head_dim)
    query_rows = query_rows.transpose(1, 2, 0, 3).reshape(kv_local, group_size * tokens_here, head_dim)
    partner_rows = lax.ppermute(query_rows, "half", perm=[(0, 1)])
    partner_rows, kv_piece = lax.optimization_barrier((partner_rows, kv_piece))
    kv_all = lax.all_to_all(
        jnp.broadcast_to(kv_piece[None], (half_size,) + kv_piece.shape),
        "hseq",
        split_axis=0,
        concat_axis=0,
        tiled=True,
    )
    flags = jnp.reshape(half_pos * tokens_here, (1,)).astype(jnp.int32)
    shapes = dict(cache_rows=cache_rows, group_rows=tokens_here)

    def empty_partial(rows_in):
        heads, rows, _ = rows_in.shape
        return jnp.concatenate(
            [
                jnp.zeros((heads, rows, head_dim), jnp.float32),
                jnp.full((heads, rows, 1), masked_score, jnp.float32),
                jnp.zeros((heads, rows, 1), jnp.float32),
            ],
            axis=2,
        )

    far_part = lax.cond(
        holds_first,
        empty_partial,
        lambda rows_in: jnp.concatenate(
            attend_partial(flags, rows_in, kv_all, "cache", **shapes), axis=2
        ),
        partner_rows,
    )
    own_part = lax.cond(
        holds_first,
        lambda rows_in: attend_partial(flags, rows_in, kv_all, "all", **shapes),
        lambda rows_in: attend_partial(flags, rows_in, kv_all, "new", **shapes),
        query_rows,
    )
    back = lax.ppermute(far_part, "half", perm=[(1, 0)])
    back_acc = back[..., :head_dim]
    back_best = back[..., head_dim : head_dim + 1]
    back_total = back[..., head_dim + 1 :]
    back_best = jnp.where(holds_first, back_best, masked_score)
    back_total = jnp.where(holds_first, back_total, 0.0)
    back_acc = jnp.where(holds_first, back_acc, 0.0)
    own_acc, own_best, own_total = own_part
    best = jnp.maximum(own_best, back_best)
    own_scale = jnp.exp(own_best - best)
    back_scale = jnp.exp(back_best - best)
    attended = (own_acc * own_scale + back_acc * back_scale) / (
        own_total * own_scale + back_total * back_scale
    )
    attended = attended.astype(jnp.bfloat16).reshape(kv_local, group_size, tokens_here, head_dim)
    attended = attended.transpose(2, 0, 1, 3).reshape(tokens_here, -1)
    exp_count = lax.axis_size("exp")
    projected = jnp.dot(attended, o_weight, preferred_element_type=jnp.float32).astype(jnp.bfloat16)
    pieces = lax.all_to_all(
        projected.reshape(exp_count, -1, projected.shape[1]), "exp", split_axis=0, concat_axis=0, tiled=True
    )
    mixed_rows = jnp.sum(pieces.astype(jnp.float32), axis=0)
    moe_rows = mixed_rows.shape[0]
    residual = (
        lax.dynamic_slice_in_dim(hidden_in, exp_index * moe_rows, moe_rows, 0).astype(jnp.float32)
        + residual_scale * mixed_rows
    )
    moe_in = rms_norm(residual, moe_gain)
    top_count = routes.shape[1]
    experts_here = expert_in.shape[0]
    capacity = 2 * moe_rows * top_count // EXPERTS
    share = route_prob / jnp.sum(route_prob, axis=-1, keepdims=True)
    expert_ids = jnp.arange(EXPERTS, dtype=jnp.int32)
    route_hits = routes[:, :, None] == expert_ids[None, None, :]
    full_weight = jnp.sum(jnp.where(route_hits, share[:, :, None], 0.0), axis=1)
    full_hi = full_weight.astype(jnp.bfloat16)
    full_lo = (full_weight - full_hi.astype(jnp.float32)).astype(jnp.bfloat16)
    full_named = jnp.any(route_hits, axis=1).astype(jnp.bfloat16)
    model_width = moe_in.shape[1]
    side_width = 128 * pl_cdiv(3 * EXPERTS, 128)
    side = jnp.concatenate(
        [
            full_named,
            full_hi,
            full_lo,
            jnp.zeros((moe_rows, side_width - 3 * EXPERTS), jnp.bfloat16),
        ],
        axis=1,
    )
    packed = jnp.concatenate([moe_in, side], axis=1)
    crossed = lax.ppermute(packed, "half", perm=[(0, 1), (1, 0)])
    pair = jnp.where(
        holds_first, jnp.stack([packed, crossed]), jnp.stack([crossed, packed])
    )
    fanned = lax.all_to_all(
        jnp.broadcast_to(pair[None], (half_size,) + pair.shape),
        "hseq",
        split_axis=0,
        concat_axis=0,
        tiled=True,
    )
    packed_all = fanned.transpose(1, 0, 2, 3).reshape(seq_count * moe_rows, -1)
    rows_all = packed_all[:, :model_width]
    total_rows = rows_all.shape[0]
    local_first = seq_index * experts_here
    side_all = packed_all[:, model_width:]
    named = (
        lax.dynamic_slice_in_dim(side_all, local_first, experts_here, 1) > 0
    )
    weight_hi = lax.dynamic_slice_in_dim(side_all, EXPERTS + local_first, experts_here, 1)
    weight_lo = lax.dynamic_slice_in_dim(side_all, 2 * EXPERTS + local_first, experts_here, 1)
    named_blocks = named.reshape(seq_count, moe_rows, experts_here).astype(jnp.int32)
    earlier_rows = (
        jnp.arange(moe_rows, dtype=jnp.int32)[None, :] < jnp.arange(moe_rows, dtype=jnp.int32)[:, None]
    ).astype(jnp.bfloat16)
    rank = jnp.einsum(
        "ij,bjx->bix", earlier_rows, named_blocks.astype(jnp.bfloat16), preferred_element_type=jnp.float32
    ).astype(jnp.int32)
    slot = (jnp.arange(seq_count, dtype=jnp.int32)[:, None, None] * capacity + rank).reshape(
        total_rows, experts_here
    )
    slots_total = seq_count * capacity
    picks = named[:, :, None] & (
        slot[:, :, None] == jnp.arange(slots_total, dtype=jnp.int32)[None, None, :]
    )
    onehot = picks.astype(jnp.bfloat16)
    rows_in = jnp.einsum(
        "nec,nd->ecd", onehot, rows_all, preferred_element_type=jnp.float32
    ).astype(jnp.bfloat16)
    hidden = jnp.einsum("ecd,edf->ecf", rows_in, expert_in, preferred_element_type=jnp.float32)
    half_width = hidden.shape[-1] // 2
    active = (jax.nn.silu(hidden[..., :half_width]) * hidden[..., half_width:]).astype(jnp.bfloat16)
    produced = jnp.einsum(
        "ecf,efd->ecd", active, expert_out, preferred_element_type=jnp.float32
    ).astype(jnp.bfloat16)
    scaled_hi = jnp.where(picks, weight_hi[:, :, None], jnp.zeros_like(onehot))
    scaled_lo = jnp.where(picks, weight_lo[:, :, None], jnp.zeros_like(onehot))
    partial = jnp.einsum(
        "nec,ecd->nd", scaled_hi, produced, preferred_element_type=jnp.float32
    ) + jnp.einsum("nec,ecd->nd", scaled_lo, produced, preferred_element_type=jnp.float32)
    by_dest = partial.astype(jnp.bfloat16).reshape(halves, half_size, moe_rows, -1)
    from_half = lax.all_to_all(
        by_dest.transpose(1, 0, 2, 3), "hseq", split_axis=0, concat_axis=0, tiled=True
    )
    half_sums = jnp.sum(from_half.astype(jnp.float32), axis=0)
    own_sum = jnp.where(holds_first, half_sums[0], half_sums[1])
    other_sum = jnp.where(holds_first, half_sums[1], half_sums[0])
    from_partner = lax.ppermute(other_sum.astype(jnp.bfloat16), "half", perm=[(0, 1), (1, 0)])
    moe = own_sum + from_partner.astype(jnp.float32)
    hidden_out = (residual + residual_scale * moe).astype(jnp.bfloat16)
    return (hidden_out, page_rows)


def solution(mesh):
    seq_count, exp_count = mesh.devices.shape
    split_mesh = Mesh(
        mesh.devices.reshape(2, seq_count // 2, exp_count), ("half", "hseq", "exp")
    )
    return jax.shard_map(
        body,
        mesh=split_mesh,
        in_specs=(
            P(SEQ_AXES, None),
            P(),
            P(None, "exp"),
            P(None, "exp"),
            P(None, "exp"),
            P("exp", None),
            P(SEQ_AXES, "exp"),
            P(),
            P(SEQ_AXES, None, None),
            P(SEQ_AXES, None, None),
            P(("half", "hseq", "exp"), None),
            P(("half", "hseq", "exp"), None),
            P(),
        ),
        out_specs=(P(("half", "hseq", "exp"), None), P(SEQ_AXES, "exp", None, None)),
        check_vma=False,
    )
```
